32 devices in a mesh: groups: 2 (over y), gz: 4 (over z), sec: 2 (over x), ch: 2 (over core).
Axes of the slice: x: 2, y: 2, z: 4, core: 2. Of those that a mesh axis runs over, the one named last changes fastest.
Arguments:
- coarse: bfloat16 [64, 32, 4, 256], P('ch', ('groups', 'gz', 'sec')), parts along dimension 1, may hold values from -6 to 6
- saved_pre: bfloat16 [32, 64, 8, 512], P('ch', ('groups', 'gz', 'sec')), parts along dimension 1, may hold values from -6 to 6
- out_grad: bfloat16 [32, 64, 8, 512], P('ch', ('groups', 'gz', 'sec')), parts along dimension 1, may hold values from -6 to 6
- up_weight: bfloat16 [27, 32, 64], replicated, may hold values from -0.21875 to 0.21875
- refine_weight: bfloat16 [27, 32, 32], replicated, may hold values from -0.21875 to 0.21875
Outputs:
- grad_coarse: bfloat16 [64, 32, 4, 256], P('ch', ('groups', 'gz', 'sec')), parts along dimension 1
- grad_up: float32 [54, 32, 64], P('groups', 'ch'), parts along dimension 0
- grad_refine: float32 [54, 32, 32], P('groups', None, 'ch'), parts along dimension 0
The draws below stay inside these ranges and needn't reach their ends.
There are 2 independent parts, one for each index of `groups`. The reference program is written for one: setup_inputs(seed, part) draws one part's arguments, and reference() takes and returns one part's arrays. A program takes and returns all parts, laid end to end along the dimension named above; an argument that names none is the same for every part. Nothing has to cross between parts.
All inputs are finite; a program needn't handle non-finite values.
Results may differ from the reference program's by a relative error of at most 0.0049.
Values may be sent and summed in bfloat16 or wider, within the bound.
No kernel may reach another device: no remote copies, remote signals or barrier semaphores. Data moves between devices by JAX's collectives and lax.ppermute only.
A program may use at most 128 MiB of HBM per device.

```python
import jax
import jax.numpy as jnp
from jax import lax

CH = 32
CIN = 64
XF = 8
YF = 512
ZF = 32
ZC = 16
XC = 4
YC = 256


def steps_of(stream_key, shape, pieces, low, largest):
    def one(axis_at, parts):
        heights = jax.random.uniform(jax.random.fold_in(jax.random.fold_in(stream_key, 6), axis_at), (parts,), jnp.float32, low / len(pieces), largest / len(pieces))
        return jnp.repeat(jnp.exp(heights), shape[axis_at] // parts).reshape((-1,) + (1,) * (len(shape) - axis_at - 1))

    factor_of = one(*pieces[0])
    for cut in pieces[1:]:
        factor_of = factor_of * one(*cut)
    return factor_of


def noise(rng, extent, scale, limit, cuts=(), kind=jnp.bfloat16):
    values = scale * jax.random.normal(rng, extent, jnp.float32)
    if cuts:
        values = values * steps_of(rng, extent, cuts, -0.22, 0.18)
    return jnp.clip(values, -limit, limit).astype(kind)


def setup_inputs(seed: int = 0, part: int = 0) -> dict:
    seeds = jax.random.split(jax.random.key(seed), 6)
    own_keys = jax.random.split(jax.random.fold_in(seeds[5], part), 6)
    coarse = noise(own_keys[0], (CIN, ZC, XC, YC), 1.0, 6.0, ((0, 2), (1, 8)))
    saved_pre = noise(own_keys[1], (CH, ZF, XF, YF), 1.0, 6.0, ((0, 2), (1, 8)))
    out_grad = noise(own_keys[2], (CH, ZF, XF, YF), 1.0, 6.0, ((0, 2), (1, 8)))
    up_weight = noise(seeds[3], (27, CH, CIN), (27 * CH) ** -0.5, 0.21875)
    refine_weight = noise(seeds[4], (27, CH, CH), (27 * CH) ** -0.5, 0.21875)
    return dict(coarse=coarse, saved_pre=saved_pre, out_grad=out_grad, up_weight=up_weight, refine_weight=refine_weight)


leak_slope = 0.2


def kernel_offsets():
    return [(along_z, along_x, along_y) for along_z in range(3) for along_x in range(3) for along_y in range(3)]


def shift_zero_x(field, amount):
    width = field.shape[2]
    padded = jnp.pad(field, ((0, 0), (0, 0), (2, 2), (0, 0)))
    return padded[:, :, 2 - amount:2 - amount + width, :]


def reference(coarse, saved_pre, out_grad, up_weight, refine_weight):
    pre_act = saved_pre.astype(jnp.float32)
    slopes = jnp.where(pre_act > 0, 1.0, leak_slope).astype(jnp.float32)
    hidden = lax.optimization_barrier((pre_act * slopes).astype(jnp.bfloat16)).astype(jnp.float32)
    upstream = out_grad.astype(jnp.float32)
    grad_hidden = jnp.zeros(pre_act.shape, jnp.float32)
    refine_terms = []
    for tap_number, (along_z, along_x, along_y) in enumerate(kernel_offsets()):
        shifted = jnp.roll(upstream, (2 * (along_z - 1), 2 * (along_y - 1)), axis=(1, 3))
        shifted = shift_zero_x(shifted, 2 * (along_x - 1))
        weights = refine_weight[tap_number].astype(jnp.float32)
        grad_hidden = grad_hidden + jnp.einsum("oc,ozxy->czxy", weights, shifted)
        refine_terms.append(jnp.einsum("ozxy,czxy->oc", shifted, hidden))
    fine_total = ZF * XF * YF
    grad_refine = jnp.stack(refine_terms) * (float(fine_total) ** -0.5)
    grad_pre = lax.optimization_barrier((grad_hidden * slopes).astype(jnp.bfloat16)).astype(jnp.float32)
    coarse_values = coarse.astype(jnp.float32)
    grad_coarse = jnp.zeros(coarse.shape, jnp.float32)
    up_terms = []
    for tap_number, (along_z, along_x, along_y) in enumerate(kernel_offsets()):
        moved = jnp.roll(grad_pre, (1 - along_z, 1 - along_y), axis=(1, 3))
        selected = shift_zero_x(moved, 1 - along_x)[:, ::2, ::2, ::2]
        weights = up_weight[tap_number].astype(jnp.float32)
        grad_coarse = grad_coarse + jnp.einsum("fc,fzxy->czxy", weights, selected)
        up_terms.append(jnp.einsum("czxy,fzxy->fc", coarse_values, selected))
    coarse_total = ZC * XC * YC
    grad_up = jnp.stack(up_terms) * (float(coarse_total) ** -0.5)
    return (grad_coarse.astype(jnp.bfloat16), grad_up, grad_refine)
```

```python
import jax
import jax.numpy as jnp
from jax import lax
from jax.sharding import PartitionSpec as P

leak_slope = 0.2
SPATIAL = ("NCDHW", "OIDHW", "NCDHW")


def padded(block, sides, width):
    for axis, dim in sides:
        count = lax.axis_size(axis)
        forward = [(i, i + 1) for i in range(count - 1)]
        forward.append((count - 1, 0))
        backward = [(target, source) for source, target in forward]
        low = lax.ppermute(
            lax.slice_in_dim(block, block.shape[dim] - width, None, axis=dim), axis, forward
        )
        high = lax.ppermute(lax.slice_in_dim(block, 0, width, axis=dim), axis, backward)
        block = jnp.concatenate([low, block, high], axis=dim)
    return block


def passed_along(block, axis, distance):
    devices = range(lax.axis_size(axis))
    route = [((i - distance) % len(devices), i) for i in devices]
    return lax.ppermute(block, axis, route)


def wrap_y(block, low, high):
    size = block.shape[3]
    parts = [block[:, :, :, size - low :], block, block[:, :, :, :high]]
    return jnp.concatenate([p for p in parts if p.shape[3]], axis=3)


def conv(lhs, rhs, strides, dilation):
    return lax.conv_general_dilated(
        lhs,
        rhs,
        window_strides=strides,
        padding="VALID",
        rhs_dilation=dilation,
        dimension_numbers=SPATIAL,
        preferred_element_type=jnp.float32,
    )


def filter_grad(lhs, cotangent, strides, dilation):
    return lax.conv_general_dilated(
        lhs,
        cotangent,
        window_strides=strides,
        padding="VALID",
        rhs_dilation=dilation,
        dimension_numbers=("CNDHW", "IODHW", "CNDHW"),
        preferred_element_type=jnp.float32,
    )


def local(coarse, saved_pre, out_grad, up_weight, refine_weight):
    part_ch = saved_pre.shape[0]
    planes_z = saved_pre.shape[1]
    planes_x = saved_pre.shape[2]
    cells_y = saved_pre.shape[3]
    channel_start = lax.axis_index("ch") * part_ch
    pre_act = saved_pre.astype(jnp.float32)
    slopes = jnp.where(pre_act > 0, 1.0, leak_slope).astype(jnp.float32)
    hidden = (pre_act * slopes).astype(jnp.bfloat16)

    rimmed_local = padded(out_grad, ((("gz", "sec"), 1),), 2)
    every_channel = lax.all_gather(rimmed_local, "ch", axis=0, tiled=True)
    rimmed = jnp.pad(every_channel, ((0, 0), (0, 0), (2, 2), (0, 0)))
    rimmed = wrap_y(rimmed, 2, 2)[None]

    refine_cols = lax.dynamic_slice_in_dim(refine_weight, channel_start, part_ch, 2)
    refine_k = refine_cols.reshape(3, 3, 3, refine_cols.shape[1], part_ch)[::-1, ::-1, ::-1]
    refine_k = jnp.transpose(refine_k, (4, 3, 0, 1, 2))

    grad_hidden = conv(rimmed, refine_k, (1, 1, 1), (2, 2, 2))[0]
    refine_grad_k = filter_grad(rimmed, hidden[None], (2, 2, 2), (1, 1, 1))
    refine_terms = jnp.transpose(refine_grad_k[:, :, ::-1, ::-1, ::-1], (2, 3, 4, 1, 0))
    refine_terms = refine_terms.reshape(27, refine_cols.shape[1], part_ch)

    grad_pre = (grad_hidden * slopes).astype(jnp.bfloat16)
    below_z = passed_along(grad_pre[:, planes_z - 1 :, :, :], ("gz", "sec"), 1)
    raised_z = jnp.concatenate([below_z, grad_pre], axis=1)
    extended = jnp.pad(raised_z, ((0, 0), (0, 0), (1, 0), (0, 0)))
    extended = wrap_y(extended, 1, 0)[None]

    all_coarse = lax.all_gather(coarse, "ch", axis=0, tiled=True)
    up_rows = lax.dynamic_slice_in_dim(up_weight, channel_start, part_ch, 1)
    up_k = jnp.transpose(up_rows.reshape(3, 3, 3, part_ch, up_rows.shape[2]), (4, 3, 0, 1, 2))

    running = conv(extended, up_k, (2, 2, 2), (1, 1, 1))
    up_grad_k = filter_grad(extended, all_coarse[None], (1, 1, 1), (2, 2, 2))
    up_terms = jnp.transpose(up_grad_k, (2, 3, 4, 1, 0)).reshape(27, part_ch, up_rows.shape[2])

    coarse_summed = lax.psum_scatter(running[0], "ch", scatter_dimension=0, tiled=True)
    grad_coarse = coarse_summed.astype(jnp.bfloat16)
    flat = jnp.concatenate([up_terms.reshape(-1), refine_terms.reshape(-1)])
    flat = lax.psum(flat, ("gz", "sec"))
    up_summed = flat[: up_terms.size].reshape(up_terms.shape)
    refine_summed = flat[up_terms.size :].reshape(refine_terms.shape)
    fine_total = planes_z * lax.axis_size("gz") * lax.axis_size("sec") * planes_x * cells_y
    coarse_total = fine_total // 8
    grad_up = up_summed * float(coarse_total) ** (-0.5)
    grad_refine = refine_summed * float(fine_total) ** (-0.5)
    return (grad_coarse, grad_up, grad_refine)


def solution(mesh):
    placed = (
        P("ch", ("groups", "gz", "sec"), None, None),
        P("ch", ("groups", "gz", "sec"), None, None),
        P("ch", ("groups", "gz", "sec"), None, None),
        P(),
        P(),
    )
    return jax.shard_map(
        local,
        mesh=mesh,
        in_specs=placed,
        out_specs=(
            P("ch", ("groups", "gz", "sec"), None, None),
            P("groups", "ch", None),
            P("groups", None, "ch"),
        ),
        check_vma=False,
    )
```

```python
import functools

import jax
import jax.numpy as jnp
from jax import lax
from jax.experimental import pallas as pl
from jax.experimental.pallas import tpu as pltpu
from jax.sharding import PartitionSpec as P

leak_slope = 0.2


def padded(block, sides, width):
    for axis, dim in sides:
        count = lax.axis_size(axis)
        forward = [(i, i + 1) for i in range(count - 1)]
        forward.append((count - 1, 0))
        backward = [(target, source) for source, target in forward]
        low = lax.ppermute(
            lax.slice_in_dim(block, block.shape[dim] - width, None, axis=dim), axis, forward
        )
        high = lax.ppermute(lax.slice_in_dim(block, 0, width, axis=dim), axis, backward)
        block = jnp.concatenate([low, block, high], axis=dim)
    return block


def passed_along(block, axis, distance):
    devices = range(lax.axis_size(axis))
    route = [((i - distance) % len(devices), i) for i in devices]
    return lax.ppermute(block, axis, route)


def vmem_specs(count):
    return [pl.BlockSpec(memory_space=pltpu.VMEM)] * count


def fine_kernel(g_ref, sp_ref, w_ref, gp_ref, r_ref):
    planes_z, planes_x, part_ch, cells_y = sp_ref.shape
    wide = g_ref.shape[4]
    r_ref[...] = jnp.zeros(r_ref.shape, r_ref.dtype)

    def body(step, carry):
        z = step // planes_x
        x = step % planes_x
        pre_act = sp_ref[z, x].astype(jnp.float32)
        slopes = jnp.where(pre_act > 0, 1.0, leak_slope).astype(jnp.float32)
        hidden = (pre_act * slopes).astype(jnp.bfloat16).astype(jnp.float32)
        rolled = jnp.concatenate(
            [pltpu.roll(hidden, 2, 1), hidden, pltpu.roll(hidden, cells_y - 2, 1)], axis=0
        ).astype(jnp.bfloat16)
        total = jnp.zeros((3 * part_ch, cells_y), jnp.float32)
        for dz in range(3):
            block = g_ref[z % 2, z // 2 + 2 - dz, x % 2, pl.ds(x // 2, 3)]
            block = block.reshape(3 * wide, cells_y)
            total = total + jnp.dot(w_ref[dz], block, preferred_element_type=jnp.float32)
            r_ref[dz] += lax.dot_general(
                block, rolled, (((1,), (1,)), ((), ())), preferred_element_type=jnp.float32
            )
        grad_hidden = (
            pltpu.roll(total[:part_ch], cells_y - 2, 1)
            + total[part_ch : 2 * part_ch]
            + pltpu.roll(total[2 * part_ch :], 2, 1)
        )
        gp_ref[z, x] = (grad_hidden * slopes).astype(gp_ref.dtype)
        return carry

    lax.fori_loop(0, planes_z * planes_x, body, 0)


def coarse_kernel(gp_ref, below_ref, c_ref, u_ref, gc_ref, gu_ref, y_ref):
    planes_z = gp_ref.shape[0]
    cells_y = gp_ref.shape[2]
    rows_x = y_ref.shape[1] - 1
    part_ch = y_ref.shape[3]
    half_y = y_ref.shape[4]
    coarse_z, coarse_x = c_ref.shape[0], c_ref.shape[1]
    at_y = lax.broadcasted_iota(jnp.int32, (cells_y, 3 * half_y), 0)
    col = lax.broadcasted_iota(jnp.int32, (cells_y, 3 * half_y), 1)
    target = 2 * (col % half_y) + col // half_y - 1
    target = jnp.where(target < 0, target + cells_y, target)
    pick = (at_y == target).astype(jnp.bfloat16)
    y_ref[:, 0] = jnp.zeros(y_ref[:, 0].shape, y_ref.dtype)
    for zg in range(planes_z + 1):
        source = below_ref[0] if zg == 0 else gp_ref[zg - 1]
        picked = jnp.dot(source, pick, preferred_element_type=jnp.float32).astype(y_ref.dtype)
        for dy in range(3):
            part = picked[:, dy * half_y : (dy + 1) * half_y]
            y_ref[zg, 1:, dy] = part.reshape(rows_x, part_ch, half_y)
    gu_ref[...] = jnp.zeros(gu_ref.shape, gu_ref.dtype)

    def body(step, carry):
        iz = step // coarse_x
        ix = step % coarse_x
        crow = c_ref[iz, ix]
        total = jnp.zeros(gc_ref.shape[2:], jnp.float32)
        for dz in range(3):
            block = y_ref[2 * iz + dz, pl.ds(2 * ix, 3)]
            block = block.reshape(9 * part_ch, half_y)
            total = total + jnp.dot(u_ref[dz], block, preferred_element_type=jnp.float32)
            gu_ref[dz] += lax.dot_general(
                block, crow, (((1,), (1,)), ((), ())), preferred_element_type=jnp.float32
            )
        gc_ref[iz, ix] = total
        return carry

    lax.fori_loop(0, coarse_z * coarse_x, body, 0)


def local(coarse, saved_pre, out_grad, up_weight, refine_weight):
    part_ch = saved_pre.shape[0]
    planes_z = saved_pre.shape[1]
    planes_x = saved_pre.shape[2]
    cells_y = saved_pre.shape[3]
    all_ch = part_ch * lax.axis_size("ch")
    channel_start = lax.axis_index("ch") * part_ch

    rimmed_local = padded(out_grad, ((("gz", "sec"), 1),), 2)
    every_channel = lax.all_gather(rimmed_local, "ch", axis=0, tiled=True)
    rimmed = jnp.pad(every_channel, ((0, 0), (0, 0), (2, 2), (0, 0)))
    halo_z, halo_x = rimmed.shape[1], rimmed.shape[2]
    rimmed = rimmed.reshape(all_ch, halo_z // 2, 2, halo_x // 2, 2, cells_y)
    rimmed = jnp.transpose(rimmed, (2, 1, 4, 3, 0, 5))
    pre_rows = jnp.transpose(saved_pre, (1, 2, 0, 3))

    refine_cols = lax.dynamic_slice_in_dim(refine_weight, channel_start, part_ch, 2)
    refine_w = refine_cols.reshape(3, 3, 3, all_ch, part_ch)[:, ::-1]
    refine_w = jnp.transpose(refine_w, (0, 2, 4, 1, 3)).reshape(3, 3 * part_ch, 3 * all_ch)

    grad_pre, refine_acc = pl.pallas_call(
        fine_kernel,
        out_shape=(
            jax.ShapeDtypeStruct((planes_z, planes_x, part_ch, cells_y), jnp.bfloat16),
            jax.ShapeDtypeStruct((3, 3 * all_ch, 3 * part_ch), jnp.float32),
        ),
        in_specs=vmem_specs(3),
        out_specs=tuple(vmem_specs(2)),
    )(rimmed, pre_rows, refine_w)
    refine_terms = refine_acc.reshape(3, 3, all_ch, 3, part_ch)[:, ::-1]
    refine_terms = jnp.transpose(refine_terms, (0, 1, 3, 2, 4)).reshape(27, all_ch, part_ch)

    grad_rows = grad_pre.reshape(planes_z, planes_x * part_ch, cells_y)
    below_z = passed_along(grad_rows[planes_z - 1 :], ("gz", "sec"), 1)

    all_coarse = lax.all_gather(coarse, "ch", axis=0, tiled=True)
    coarse_in = all_coarse.shape[0]
    coarse_z, coarse_x, cells_yc = coarse.shape[1], coarse.shape[2], coarse.shape[3]
    coarse_rows = jnp.transpose(all_coarse, (1, 2, 0, 3))
    up_rows = lax.dynamic_slice_in_dim(up_weight, channel_start, part_ch, 1)
    up_w = jnp.transpose(up_rows.reshape(3, 9, part_ch, coarse_in), (0, 3, 1, 2))
    up_w = up_w.reshape(3, coarse_in, 9 * part_ch)

    coarse_acc, up_acc = pl.pallas_call(
        coarse_kernel,
        out_shape=(
            jax.ShapeDtypeStruct((coarse_z, coarse_x, coarse_in, cells_yc), jnp.float32),
            jax.ShapeDtypeStruct((3, 9 * part_ch, coarse_in), jnp.float32),
        ),
        in_specs=vmem_specs(4),
        out_specs=tuple(vmem_specs(2)),
        scratch_shapes=[
            pltpu.VMEM((planes_z + 1, planes_x + 1, 3, part_ch, cells_yc), jnp.bfloat16)
        ],
    )(grad_rows, below_z, coarse_rows, up_w)
    up_terms = up_acc.reshape(27, part_ch, coarse_in)
    running = jnp.transpose(coarse_acc, (2, 0, 1, 3))

    coarse_summed = lax.psum_scatter(running, "ch", scatter_dimension=0, tiled=True)
    grad_coarse = coarse_summed.astype(jnp.bfloat16)
    flat = jnp.concatenate([up_terms.reshape(-1), refine_terms.reshape(-1)])
    flat = lax.psum(flat, ("gz", "sec"))
    up_summed = flat[: up_terms.size].reshape(up_terms.shape)
    refine_summed = flat[up_terms.size :].reshape(refine_terms.shape)
    fine_total = planes_z * lax.axis_size("gz") * lax.axis_size("sec") * planes_x * cells_y
    coarse_total = fine_total // 8
    grad_up = up_summed * float(coarse_total) ** (-0.5)
    grad_refine = refine_summed * float(fine_total) ** (-0.5)
    return (grad_coarse, grad_up, grad_refine)


def solution(mesh):
    placed = (
        P("ch", ("groups", "gz", "sec"), None, None),
        P("ch", ("groups", "gz", "sec"), None, None),
        P("ch", ("groups", "gz", "sec"), None, None),
        P(),
        P(),
    )
    return jax.shard_map(
        local,
        mesh=mesh,
        in_specs=placed,
        out_specs=(
            P("ch", ("groups", "gz", "sec"), None, None),
            P("groups", "ch", None),
            P("groups", None, "ch"),
        ),
        check_vma=False,
    )
```

```python
import functools

import jax
import jax.numpy as jnp
from jax import lax
from jax.experimental import pallas as pl
from jax.experimental.pallas import tpu as pltpu
from jax.sharding import PartitionSpec as P

leak_slope = 0.2


def padded(block, sides, width):
    for axis, dim in sides:
        count = lax.axis_size(axis)
        forward = [(i, i + 1) for i in range(count - 1)]
        forward.append((count - 1, 0))
        backward = [(target, source) for source, target in forward]
        low = lax.ppermute(
            lax.slice_in_dim(block, block.shape[dim] - width, None, axis=dim), axis, forward
        )
        high = lax.ppermute(lax.slice_in_dim(block, 0, width, axis=dim), axis, backward)
        block = jnp.concatenate([low, block, high], axis=dim)
    return block


def passed_along(block, axis, distance):
    devices = range(lax.axis_size(axis))
    route = [((i - distance) % len(devices), i) for i in devices]
    return lax.ppermute(block, axis, route)


def summed_over_slabs(block, axis):
    count = lax.axis_size(axis)
    if count & (count - 1):
        return lax.psum(block, axis)
    step = 1
    while step < count:
        route = [(i, i ^ step) for i in range(count)]
        block = block + lax.ppermute(block, axis, route)
        step *= 2
    return block


def vmem_specs(count):
    return [pl.BlockSpec(memory_space=pltpu.VMEM)] * count


def fine_kernel(g_ref, sp_ref, w_ref, gp_ref, r_ref):
    planes_z, planes_x, part_ch, cells_y = sp_ref.shape
    wide = g_ref.shape[4]
    r_ref[...] = jnp.zeros(r_ref.shape, r_ref.dtype)

    def body(step, carry):
        z = step // planes_x
        x = step % planes_x
        pre_act = sp_ref[z, x].astype(jnp.float32)
        slopes = jnp.where(pre_act > 0, 1.0, leak_slope).astype(jnp.float32)
        hidden = (pre_act * slopes).astype(jnp.bfloat16).astype(jnp.float32)
        rolled = jnp.concatenate(
            [pltpu.roll(hidden, 2, 1), hidden, pltpu.roll(hidden, cells_y - 2, 1)], axis=0
        ).astype(jnp.bfloat16)
        total = jnp.zeros((3 * part_ch, cells_y), jnp.float32)
        for dz in range(3):
            block = g_ref[z % 2, z // 2 + 2 - dz, x % 2, pl.ds(x // 2, 3)]
            block = block.reshape(3 * wide, cells_y)
            total = total + jnp.dot(w_ref[dz], block, preferred_element_type=jnp.float32)
            r_ref[dz] += lax.dot_general(
                block, rolled, (((1,), (1,)), ((), ())), preferred_element_type=jnp.float32
            )
        grad_hidden = (
            pltpu.roll(total[:part_ch], cells_y - 2, 1)
            + total[part_ch : 2 * part_ch]
            + pltpu.roll(total[2 * part_ch :], 2, 1)
        )
        gp_ref[z, x] = (grad_hidden * slopes).astype(gp_ref.dtype)
        return carry

    lax.fori_loop(0, planes_z * planes_x, body, 0)


def coarse_kernel(gp_ref, below_ref, c_ref, u_ref, gc_ref, gu_ref, y_ref):
    planes_z = gp_ref.shape[0]
    cells_y = gp_ref.shape[2]
    rows_x = y_ref.shape[1] - 1
    part_ch = y_ref.shape[3]
    half_y = y_ref.shape[4]
    coarse_z, coarse_x = c_ref.shape[0], c_ref.shape[1]
    at_y = lax.broadcasted_iota(jnp.int32, (cells_y, 3 * half_y), 0)
    col = lax.broadcasted_iota(jnp.int32, (cells_y, 3 * half_y), 1)
    target = 2 * (col % half_y) + col // half_y - 1
    target = jnp.where(target < 0, target + cells_y, target)
    pick = (at_y == target).astype(jnp.bfloat16)
    y_ref[:, 0] = jnp.zeros(y_ref[:, 0].shape, y_ref.dtype)
    for zg in range(planes_z + 1):
        source = below_ref[0] if zg == 0 else gp_ref[zg - 1]
        picked = jnp.dot(source, pick, preferred_element_type=jnp.float32).astype(y_ref.dtype)
        for dy in range(3):
            part = picked[:, dy * half_y : (dy + 1) * half_y]
            y_ref[zg, 1:, dy] = part.reshape(rows_x, part_ch, half_y)
    gu_ref[...] = jnp.zeros(gu_ref.shape, gu_ref.dtype)

    def body(step, carry):
        iz = step // coarse_x
        ix = step % coarse_x
        crow = c_ref[iz, ix]
        total = jnp.zeros(gc_ref.shape[2:], jnp.float32)
        for dz in range(3):
            block = y_ref[2 * iz + dz, pl.ds(2 * ix, 3)]
            block = block.reshape(9 * part_ch, half_y)
            total = total + jnp.dot(u_ref[dz], block, preferred_element_type=jnp.float32)
            gu_ref[dz] += lax.dot_general(
                block, crow, (((1,), (1,)), ((), ())), preferred_element_type=jnp.float32
            )
        gc_ref[iz, ix] = total
        return carry

    lax.fori_loop(0, coarse_z * coarse_x, body, 0)


def local(coarse, saved_pre, out_grad, up_weight, refine_weight):
    part_ch = saved_pre.shape[0]
    planes_z = saved_pre.shape[1]
    planes_x = saved_pre.shape[2]
    cells_y = saved_pre.shape[3]
    all_ch = part_ch * lax.axis_size("ch")
    channel_start = lax.axis_index("ch") * part_ch

    rimmed_local = padded(out_grad, ((("gz", "sec"), 1),), 2)
    every_channel = lax.all_gather(rimmed_local, "ch", axis=0, tiled=True)
    rimmed = jnp.pad(every_channel, ((0, 0), (0, 0), (2, 2), (0, 0)))
    halo_z, halo_x = rimmed.shape[1], rimmed.shape[2]
    rimmed = rimmed.reshape(all_ch, halo_z // 2, 2, halo_x // 2, 2, cells_y)
    rimmed = jnp.transpose(rimmed, (2, 1, 4, 3, 0, 5))
    pre_rows = jnp.transpose(saved_pre, (1, 2, 0, 3))

    refine_cols = lax.dynamic_slice_in_dim(refine_weight, channel_start, part_ch, 2)
    refine_w = refine_cols.reshape(3, 3, 3, all_ch, part_ch)[:, ::-1]
    refine_w = jnp.transpose(refine_w, (0, 2, 4, 1, 3)).reshape(3, 3 * part_ch, 3 * all_ch)

    grad_pre, refine_acc = pl.pallas_call(
        fine_kernel,
        out_shape=(
            jax.ShapeDtypeStruct((planes_z, planes_x, part_ch, cells_y), jnp.bfloat16),
            jax.ShapeDtypeStruct((3, 3 * all_ch, 3 * part_ch), jnp.float32),
        ),
        in_specs=vmem_specs(3),
        out_specs=tuple(vmem_specs(2)),
    )(rimmed, pre_rows, refine_w)
    refine_terms = refine_acc.reshape(3, 3, all_ch, 3, part_ch)[:, ::-1]
    refine_terms = jnp.transpose(refine_terms, (0, 1, 3, 2, 4)).reshape(27, all_ch, part_ch)
    refine_summed = summed_over_slabs(refine_terms, ("gz", "sec"))

    grad_rows = grad_pre.reshape(planes_z, planes_x * part_ch, cells_y)
    below_z = passed_along(grad_rows[planes_z - 1 :], ("gz", "sec"), 1)

    all_coarse = lax.all_gather(coarse, "ch", axis=0, tiled=True)
    coarse_in = all_coarse.shape[0]
    coarse_z, coarse_x, cells_yc = coarse.shape[1], coarse.shape[2], coarse.shape[3]
    coarse_rows = jnp.transpose(all_coarse, (1, 2, 0, 3))
    up_rows = lax.dynamic_slice_in_dim(up_weight, channel_start, part_ch, 1)
    up_w = jnp.transpose(up_rows.reshape(3, 9, part_ch, coarse_in), (0, 3, 1, 2))
    up_w = up_w.reshape(3, coarse_in, 9 * part_ch)

    coarse_acc, up_acc = pl.pallas_call(
        coarse_kernel,
        out_shape=(
            jax.ShapeDtypeStruct((coarse_z, coarse_x, coarse_in, cells_yc), jnp.float32),
            jax.ShapeDtypeStruct((3, 9 * part_ch, coarse_in), jnp.float32),
        ),
        in_specs=vmem_specs(4),
        out_specs=tuple(vmem_specs(2)),
        scratch_shapes=[
            pltpu.VMEM((planes_z + 1, planes_x + 1, 3, part_ch, cells_yc), jnp.bfloat16)
        ],
    )(grad_rows, below_z, coarse_rows, up_w)
    up_terms = up_acc.reshape(27, part_ch, coarse_in)
    running = jnp.transpose(coarse_acc, (2, 0, 1, 3))

    coarse_summed = lax.psum_scatter(running, "ch", scatter_dimension=0, tiled=True)
    grad_coarse = coarse_summed.astype(jnp.bfloat16)
    up_summed = summed_over_slabs(up_terms, ("gz", "sec"))
    fine_total = planes_z * lax.axis_size("gz") * lax.axis_size("sec") * planes_x * cells_y
    coarse_total = fine_total // 8
    grad_up = up_summed * float(coarse_total) ** (-0.5)
    grad_refine = refine_summed * float(fine_total) ** (-0.5)
    return (grad_coarse, grad_up, grad_refine)


def solution(mesh):
    placed = (
        P("ch", ("groups", "gz", "sec"), None, None),
        P("ch", ("groups", "gz", "sec"), None, None),
        P("ch", ("groups", "gz", "sec"), None, None),
        P(),
        P(),
    )
    return jax.shard_map(
        local,
        mesh=mesh,
        in_specs=placed,
        out_specs=(
            P("ch", ("groups", "gz", "sec"), None, None),
            P("groups", "ch", None),
            P("groups", None, "ch"),
        ),
        check_vma=False,
    )
```

```python
import functools

import jax
import jax.numpy as jnp
from jax import lax
from jax.experimental import pallas as pl
from jax.experimental.pallas import tpu as pltpu
from jax.sharding import PartitionSpec as P

leak_slope = 0.2


def padded(block, sides, width):
    for axis, dim in sides:
        count = lax.axis_size(axis)
        forward = [(i, i + 1) for i in range(count - 1)]
        forward.append((count - 1, 0))
        backward = [(target, source) for source, target in forward]
        low = lax.ppermute(
            lax.slice_in_dim(block, block.shape[dim] - width, None, axis=dim), axis, forward
        )
        high = lax.ppermute(lax.slice_in_dim(block, 0, width, axis=dim), axis, backward)
        block = jnp.concatenate([low, block, high], axis=dim)
    return block


def passed_along(block, axis, distance):
    devices = range(lax.axis_size(axis))
    route = [((i - distance) % len(devices), i) for i in devices]
    return lax.ppermute(block, axis, route)


def summed_over_slabs(block, axis):
    count = lax.axis_size(axis)
    if count & (count - 1):
        return lax.psum(block, axis)
    step = 1
    while step < count:
        route = [(i, i ^ step) for i in range(count)]
        block = block + lax.ppermute(block, axis, route)
        step *= 2
    return block


def vmem_specs(count):
    return [pl.BlockSpec(memory_space=pltpu.VMEM)] * count


def fine_kernel(g_ref, sp_ref, w_ref, gp_ref, r_ref):
    planes_z, planes_x, part_ch, cells_y = sp_ref.shape
    wide = g_ref.shape[4]
    r_ref[...] = jnp.zeros(r_ref.shape, r_ref.dtype)

    def body(step, carry):
        z = step // planes_x
        x = step % planes_x
        pre_act = sp_ref[z, x].astype(jnp.float32)
        slopes = jnp.where(pre_act > 0, 1.0, leak_slope).astype(jnp.float32)
        hidden = (pre_act * slopes).astype(jnp.bfloat16).astype(jnp.float32)
        rolled = jnp.concatenate(
            [pltpu.roll(hidden, 2, 1), hidden, pltpu.roll(hidden, cells_y - 2, 1)], axis=0
        ).astype(jnp.bfloat16)
        total = jnp.zeros((3 * part_ch, cells_y), jnp.float32)
        for dz in range(3):
            block = g_ref[z % 2, z // 2 + 2 - dz, x % 2, pl.ds(x // 2, 3)]
            block = block.reshape(3 * wide, cells_y)
            total = total + jnp.dot(w_ref[dz], block, preferred_element_type=jnp.float32)
            r_ref[dz] += lax.dot_general(
                block, rolled, (((1,), (1,)), ((), ())), preferred_element_type=jnp.float32
            )
        grad_hidden = (
            pltpu.roll(total[:part_ch], cells_y - 2, 1)
            + total[part_ch : 2 * part_ch]
            + pltpu.roll(total[2 * part_ch :], 2, 1)
        )
        gp_ref[z, x] = (grad_hidden * slopes).astype(gp_ref.dtype)
        return carry

    lax.fori_loop(0, planes_z * planes_x, body, 0)


def coarse_kernel(gp_ref, below_ref, c_ref, u_ref, gc_ref, gu_ref, y_ref):
    planes_z = gp_ref.shape[0]
    cells_y = gp_ref.shape[2]
    rows_x = y_ref.shape[1] - 1
    part_ch = y_ref.shape[3]
    half_y = y_ref.shape[4]
    coarse_z, coarse_x = c_ref.shape[0], c_ref.shape[1]
    at_y = lax.broadcasted_iota(jnp.int32, (cells_y, 3 * half_y), 0)
    col = lax.broadcasted_iota(jnp.int32, (cells_y, 3 * half_y), 1)
    target = 2 * (col % half_y) + col // half_y - 1
    target = jnp.where(target < 0, target + cells_y, target)
    pick = (at_y == target).astype(jnp.bfloat16)
    y_ref[:, 0] = jnp.zeros(y_ref[:, 0].shape, y_ref.dtype)
    for zg in range(planes_z + 1):
        source = below_ref[0] if zg == 0 else gp_ref[zg - 1]
        picked = jnp.dot(source, pick, preferred_element_type=jnp.float32).astype(y_ref.dtype)
        for dy in range(3):
            part = picked[:, dy * half_y : (dy + 1) * half_y]
            y_ref[zg, 1:, dy] = part.reshape(rows_x, part_ch, half_y)
    gu_ref[...] = jnp.zeros(gu_ref.shape, gu_ref.dtype)

    def body(step, carry):
        iz = step // coarse_x
        ix = step % coarse_x
        crow = c_ref[iz, ix]
        total = jnp.zeros(gc_ref.shape[2:], jnp.float32)
        for dz in range(3):
            block = y_ref[2 * iz + dz, pl.ds(2 * ix, 3)]
            block = block.reshape(9 * part_ch, half_y)
            total = total + jnp.dot(u_ref[dz], block, preferred_element_type=jnp.float32)
            gu_ref[dz] += lax.dot_general(
                block, crow, (((1,), (1,)), ((), ())), preferred_element_type=jnp.float32
            )
        gc_ref[iz, ix] = total
        return carry

    lax.fori_loop(0, coarse_z * coarse_x, body, 0)


def local(coarse, saved_pre, out_grad, up_weight, refine_weight):
    part_ch = saved_pre.shape[0]
    planes_z = saved_pre.shape[1]
    planes_x = saved_pre.shape[2]
    cells_y = saved_pre.shape[3]
    all_ch = part_ch * lax.axis_size("ch")
    channel_start = lax.axis_index("ch") * part_ch

    rimmed_local = padded(out_grad, ((("gz", "sec"), 1),), 2)
    every_channel = lax.all_gather(rimmed_local, "ch", axis=0, tiled=True)
    rimmed = jnp.pad(every_channel, ((0, 0), (0, 0), (2, 2), (0, 0)))
    halo_z, halo_x = rimmed.shape[1], rimmed.shape[2]
    rimmed = rimmed.reshape(all_ch, halo_z // 2, 2, halo_x // 2, 2, cells_y)
    rimmed = jnp.transpose(rimmed, (2, 1, 4, 3, 0, 5))
    pre_rows = jnp.transpose(saved_pre, (1, 2, 0, 3))

    refine_cols = lax.dynamic_slice_in_dim(refine_weight, channel_start, part_ch, 2)
    refine_w = refine_cols.reshape(3, 3, 3, all_ch, part_ch)[:, ::-1]
    refine_w = jnp.transpose(refine_w, (0, 2, 4, 1, 3)).reshape(3, 3 * part_ch, 3 * all_ch)

    grad_pre, refine_acc = pl.pallas_call(
        fine_kernel,
        out_shape=(
            jax.ShapeDtypeStruct((planes_z, planes_x, part_ch, cells_y), jnp.bfloat16),
            jax.ShapeDtypeStruct((3, 3 * all_ch, 3 * part_ch), jnp.float32),
        ),
        in_specs=vmem_specs(3),
        out_specs=tuple(vmem_specs(2)),
    )(rimmed, pre_rows, refine_w)
    refine_terms = refine_acc.reshape(3, 3, all_ch, 3, part_ch)[:, ::-1]
    refine_terms = jnp.transpose(refine_terms, (0, 1, 3, 2, 4)).reshape(27, all_ch, part_ch)

    grad_rows = grad_pre.reshape(planes_z, planes_x * part_ch, cells_y)
    below_z = passed_along(grad_rows[planes_z - 1 :], ("gz", "sec"), 1)

    all_coarse = lax.all_gather(coarse, "ch", axis=0, tiled=True)
    coarse_in = all_coarse.shape[0]
    coarse_z, coarse_x, cells_yc = coarse.shape[1], coarse.shape[2], coarse.shape[3]
    coarse_rows = jnp.transpose(all_coarse, (1, 2, 0, 3))
    up_rows = lax.dynamic_slice_in_dim(up_weight, channel_start, part_ch, 1)
    up_w = jnp.transpose(up_rows.reshape(3, 9, part_ch, coarse_in), (0, 3, 1, 2))
    up_w = up_w.reshape(3, coarse_in, 9 * part_ch)

    coarse_acc, up_acc = pl.pallas_call(
        coarse_kernel,
        out_shape=(
            jax.ShapeDtypeStruct((coarse_z, coarse_x, coarse_in, cells_yc), jnp.float32),
            jax.ShapeDtypeStruct((3, 9 * part_ch, coarse_in), jnp.float32),
        ),
        in_specs=vmem_specs(4),
        out_specs=tuple(vmem_specs(2)),
        scratch_shapes=[
            pltpu.VMEM((planes_z + 1, planes_x + 1, 3, part_ch, cells_yc), jnp.bfloat16)
        ],
    )(grad_rows, below_z, coarse_rows, up_w)
    up_terms = up_acc.reshape(27, part_ch, coarse_in)
    running = jnp.transpose(coarse_acc, (2, 0, 1, 3))

    coarse_summed = lax.psum_scatter(running, "ch", scatter_dimension=0, tiled=True)
    grad_coarse = coarse_summed.astype(jnp.bfloat16)
    flat = jnp.concatenate([up_terms.reshape(-1), refine_terms.reshape(-1)])
    flat = summed_over_slabs(flat, ("gz", "sec"))
    up_summed = flat[: up_terms.size].reshape(up_terms.shape)
    refine_summed = flat[up_terms.size :].reshape(refine_terms.shape)
    fine_total = planes_z * lax.axis_size("gz") * lax.axis_size("sec") * planes_x * cells_y
    coarse_total = fine_total // 8
    grad_up = up_summed * float(coarse_total) ** (-0.5)
    grad_refine = refine_summed * float(fine_total) ** (-0.5)
    return (grad_coarse, grad_up, grad_refine)


def solution(mesh):
    placed = (
        P("ch", ("groups", "gz", "sec"), None, None),
        P("ch", ("groups", "gz", "sec"), None, None),
        P("ch", ("groups", "gz", "sec"), None, None),
        P(),
        P(),
    )
    return jax.shard_map(
        local,
        mesh=mesh,
        in_specs=placed,
        out_specs=(
            P("ch", ("groups", "gz", "sec"), None, None),
            P("groups", "ch", None),
            P("groups", None, "ch"),
        ),
        check_vma=False,
    )
```

```python
import functools

import jax
import jax.numpy as jnp
from jax import lax
from jax.experimental import pallas as pl
from jax.experimental.pallas import tpu as pltpu
from jax.sharding import PartitionSpec as P

leak_slope = 0.2


def padded(block, sides, width):
    for axis, dim in sides:
        count = lax.axis_size(axis)
        forward = [(i, i + 1) for i in range(count - 1)]
        forward.append((count - 1, 0))
        backward = [(target, source) for source, target in forward]
        low = lax.ppermute(
            lax.slice_in_dim(block, block.shape[dim] - width, None, axis=dim), axis, forward
        )
        high = lax.ppermute(lax.slice_in_dim(block, 0, width, axis=dim), axis, backward)
        block = jnp.concatenate([low, block, high], axis=dim)
    return block


def passed_along(block, axis, distance):
    devices = range(lax.axis_size(axis))
    route = [((i - distance) % len(devices), i) for i in devices]
    return lax.ppermute(block, axis, route)


def summed_over_slabs(block, axis):
    count = lax.axis_size(axis)
    if count & (count - 1):
        return lax.psum(block, axis)
    step = 1
    while step < count:
        route = [(i, i ^ step) for i in range(count)]
        block = block + lax.ppermute(block, axis, route)
        step *= 2
    return block


def vmem_specs(count):
    return [pl.BlockSpec(memory_space=pltpu.VMEM)] * count


def fine_kernel(g_ref, sp_ref, w_ref, gp_ref, r_ref):
    planes_z, planes_x, part_ch, cells_y = sp_ref.shape
    wide = g_ref.shape[4]
    r_ref[...] = jnp.zeros(r_ref.shape, r_ref.dtype)

    def body(step, carry):
        z = step // planes_x
        x = step % planes_x
        pre_act = sp_ref[z, x].astype(jnp.float32)
        slopes = jnp.where(pre_act > 0, 1.0, leak_slope).astype(jnp.float32)
        hidden = (pre_act * slopes).astype(jnp.bfloat16).astype(jnp.float32)
        rolled = jnp.concatenate(
            [pltpu.roll(hidden, 2, 1), hidden, pltpu.roll(hidden, cells_y - 2, 1)], axis=0
        ).astype(jnp.bfloat16)
        total = jnp.zeros((3 * part_ch, cells_y), jnp.float32)
        for dz in range(3):
            block = g_ref[z % 2, z // 2 + 2 - dz, x % 2, pl.ds(x // 2, 3)]
            block = block.reshape(3 * wide, cells_y)
            total = total + jnp.dot(w_ref[dz], block, preferred_element_type=jnp.float32)
            r_ref[dz] += lax.dot_general(
                block, rolled, (((1,), (1,)), ((), ())), preferred_element_type=jnp.float32
            )
        grad_hidden = (
            pltpu.roll(total[:part_ch], cells_y - 2, 1)
            + total[part_ch : 2 * part_ch]
            + pltpu.roll(total[2 * part_ch :], 2, 1)
        )
        gp_ref[z, x] = (grad_hidden * slopes).astype(gp_ref.dtype)
        return carry

    lax.fori_loop(0, planes_z * planes_x, body, 0)


def coarse_kernel(gp_ref, below_ref, c_ref, u_ref, gc_ref, gu_ref, y_ref):
    planes_z = gp_ref.shape[0]
    cells_y = gp_ref.shape[2]
    rows_x = y_ref.shape[1] - 1
    part_ch = y_ref.shape[3]
    half_y = y_ref.shape[4]
    coarse_z, coarse_x = c_ref.shape[0], c_ref.shape[1]
    at_y = lax.broadcasted_iota(jnp.int32, (cells_y, 3 * half_y), 0)
    col = lax.broadcasted_iota(jnp.int32, (cells_y, 3 * half_y), 1)
    target = 2 * (col % half_y) + col // half_y - 1
    target = jnp.where(target < 0, target + cells_y, target)
    pick = (at_y == target).astype(jnp.bfloat16)
    y_ref[:, 0] = jnp.zeros(y_ref[:, 0].shape, y_ref.dtype)
    for zg in range(planes_z + 1):
        source = below_ref[0] if zg == 0 else gp_ref[zg - 1]
        picked = jnp.dot(source, pick, preferred_element_type=jnp.float32).astype(y_ref.dtype)
        for dy in range(3):
            part = picked[:, dy * half_y : (dy + 1) * half_y]
            y_ref[zg, 1:, dy] = part.reshape(rows_x, part_ch, half_y)
    gu_ref[...] = jnp.zeros(gu_ref.shape, gu_ref.dtype)

    def body(step, carry):
        iz = step // coarse_x
        ix = step % coarse_x
        crow = c_ref[iz, ix]
        total = jnp.zeros(gc_ref.shape[2:], jnp.float32)
        for dz in range(3):
            block = y_ref[2 * iz + dz, pl.ds(2 * ix, 3)]
            block = block.reshape(9 * part_ch, half_y)
            total = total + jnp.dot(u_ref[dz], block, preferred_element_type=jnp.float32)
            gu_ref[dz] += lax.dot_general(
                block, crow, (((1,), (1,)), ((), ())), preferred_element_type=jnp.float32
            )
        gc_ref[iz, ix] = total
        return carry

    lax.fori_loop(0, coarse_z * coarse_x, body, 0)


def local(coarse, saved_pre, out_grad, up_weight, refine_weight):
    part_ch = saved_pre.shape[0]
    planes_z = saved_pre.shape[1]
    planes_x = saved_pre.shape[2]
    cells_y = saved_pre.shape[3]
    all_ch = part_ch * lax.axis_size("ch")
    channel_start = lax.axis_index("ch") * part_ch

    rows = jnp.transpose(out_grad, (1, 2, 0, 3))
    count = lax.axis_size(("gz", "sec"))
    forward = [(i, (i + 1) % count) for i in range(count)]
    backward = [(target, source) for source, target in forward]
    swap = [(i, i ^ 1) for i in range(lax.axis_size("ch"))]
    low = lax.ppermute(rows[planes_z - 2 :], ("gz", "sec"), forward)
    high = lax.ppermute(rows[:2], ("gz", "sec"), backward)
    rows_other = lax.ppermute(rows, "ch", swap)
    low_other = lax.ppermute(low, "ch", swap)
    high_other = lax.ppermute(high, "ch", swap)
    mine = jnp.concatenate([low, rows, high], axis=0)
    other = jnp.concatenate([low_other, rows_other, high_other], axis=0)
    rimmed = jnp.concatenate([mine, other], axis=2)
    rimmed = jnp.pad(rimmed, ((0, 0), (2, 2), (0, 0), (0, 0)))
    halo_z, halo_x = rimmed.shape[0], rimmed.shape[1]
    rimmed = rimmed.reshape(halo_z // 2, 2, halo_x // 2, 2, all_ch, cells_y)
    rimmed = jnp.transpose(rimmed, (1, 0, 3, 2, 4, 5))
    pre_rows = jnp.transpose(saved_pre, (1, 2, 0, 3))

    refine_cols = lax.dynamic_slice_in_dim(refine_weight, channel_start, part_ch, 2)
    refine_cols = jnp.roll(refine_cols, -channel_start, axis=1)
    refine_w = refine_cols.reshape(3, 3, 3, all_ch, part_ch)[:, ::-1]
    refine_w = jnp.transpose(refine_w, (0, 2, 4, 1, 3)).reshape(3, 3 * part_ch, 3 * all_ch)

    grad_pre, refine_acc = pl.pallas_call(
        fine_kernel,
        out_shape=(
            jax.ShapeDtypeStruct((planes_z, planes_x, part_ch, cells_y), jnp.bfloat16),
            jax.ShapeDtypeStruct((3, 3 * all_ch, 3 * part_ch), jnp.float32),
        ),
        in_specs=vmem_specs(3),
        out_specs=tuple(vmem_specs(2)),
    )(rimmed, pre_rows, refine_w)
    refine_terms = refine_acc.reshape(3, 3, all_ch, 3, part_ch)[:, ::-1]
    refine_terms = jnp.transpose(refine_terms, (0, 1, 3, 2, 4)).reshape(27, all_ch, part_ch)
    refine_terms = jnp.roll(refine_terms, channel_start, axis=1)

    grad_rows = grad_pre.reshape(planes_z, planes_x * part_ch, cells_y)
    below_z = passed_along(grad_rows[planes_z - 1 :], ("gz", "sec"), 1)

    all_coarse = lax.all_gather(coarse, "ch", axis=0, tiled=True)
    coarse_in = all_coarse.shape[0]
    coarse_z, coarse_x, cells_yc = coarse.shape[1], coarse.shape[2], coarse.shape[3]
    coarse_rows = jnp.transpose(all_coarse, (1, 2, 0, 3))
    up_rows = lax.dynamic_slice_in_dim(up_weight, channel_start, part_ch, 1)
    up_w = jnp.transpose(up_rows.reshape(3, 9, part_ch, coarse_in), (0, 3, 1, 2))
    up_w = up_w.reshape(3, coarse_in, 9 * part_ch)

    coarse_acc, up_acc = pl.pallas_call(
        coarse_kernel,
        out_shape=(
            jax.ShapeDtypeStruct((coarse_z, coarse_x, coarse_in, cells_yc), jnp.float32),
            jax.ShapeDtypeStruct((3, 9 * part_ch, coarse_in), jnp.float32),
        ),
        in_specs=vmem_specs(4),
        out_specs=tuple(vmem_specs(2)),
        scratch_shapes=[
            pltpu.VMEM((planes_z + 1, planes_x + 1, 3, part_ch, cells_yc), jnp.bfloat16)
        ],
    )(grad_rows, below_z, coarse_rows, up_w)
    up_terms = up_acc.reshape(27, part_ch, coarse_in)
    running = jnp.transpose(coarse_acc, (2, 0, 1, 3))

    coarse_summed = lax.psum_scatter(running, "ch", scatter_dimension=0, tiled=True)
    grad_coarse = coarse_summed.astype(jnp.bfloat16)
    flat = jnp.concatenate([up_terms.reshape(-1), refine_terms.reshape(-1)])
    flat = summed_over_slabs(flat, ("gz", "sec"))
    up_summed = flat[: up_terms.size].reshape(up_terms.shape)
    refine_summed = flat[up_terms.size :].reshape(refine_terms.shape)
    fine_total = planes_z * lax.axis_size("gz") * lax.axis_size("sec") * planes_x * cells_y
    coarse_total = fine_total // 8
    grad_up = up_summed * float(coarse_total) ** (-0.5)
    grad_refine = refine_summed * float(fine_total) ** (-0.5)
    return (grad_coarse, grad_up, grad_refine)


def solution(mesh):
    placed = (
        P("ch", ("groups", "gz", "sec"), None, None),
        P("ch", ("groups", "gz", "sec"), None, None),
        P("ch", ("groups", "gz", "sec"), None, None),
        P(),
        P(),
    )
    return jax.shard_map(
        local,
        mesh=mesh,
        in_specs=placed,
        out_specs=(
            P("ch", ("groups", "gz", "sec"), None, None),
            P("groups", "ch", None),
            P("groups", None, "ch"),
        ),
        check_vma=False,
    )
```

```python
import functools

import jax
import jax.numpy as jnp
from jax import lax
from jax.experimental import pallas as pl
from jax.experimental.pallas import tpu as pltpu
from jax.sharding import PartitionSpec as P

leak_slope = 0.2


def padded(block, sides, width):
    for axis, dim in sides:
        count = lax.axis_size(axis)
        forward = [(i, i + 1) for i in range(count - 1)]
        forward.append((count - 1, 0))
        backward = [(target, source) for source, target in forward]
        low = lax.ppermute(
            lax.slice_in_dim(block, block.shape[dim] - width, None, axis=dim), axis, forward
        )
        high = lax.ppermute(lax.slice_in_dim(block, 0, width, axis=dim), axis, backward)
        block = jnp.concatenate([low, block, high], axis=dim)
    return block


def passed_along(block, axis, distance):
    devices = range(lax.axis_size(axis))
    route = [((i - distance) % len(devices), i) for i in devices]
    return lax.ppermute(block, axis, route)


def summed_over_slabs(block, axis):
    count = lax.axis_size(axis)
    if count & (count - 1):
        return lax.psum(block, axis)
    step = 1
    while step < count:
        route = [(i, i ^ step) for i in range(count)]
        block = block + lax.ppermute(block, axis, route)
        step *= 2
    return block


def vmem_specs(count):
    return [pl.BlockSpec(memory_space=pltpu.VMEM)] * count


def fine_kernel(g_ref, sp_ref, w_ref, gp_ref, r_ref):
    planes_z, planes_x, part_ch, cells_y = sp_ref.shape
    wide = g_ref.shape[4]
    r_ref[...] = jnp.zeros(r_ref.shape, r_ref.dtype)

    def body(step, carry):
        z = step // planes_x
        x = step % planes_x
        pre_act = sp_ref[z, x].astype(jnp.float32)
        slopes = jnp.where(pre_act > 0, 1.0, leak_slope).astype(jnp.float32)
        hidden = (pre_act * slopes).astype(jnp.bfloat16).astype(jnp.float32)
        rolled = jnp.concatenate(
            [pltpu.roll(hidden, 2, 1), hidden, pltpu.roll(hidden, cells_y - 2, 1)], axis=0
        ).astype(jnp.bfloat16)
        total = jnp.zeros((3 * part_ch, cells_y), jnp.float32)
        for dz in range(3):
            block = g_ref[z % 2, z // 2 + 2 - dz, x % 2, pl.ds(x // 2, 3)]
            block = block.reshape(3 * wide, cells_y)
            total = total + jnp.dot(w_ref[dz], block, preferred_element_type=jnp.float32)
            r_ref[dz] += lax.dot_general(
                block, rolled, (((1,), (1,)), ((), ())), preferred_element_type=jnp.float32
            )
        grad_hidden = (
            pltpu.roll(total[:part_ch], cells_y - 2, 1)
            + total[part_ch : 2 * part_ch]
            + pltpu.roll(total[2 * part_ch :], 2, 1)
        )
        gp_ref[z, x] = (grad_hidden * slopes).astype(gp_ref.dtype)
        return carry

    lax.fori_loop(0, planes_z * planes_x, body, 0)


def coarse_kernel(gp_ref, below_ref, c_ref, u_ref, gc_ref, gu_ref, y_ref):
    planes_z = gp_ref.shape[0]
    cells_y = gp_ref.shape[2]
    rows_x = y_ref.shape[1] - 1
    part_ch = y_ref.shape[3]
    half_y = y_ref.shape[4]
    coarse_z, coarse_x = c_ref.shape[0], c_ref.shape[1]
    at_y = lax.broadcasted_iota(jnp.int32, (cells_y, 3 * half_y), 0)
    col = lax.broadcasted_iota(jnp.int32, (cells_y, 3 * half_y), 1)
    target = 2 * (col % half_y) + col // half_y - 1
    target = jnp.where(target < 0, target + cells_y, target)
    pick = (at_y == target).astype(jnp.bfloat16)
    y_ref[:, 0] = jnp.zeros(y_ref[:, 0].shape, y_ref.dtype)
    for zg in range(planes_z + 1):
        source = below_ref[0] if zg == 0 else gp_ref[zg - 1]
        picked = jnp.dot(source, pick, preferred_element_type=jnp.float32).astype(y_ref.dtype)
        for dy in range(3):
            part = picked[:, dy * half_y : (dy + 1) * half_y]
            y_ref[zg, 1:, dy] = part.reshape(rows_x, part_ch, half_y)
    gu_ref[...] = jnp.zeros(gu_ref.shape, gu_ref.dtype)

    def body(step, carry):
        iz = step // coarse_x
        ix = step % coarse_x
        crow = c_ref[iz, ix]
        total = jnp.zeros(gc_ref.shape[2:], jnp.float32)
        for dz in range(3):
            block = y_ref[2 * iz + dz, pl.ds(2 * ix, 3)]
            block = block.reshape(9 * part_ch, half_y)
            total = total + jnp.dot(u_ref[dz], block, preferred_element_type=jnp.float32)
            gu_ref[dz] += lax.dot_general(
                block, crow, (((1,), (1,)), ((), ())), preferred_element_type=jnp.float32
            )
        gc_ref[iz, ix] = total
        return carry

    lax.fori_loop(0, coarse_z * coarse_x, body, 0)


def local(coarse, saved_pre, out_grad, up_weight, refine_weight):
    part_ch = saved_pre.shape[0]
    planes_z = saved_pre.shape[1]
    planes_x = saved_pre.shape[2]
    cells_y = saved_pre.shape[3]
    all_ch = part_ch * lax.axis_size("ch")
    channel_start = lax.axis_index("ch") * part_ch

    rows = jnp.transpose(out_grad, (1, 2, 0, 3))
    count = lax.axis_size(("gz", "sec"))
    forward = [(i, (i + 1) % count) for i in range(count)]
    backward = [(target, source) for source, target in forward]
    swap = [(i, i ^ 1) for i in range(lax.axis_size("ch"))]
    low = lax.ppermute(rows[planes_z - 2 :], ("gz", "sec"), forward)
    high = lax.ppermute(rows[:2], ("gz", "sec"), backward)
    rows_other = lax.ppermute(rows, "ch", swap)
    low_other = lax.ppermute(low, "ch", swap)
    high_other = lax.ppermute(high, "ch", swap)
    mine = jnp.concatenate([low, rows, high], axis=0)
    other = jnp.concatenate([low_other, rows_other, high_other], axis=0)
    rimmed = jnp.concatenate([mine, other], axis=2)
    rimmed = jnp.pad(rimmed, ((0, 0), (2, 2), (0, 0), (0, 0)))
    halo_z, halo_x = rimmed.shape[0], rimmed.shape[1]
    rimmed = rimmed.reshape(halo_z // 2, 2, halo_x // 2, 2, all_ch, cells_y)
    rimmed = jnp.transpose(rimmed, (1, 0, 3, 2, 4, 5))
    pre_rows = jnp.transpose(saved_pre, (1, 2, 0, 3))

    refine_cols = lax.dynamic_slice_in_dim(refine_weight, channel_start, part_ch, 2)
    refine_cols = jnp.roll(refine_cols, -channel_start, axis=1)
    refine_w = refine_cols.reshape(3, 3, 3, all_ch, part_ch)[:, ::-1]
    refine_w = jnp.transpose(refine_w, (0, 2, 4, 1, 3)).reshape(3, 3 * part_ch, 3 * all_ch)

    grad_pre, refine_acc = pl.pallas_call(
        fine_kernel,
        out_shape=(
            jax.ShapeDtypeStruct((planes_z, planes_x, part_ch, cells_y), jnp.bfloat16),
            jax.ShapeDtypeStruct((3, 3 * all_ch, 3 * part_ch), jnp.float32),
        ),
        in_specs=vmem_specs(3),
        out_specs=tuple(vmem_specs(2)),
    )(rimmed, pre_rows, refine_w)
    refine_terms = refine_acc.reshape(3, 3, all_ch, 3, part_ch)[:, ::-1]
    refine_terms = jnp.transpose(refine_terms, (0, 1, 3, 2, 4)).reshape(27, all_ch, part_ch)
    refine_terms = jnp.roll(refine_terms, channel_start, axis=1)

    grad_rows = grad_pre.reshape(planes_z, planes_x * part_ch, cells_y)
    below_z = passed_along(grad_rows[planes_z - 1 :], ("gz", "sec"), 1)

    coarse_own = jnp.transpose(coarse, (1, 2, 0, 3))
    coarse_rows = jnp.concatenate([coarse_own, lax.ppermute(coarse_own, "ch", swap)], axis=2)
    coarse_in = coarse_rows.shape[2]
    coarse_start = lax.axis_index("ch") * coarse.shape[0]
    coarse_z, coarse_x, cells_yc = coarse.shape[1], coarse.shape[2], coarse.shape[3]
    up_rows = lax.dynamic_slice_in_dim(up_weight, channel_start, part_ch, 1)
    up_rows = jnp.roll(up_rows, -coarse_start, axis=2)
    up_w = jnp.transpose(up_rows.reshape(3, 9, part_ch, coarse_in), (0, 3, 1, 2))
    up_w = up_w.reshape(3, coarse_in, 9 * part_ch)

    coarse_acc, up_acc = pl.pallas_call(
        coarse_kernel,
        out_shape=(
            jax.ShapeDtypeStruct((coarse_z, coarse_x, coarse_in, cells_yc), jnp.float32),
            jax.ShapeDtypeStruct((3, 9 * part_ch, coarse_in), jnp.float32),
        ),
        in_specs=vmem_specs(4),
        out_specs=tuple(vmem_specs(2)),
        scratch_shapes=[
            pltpu.VMEM((planes_z + 1, planes_x + 1, 3, part_ch, cells_yc), jnp.bfloat16)
        ],
    )(grad_rows, below_z, coarse_rows, up_w)
    up_terms = jnp.roll(up_acc.reshape(27, part_ch, coarse_in), coarse_start, axis=2)
    own_k = coarse.shape[0]
    received = lax.ppermute(coarse_acc[:, :, own_k:], "ch", swap)
    coarse_summed = coarse_acc[:, :, :own_k] + received
    grad_coarse = jnp.transpose(coarse_summed, (2, 0, 1, 3)).astype(jnp.bfloat16)
    flat = jnp.concatenate([up_terms.reshape(-1), refine_terms.reshape(-1)])
    flat = summed_over_slabs(flat, ("gz", "sec"))
    up_summed = flat[: up_terms.size].reshape(up_terms.shape)
    refine_summed = flat[up_terms.size :].reshape(refine_terms.shape)
    fine_total = planes_z * lax.axis_size("gz") * lax.axis_size("sec") * planes_x * cells_y
    coarse_total = fine_total // 8
    grad_up = up_summed * float(coarse_total) ** (-0.5)
    grad_refine = refine_summed * float(fine_total) ** (-0.5)
    return (grad_coarse, grad_up, grad_refine)


def solution(mesh):
    placed = (
        P("ch", ("groups", "gz", "sec"), None, None),
        P("ch", ("groups", "gz", "sec"), None, None),
        P("ch", ("groups", "gz", "sec"), None, None),
        P(),
        P(),
    )
    return jax.shard_map(
        local,
        mesh=mesh,
        in_specs=placed,
        out_specs=(
            P("ch", ("groups", "gz", "sec"), None, None),
            P("groups", "ch", None),
            P("groups", None, "ch"),
        ),
        check_vma=False,
    )
```

```python
import functools

import jax
import jax.numpy as jnp
from jax import lax
from jax.experimental import pallas as pl
from jax.experimental.pallas import tpu as pltpu
from jax.sharding import PartitionSpec as P

leak_slope = 0.2


def padded(block, sides, width):
    for axis, dim in sides:
        count = lax.axis_size(axis)
        forward = [(i, i + 1) for i in range(count - 1)]
        forward.append((count - 1, 0))
        backward = [(target, source) for source, target in forward]
        low = lax.ppermute(
            lax.slice_in_dim(block, block.shape[dim] - width, None, axis=dim), axis, forward
        )
        high = lax.ppermute(lax.slice_in_dim(block, 0, width, axis=dim), axis, backward)
        block = jnp.concatenate([low, block, high], axis=dim)
    return block


def passed_along(block, axis, distance):
    devices = range(lax.axis_size(axis))
    route = [((i - distance) % len(devices), i) for i in devices]
    return lax.ppermute(block, axis, route)


def summed_over_slabs(block, axis):
    count = lax.axis_size(axis)
    if count & (count - 1):
        return lax.psum(block, axis)
    step = 1
    while step < count:
        route = [(i, i ^ step) for i in range(count)]
        block = block + lax.ppermute(block, axis, route)
        step *= 2
    return block


def vmem_specs(count):
    return [pl.BlockSpec(memory_space=pltpu.VMEM)] * count


def fine_kernel(z_lo, z_hi, g_ref, sp_ref, w_ref, gp_ref, r_ref):
    planes_z, planes_x, part_ch, cells_y = sp_ref.shape
    wide = g_ref.shape[4]
    r_ref[...] = jnp.zeros(r_ref.shape, r_ref.dtype)

    def body(step, carry):
        z = z_lo + step // planes_x
        x = step % planes_x
        pre_act = sp_ref[z, x].astype(jnp.float32)
        slopes = jnp.where(pre_act > 0, 1.0, leak_slope).astype(jnp.float32)
        hidden = (pre_act * slopes).astype(jnp.bfloat16).astype(jnp.float32)
        rolled = jnp.concatenate(
            [pltpu.roll(hidden, 2, 1), hidden, pltpu.roll(hidden, cells_y - 2, 1)], axis=0
        ).astype(jnp.bfloat16)
        total = jnp.zeros((3 * part_ch, cells_y), jnp.float32)
        for dz in range(3):
            block = g_ref[z % 2, z // 2 + 2 - dz, x % 2, pl.ds(x // 2, 3)]
            block = block.reshape(3 * wide, cells_y)
            total = total + jnp.dot(w_ref[dz], block, preferred_element_type=jnp.float32)
            r_ref[dz] += lax.dot_general(
                block, rolled, (((1,), (1,)), ((), ())), preferred_element_type=jnp.float32
            )
        grad_hidden = (
            pltpu.roll(total[:part_ch], cells_y - 2, 1)
            + total[part_ch : 2 * part_ch]
            + pltpu.roll(total[2 * part_ch :], 2, 1)
        )
        gp_ref[z - z_lo, x] = (grad_hidden * slopes).astype(gp_ref.dtype)
        return carry

    lax.fori_loop(0, (z_hi - z_lo) * planes_x, body, 0)


def coarse_kernel(gp_ref, last_ref, below_ref, c_ref, u_ref, gc_ref, gu_ref, y_ref):
    planes_z = gp_ref.shape[0] + 1
    cells_y = gp_ref.shape[2]
    rows_x = y_ref.shape[1] - 1
    part_ch = y_ref.shape[3]
    half_y = y_ref.shape[4]
    coarse_z, coarse_x = c_ref.shape[0], c_ref.shape[1]
    at_y = lax.broadcasted_iota(jnp.int32, (cells_y, 3 * half_y), 0)
    col = lax.broadcasted_iota(jnp.int32, (cells_y, 3 * half_y), 1)
    target = 2 * (col % half_y) + col // half_y - 1
    target = jnp.where(target < 0, target + cells_y, target)
    pick = (at_y == target).astype(jnp.bfloat16)
    y_ref[:, 0] = jnp.zeros(y_ref[:, 0].shape, y_ref.dtype)
    for zg in range(planes_z + 1):
        if zg == 0:
            source = below_ref[0]
        elif zg == planes_z:
            source = last_ref[0]
        else:
            source = gp_ref[zg - 1]
        picked = jnp.dot(source, pick, preferred_element_type=jnp.float32).astype(y_ref.dtype)
        for dy in range(3):
            part = picked[:, dy * half_y : (dy + 1) * half_y]
            y_ref[zg, 1:, dy] = part.reshape(rows_x, part_ch, half_y)
    gu_ref[...] = jnp.zeros(gu_ref.shape, gu_ref.dtype)

    def body(step, carry):
        iz = step // coarse_x
        ix = step % coarse_x
        crow = c_ref[iz, ix]
        total = jnp.zeros(gc_ref.shape[2:], jnp.float32)
        for dz in range(3):
            block = y_ref[2 * iz + dz, pl.ds(2 * ix, 3)]
            block = block.reshape(9 * part_ch, half_y)
            total = total + jnp.dot(u_ref[dz], block, preferred_element_type=jnp.float32)
            gu_ref[dz] += lax.dot_general(
                block, crow, (((1,), (1,)), ((), ())), preferred_element_type=jnp.float32
            )
        gc_ref[iz, ix] = total
        return carry

    lax.fori_loop(0, coarse_z * coarse_x, body, 0)


def local(coarse, saved_pre, out_grad, up_weight, refine_weight):
    part_ch = saved_pre.shape[0]
    planes_z = saved_pre.shape[1]
    planes_x = saved_pre.shape[2]
    cells_y = saved_pre.shape[3]
    all_ch = part_ch * lax.axis_size("ch")
    channel_start = lax.axis_index("ch") * part_ch

    rows = jnp.transpose(out_grad, (1, 2, 0, 3))
    count = lax.axis_size(("gz", "sec"))
    forward = [(i, (i + 1) % count) for i in range(count)]
    backward = [(target, source) for source, target in forward]
    swap = [(i, i ^ 1) for i in range(lax.axis_size("ch"))]
    low = lax.ppermute(rows[planes_z - 2 :], ("gz", "sec"), forward)
    high = lax.ppermute(rows[:2], ("gz", "sec"), backward)
    rows_other = lax.ppermute(rows, "ch", swap)
    low_other = lax.ppermute(low, "ch", swap)
    high_other = lax.ppermute(high, "ch", swap)
    mine = jnp.concatenate([low, rows, high], axis=0)
    other = jnp.concatenate([low_other, rows_other, high_other], axis=0)
    rimmed = jnp.concatenate([mine, other], axis=2)
    rimmed = jnp.pad(rimmed, ((0, 0), (2, 2), (0, 0), (0, 0)))
    halo_z, halo_x = rimmed.shape[0], rimmed.shape[1]
    rimmed = rimmed.reshape(halo_z // 2, 2, halo_x // 2, 2, all_ch, cells_y)
    rimmed = jnp.transpose(rimmed, (1, 0, 3, 2, 4, 5))
    pre_rows = jnp.transpose(saved_pre, (1, 2, 0, 3))

    refine_cols = lax.dynamic_slice_in_dim(refine_weight, channel_start, part_ch, 2)
    refine_cols = jnp.roll(refine_cols, -channel_start, axis=1)
    refine_w = refine_cols.reshape(3, 3, 3, all_ch, part_ch)[:, ::-1]
    refine_w = jnp.transpose(refine_w, (0, 2, 4, 1, 3)).reshape(3, 3 * part_ch, 3 * all_ch)

    def fine_rows(z_lo, z_hi):
        return pl.pallas_call(
            functools.partial(fine_kernel, z_lo, z_hi),
            out_shape=(
                jax.ShapeDtypeStruct((z_hi - z_lo, planes_x, part_ch, cells_y), jnp.bfloat16),
                jax.ShapeDtypeStruct((3, 3 * all_ch, 3 * part_ch), jnp.float32),
            ),
            in_specs=vmem_specs(3),
            out_specs=tuple(vmem_specs(2)),
        )(rimmed, pre_rows, refine_w)

    grad_last, refine_last = fine_rows(planes_z - 1, planes_z)
    last_rows = grad_last.reshape(1, planes_x * part_ch, cells_y)
    below_z = passed_along(last_rows, ("gz", "sec"), 1)
    grad_main, refine_main = fine_rows(0, planes_z - 1)
    grad_rows = grad_main.reshape(planes_z - 1, planes_x * part_ch, cells_y)
    refine_acc = refine_main + refine_last
    refine_terms = refine_acc.reshape(3, 3, all_ch, 3, part_ch)[:, ::-1]
    refine_terms = jnp.transpose(refine_terms, (0, 1, 3, 2, 4)).reshape(27, all_ch, part_ch)
    refine_terms = jnp.roll(refine_terms, channel_start, axis=1)


    coarse_own = jnp.transpose(coarse, (1, 2, 0, 3))
    coarse_rows = jnp.concatenate([coarse_own, lax.ppermute(coarse_own, "ch", swap)], axis=2)
    coarse_in = coarse_rows.shape[2]
    coarse_start = lax.axis_index("ch") * coarse.shape[0]
    coarse_z, coarse_x, cells_yc = coarse.shape[1], coarse.shape[2], coarse.shape[3]
    up_rows = lax.dynamic_slice_in_dim(up_weight, channel_start, part_ch, 1)
    up_rows = jnp.roll(up_rows, -coarse_start, axis=2)
    up_w = jnp.transpose(up_rows.reshape(3, 9, part_ch, coarse_in), (0, 3, 1, 2))
    up_w = up_w.reshape(3, coarse_in, 9 * part_ch)

    coarse_acc, up_acc = pl.pallas_call(
        coarse_kernel,
        out_shape=(
            jax.ShapeDtypeStruct((coarse_z, coarse_x, coarse_in, cells_yc), jnp.float32),
            jax.ShapeDtypeStruct((3, 9 * part_ch, coarse_in), jnp.float32),
        ),
        in_specs=vmem_specs(5),
        out_specs=tuple(vmem_specs(2)),
        scratch_shapes=[
            pltpu.VMEM((planes_z + 1, planes_x + 1, 3, part_ch, cells_yc), jnp.bfloat16)
        ],
    )(grad_rows, last_rows, below_z, coarse_rows, up_w)
    up_terms = jnp.roll(up_acc.reshape(27, part_ch, coarse_in), coarse_start, axis=2)
    own_k = coarse.shape[0]
    received = lax.ppermute(coarse_acc[:, :, own_k:], "ch", swap)
    coarse_summed = coarse_acc[:, :, :own_k] + received
    grad_coarse = jnp.transpose(coarse_summed, (2, 0, 1, 3)).astype(jnp.bfloat16)
    flat = jnp.concatenate([up_terms.reshape(-1), refine_terms.reshape(-1)])
    flat = summed_over_slabs(flat, ("gz", "sec"))
    up_summed = flat[: up_terms.size].reshape(up_terms.shape)
    refine_summed = flat[up_terms.size :].reshape(refine_terms.shape)
    fine_total = planes_z * lax.axis_size("gz") * lax.axis_size("sec") * planes_x * cells_y
    coarse_total = fine_total // 8
    grad_up = up_summed * float(coarse_total) ** (-0.5)
    grad_refine = refine_summed * float(fine_total) ** (-0.5)
    return (grad_coarse, grad_up, grad_refine)


def solution(mesh):
    placed = (
        P("ch", ("groups", "gz", "sec"), None, None),
        P("ch", ("groups", "gz", "sec"), None, None),
        P("ch", ("groups", "gz", "sec"), None, None),
        P(),
        P(),
    )
    return jax.shard_map(
        local,
        mesh=mesh,
        in_specs=placed,
        out_specs=(
            P("ch", ("groups", "gz", "sec"), None, None),
            P("groups", "ch", None),
            P("groups", None, "ch"),
        ),
        check_vma=False,
    )
```

```python
import functools

import jax
import jax.numpy as jnp
from jax import lax
from jax.experimental import pallas as pl
from jax.experimental.pallas import tpu as pltpu
from jax.sharding import PartitionSpec as P

leak_slope = 0.2


def padded(block, sides, width):
    for axis, dim in sides:
        count = lax.axis_size(axis)
        forward = [(i, i + 1) for i in range(count - 1)]
        forward.append((count - 1, 0))
        backward = [(target, source) for source, target in forward]
        low = lax.ppermute(
            lax.slice_in_dim(block, block.shape[dim] - width, None, axis=dim), axis, forward
        )
        high = lax.ppermute(lax.slice_in_dim(block, 0, width, axis=dim), axis, backward)
        block = jnp.concatenate([low, block, high], axis=dim)
    return block


def passed_along(block, axis, distance):
    devices = range(lax.axis_size(axis))
    route = [((i - distance) % len(devices), i) for i in devices]
    return lax.ppermute(block, axis, route)


def summed_over_slabs(block, axis):
    count = lax.axis_size(axis)
    if count & (count - 1):
        return lax.psum(block, axis)
    step = 1
    while step < count:
        route = [(i, i ^ step) for i in range(count)]
        block = block + lax.ppermute(block, axis, route)
        step *= 2
    return block


def vmem_specs(count):
    return [pl.BlockSpec(memory_space=pltpu.VMEM)] * count


def fine_kernel(z_lo, z_hi, *refs):
    pieces = refs[:6]
    sp_ref, w_ref, gp_ref, r_ref, g_ref, sems = refs[6:]
    planes_z, planes_x, part_ch, cells_y = sp_ref.shape
    wide = g_ref.shape[3]
    low_count = pieces[0].shape[0]
    needed = sorted({z + 4 - 2 * dz for z in range(z_lo, z_hi) for dz in range(3)})
    edge = jnp.zeros(g_ref[:, :, 0:2].shape, g_ref.dtype)
    g_ref[:, :, 0:2] = edge
    g_ref[:, :, planes_x + 2 :] = edge
    copies = []
    for plane in needed:
        if plane < low_count:
            part, at = 0, plane
        elif plane < low_count + planes_z:
            part, at = 1, plane - low_count
        else:
            part, at = 2, plane - low_count - planes_z
        for half in range(2):
            copy = pltpu.make_async_copy(
                pieces[3 * half + part].at[at],
                g_ref.at[plane % 2, plane // 2, pl.ds(2, planes_x), pl.ds(half * part_ch, part_ch)],
                sems.at[len(copies)],
            )
            copy.start()
            copies.append(copy)
    r_ref[...] = jnp.zeros(r_ref.shape, r_ref.dtype)
    for copy in copies:
        copy.wait()

    def body(step, carry):
        z = z_lo + step // planes_x
        x = step % planes_x
        pre_act = sp_ref[z, x].astype(jnp.float32)
        slopes = jnp.where(pre_act > 0, 1.0, leak_slope).astype(jnp.float32)
        hidden = (pre_act * slopes).astype(jnp.bfloat16).astype(jnp.float32)
        rolled = jnp.concatenate(
            [pltpu.roll(hidden, 2, 1), hidden, pltpu.roll(hidden, cells_y - 2, 1)], axis=0
        ).astype(jnp.bfloat16)
        total = jnp.zeros((3 * part_ch, cells_y), jnp.float32)
        for dx in range(3):
            block = g_ref[z % 2, pl.ds(z // 2, 3), x + 4 - 2 * dx]
            block = block.reshape(3 * wide, cells_y)
            total = total + jnp.dot(w_ref[dx], block, preferred_element_type=jnp.float32)
            r_ref[dx] += lax.dot_general(
                block, rolled, (((1,), (1,)), ((), ())), preferred_element_type=jnp.float32
            )
        grad_hidden = (
            pltpu.roll(total[:part_ch], cells_y - 2, 1)
            + total[part_ch : 2 * part_ch]
            + pltpu.roll(total[2 * part_ch :], 2, 1)
        )
        gp_ref[z - z_lo, x] = (grad_hidden * slopes).astype(gp_ref.dtype)
        return carry

    lax.fori_loop(0, (z_hi - z_lo) * planes_x, body, 0)


def coarse_kernel(gp_ref, last_ref, below_ref, c_ref, u_ref, gc_ref, gu_ref, y_ref):
    planes_z = gp_ref.shape[0] + 1
    cells_y = gp_ref.shape[2]
    rows_x = y_ref.shape[1] - 1
    part_ch = y_ref.shape[3]
    half_y = y_ref.shape[4]
    coarse_z, coarse_x = c_ref.shape[0], c_ref.shape[1]
    at_y = lax.broadcasted_iota(jnp.int32, (cells_y, 3 * half_y), 0)
    col = lax.broadcasted_iota(jnp.int32, (cells_y, 3 * half_y), 1)
    target = 2 * (col % half_y) + col // half_y - 1
    target = jnp.where(target < 0, target + cells_y, target)
    pick = (at_y == target).astype(jnp.bfloat16)
    y_ref[:, 0] = jnp.zeros(y_ref[:, 0].shape, y_ref.dtype)
    for zg in range(planes_z + 1):
        if zg == 0:
            source = below_ref[0]
        elif zg == planes_z:
            source = last_ref[0]
        else:
            source = gp_ref[zg - 1]
        picked = jnp.dot(source, pick, preferred_element_type=jnp.float32).astype(y_ref.dtype)
        for dy in range(3):
            part = picked[:, dy * half_y : (dy + 1) * half_y]
            y_ref[zg, 1:, dy] = part.reshape(rows_x, part_ch, half_y)
    gu_ref[...] = jnp.zeros(gu_ref.shape, gu_ref.dtype)

    def body(step, carry):
        iz = step // coarse_x
        ix = step % coarse_x
        crow = c_ref[iz, ix]
        total = jnp.zeros(gc_ref.shape[2:], jnp.float32)
        for dz in range(3):
            block = y_ref[2 * iz + dz, pl.ds(2 * ix, 3)]
            block = block.reshape(9 * part_ch, half_y)
            total = total + jnp.dot(u_ref[dz], block, preferred_element_type=jnp.float32)
            gu_ref[dz] += lax.dot_general(
                block, crow, (((1,), (1,)), ((), ())), preferred_element_type=jnp.float32
            )
        gc_ref[iz, ix] = total
        return carry

    lax.fori_loop(0, coarse_z * coarse_x, body, 0)


def local(coarse, saved_pre, out_grad, up_weight, refine_weight):
    part_ch = saved_pre.shape[0]
    planes_z = saved_pre.shape[1]
    planes_x = saved_pre.shape[2]
    cells_y = saved_pre.shape[3]
    all_ch = part_ch * lax.axis_size("ch")
    channel_start = lax.axis_index("ch") * part_ch

    rows = jnp.transpose(out_grad, (1, 2, 0, 3))
    count = lax.axis_size(("gz", "sec"))
    forward = [(i, (i + 1) % count) for i in range(count)]
    backward = [(target, source) for source, target in forward]
    swap = [(i, i ^ 1) for i in range(lax.axis_size("ch"))]
    low = lax.ppermute(rows[planes_z - 2 :], ("gz", "sec"), forward)
    high = lax.ppermute(rows[:2], ("gz", "sec"), backward)
    rows_other = lax.ppermute(rows, "ch", swap)
    low_other = lax.ppermute(low, "ch", swap)
    high_other = lax.ppermute(high, "ch", swap)
    halo_z = low.shape[0] + planes_z + high.shape[0]
    pre_rows = jnp.transpose(saved_pre, (1, 2, 0, 3))

    refine_cols = lax.dynamic_slice_in_dim(refine_weight, channel_start, part_ch, 2)
    refine_cols = jnp.roll(refine_cols, -channel_start, axis=1)
    refine_w = refine_cols.reshape(3, 3, 3, all_ch, part_ch)[::-1]
    refine_w = jnp.transpose(refine_w, (1, 2, 4, 0, 3)).reshape(3, 3 * part_ch, 3 * all_ch)

    def fine_rows(z_lo, z_hi):
        return pl.pallas_call(
            functools.partial(fine_kernel, z_lo, z_hi),
            out_shape=(
                jax.ShapeDtypeStruct((z_hi - z_lo, planes_x, part_ch, cells_y), jnp.bfloat16),
                jax.ShapeDtypeStruct((3, 3 * all_ch, 3 * part_ch), jnp.float32),
            ),
            in_specs=[pl.BlockSpec(memory_space=pl.ANY)] * 6 + vmem_specs(2),
            out_specs=tuple(vmem_specs(2)),
            scratch_shapes=[
                pltpu.VMEM((2, halo_z // 2, planes_x + 4, all_ch, cells_y), jnp.bfloat16),
                pltpu.SemaphoreType.DMA((4 * halo_z,)),
            ],
        )(low, rows, high, low_other, rows_other, high_other, pre_rows, refine_w)

    grad_last, refine_last = fine_rows(planes_z - 1, planes_z)
    last_rows = grad_last.reshape(1, planes_x * part_ch, cells_y)
    below_z = passed_along(last_rows, ("gz", "sec"), 1)
    grad_main, refine_main = fine_rows(0, planes_z - 1)
    grad_rows = grad_main.reshape(planes_z - 1, planes_x * part_ch, cells_y)
    refine_acc = refine_main + refine_last
    refine_terms = refine_acc.reshape(3, 3, all_ch, 3, part_ch)[:, ::-1]
    refine_terms = jnp.transpose(refine_terms, (1, 0, 3, 2, 4)).reshape(27, all_ch, part_ch)
    refine_terms = jnp.roll(refine_terms, channel_start, axis=1)


    coarse_own = jnp.transpose(coarse, (1, 2, 0, 3))
    coarse_rows = jnp.concatenate([coarse_own, lax.ppermute(coarse_own, "ch", swap)], axis=2)
    coarse_in = coarse_rows.shape[2]
    coarse_start = lax.axis_index("ch") * coarse.shape[0]
    coarse_z, coarse_x, cells_yc = coarse.shape[1], coarse.shape[2], coarse.shape[3]
    up_rows = lax.dynamic_slice_in_dim(up_weight, channel_start, part_ch, 1)
    up_rows = jnp.roll(up_rows, -coarse_start, axis=2)
    up_w = jnp.transpose(up_rows.reshape(3, 9, part_ch, coarse_in), (0, 3, 1, 2))
    up_w = up_w.reshape(3, coarse_in, 9 * part_ch)

    coarse_acc, up_acc = pl.pallas_call(
        coarse_kernel,
        out_shape=(
            jax.ShapeDtypeStruct((coarse_z, coarse_x, coarse_in, cells_yc), jnp.float32),
            jax.ShapeDtypeStruct((3, 9 * part_ch, coarse_in), jnp.float32),
        ),
        in_specs=vmem_specs(5),
        out_specs=tuple(vmem_specs(2)),
        scratch_shapes=[
            pltpu.VMEM((planes_z + 1, planes_x + 1, 3, part_ch, cells_yc), jnp.bfloat16)
        ],
    )(grad_rows, last_rows, below_z, coarse_rows, up_w)
    up_terms = jnp.roll(up_acc.reshape(27, part_ch, coarse_in), coarse_start, axis=2)
    own_k = coarse.shape[0]
    received = lax.ppermute(coarse_acc[:, :, own_k:], "ch", swap)
    coarse_summed = coarse_acc[:, :, :own_k] + received
    grad_coarse = jnp.transpose(coarse_summed, (2, 0, 1, 3)).astype(jnp.bfloat16)
    flat = jnp.concatenate([up_terms.reshape(-1), refine_terms.reshape(-1)])
    flat = summed_over_slabs(flat, ("gz", "sec"))
    up_summed = flat[: up_terms.size].reshape(up_terms.shape)
    refine_summed = flat[up_terms.size :].reshape(refine_terms.shape)
    fine_total = planes_z * lax.axis_size("gz") * lax.axis_size("sec") * planes_x * cells_y
    coarse_total = fine_total // 8
    grad_up = up_summed * float(coarse_total) ** (-0.5)
    grad_refine = refine_summed * float(fine_total) ** (-0.5)
    return (grad_coarse, grad_up, grad_refine)


def solution(mesh):
    placed = (
        P("ch", ("groups", "gz", "sec"), None, None),
        P("ch", ("groups", "gz", "sec"), None, None),
        P("ch", ("groups", "gz", "sec"), None, None),
        P(),
        P(),
    )
    return jax.shard_map(
        local,
        mesh=mesh,
        in_specs=placed,
        out_specs=(
            P("ch", ("groups", "gz", "sec"), None, None),
            P("groups", "ch", None),
            P("groups", None, "ch"),
        ),
        check_vma=False,
    )
```

```python
import functools

import jax
import jax.numpy as jnp
from jax import lax
from jax.experimental import pallas as pl
from jax.experimental.pallas import tpu as pltpu
from jax.sharding import PartitionSpec as P

leak_slope = 0.2


def padded(block, sides, width):
    for axis, dim in sides:
        count = lax.axis_size(axis)
        forward = [(i, i + 1) for i in range(count - 1)]
        forward.append((count - 1, 0))
        backward = [(target, source) for source, target in forward]
        low = lax.ppermute(
            lax.slice_in_dim(block, block.shape[dim] - width, None, axis=dim), axis, forward
        )
        high = lax.ppermute(lax.slice_in_dim(block, 0, width, axis=dim), axis, backward)
        block = jnp.concatenate([low, block, high], axis=dim)
    return block


def passed_along(block, axis, distance):
    devices = range(lax.axis_size(axis))
    route = [((i - distance) % len(devices), i) for i in devices]
    return lax.ppermute(block, axis, route)


def summed_over_slabs(block, axis):
    count = lax.axis_size(axis)
    if count & (count - 1):
        return lax.psum(block, axis)
    step = 1
    while step < count:
        route = [(i, i ^ step) for i in range(count)]
        block = block + lax.ppermute(block, axis, route)
        step *= 2
    return block


def vmem_specs(count):
    return [pl.BlockSpec(memory_space=pltpu.VMEM)] * count


def fine_kernel(z_lo, z_hi, *refs):
    pieces = refs[:6]
    sp_ref, w_ref, gp_ref, r_ref, g_ref, sems = refs[6:]
    planes_z, planes_x, part_ch, cells_y = sp_ref.shape
    wide = g_ref.shape[4]
    low_count = pieces[0].shape[0]
    needed = sorted({z + 4 - 2 * dz for z in range(z_lo, z_hi) for dz in range(3)})
    edge = jnp.zeros(g_ref[:, :, :, 0].shape, g_ref.dtype)
    g_ref[:, :, :, 0] = edge
    g_ref[:, :, :, planes_x // 2 + 1] = edge
    copies = []
    for plane in needed:
        if plane < low_count:
            part, at = 0, plane
        elif plane < low_count + planes_z:
            part, at = 1, plane - low_count
        else:
            part, at = 2, plane - low_count - planes_z
        for half in range(2):
            for parity in range(2):
                copy = pltpu.make_async_copy(
                    pieces[3 * half + part].at[at, parity],
                    g_ref.at[
                        plane % 2,
                        plane // 2,
                        parity,
                        pl.ds(1, planes_x // 2),
                        pl.ds(half * part_ch, part_ch),
                    ],
                    sems.at[len(copies)],
                )
                copy.start()
                copies.append(copy)
    r_ref[...] = jnp.zeros(r_ref.shape, r_ref.dtype)
    for copy in copies:
        copy.wait()

    def body(step, carry):
        z = z_lo + step // planes_x
        x = step % planes_x
        pre_act = sp_ref[z, x].astype(jnp.float32)
        slopes = jnp.where(pre_act > 0, 1.0, leak_slope).astype(jnp.float32)
        hidden = (pre_act * slopes).astype(jnp.bfloat16).astype(jnp.float32)
        rolled = jnp.concatenate(
            [pltpu.roll(hidden, 2, 1), hidden, pltpu.roll(hidden, cells_y - 2, 1)], axis=0
        ).astype(jnp.bfloat16)
        block = g_ref[z % 2, pl.ds(z // 2, 3), x % 2, pl.ds(x // 2, 3)]
        block = block.reshape(9 * wide, cells_y)
        total = jnp.dot(w_ref[...], block, preferred_element_type=jnp.float32)
        r_ref[...] += lax.dot_general(
            block, rolled, (((1,), (1,)), ((), ())), preferred_element_type=jnp.float32
        )
        grad_hidden = (
            pltpu.roll(total[:part_ch], cells_y - 2, 1)
            + total[part_ch : 2 * part_ch]
            + pltpu.roll(total[2 * part_ch :], 2, 1)
        )
        gp_ref[z - z_lo, x] = (grad_hidden * slopes).astype(gp_ref.dtype)
        return carry

    lax.fori_loop(0, (z_hi - z_lo) * planes_x, body, 0)


def coarse_kernel(gp_ref, last_ref, below_ref, c_ref, u_ref, gc_ref, gu_ref, y_ref):
    planes_z = gp_ref.shape[0] + 1
    cells_y = gp_ref.shape[2]
    rows_x = y_ref.shape[1] - 1
    part_ch = y_ref.shape[3]
    half_y = y_ref.shape[4]
    coarse_z, coarse_x = c_ref.shape[0], c_ref.shape[1]
    at_y = lax.broadcasted_iota(jnp.int32, (cells_y, 3 * half_y), 0)
    col = lax.broadcasted_iota(jnp.int32, (cells_y, 3 * half_y), 1)
    target = 2 * (col % half_y) + col // half_y - 1
    target = jnp.where(target < 0, target + cells_y, target)
    pick = (at_y == target).astype(jnp.bfloat16)
    y_ref[:, 0] = jnp.zeros(y_ref[:, 0].shape, y_ref.dtype)
    for zg in range(planes_z + 1):
        if zg == 0:
            source = below_ref[0]
        elif zg == planes_z:
            source = last_ref[0]
        else:
            source = gp_ref[zg - 1]
        picked = jnp.dot(source, pick, preferred_element_type=jnp.float32).astype(y_ref.dtype)
        for dy in range(3):
            part = picked[:, dy * half_y : (dy + 1) * half_y]
            y_ref[zg, 1:, dy] = part.reshape(rows_x, part_ch, half_y)
    gu_ref[...] = jnp.zeros(gu_ref.shape, gu_ref.dtype)

    def body(step, carry):
        iz = step // coarse_x
        ix = step % coarse_x
        crow = c_ref[iz, ix]
        total = jnp.zeros(gc_ref.shape[2:], jnp.float32)
        for dz in range(3):
            block = y_ref[2 * iz + dz, pl.ds(2 * ix, 3)]
            block = block.reshape(9 * part_ch, half_y)
            total = total + jnp.dot(u_ref[dz], block, preferred_element_type=jnp.float32)
            gu_ref[dz] += lax.dot_general(
                block, crow, (((1,), (1,)), ((), ())), preferred_element_type=jnp.float32
            )
        gc_ref[iz, ix] = total
        return carry

    lax.fori_loop(0, coarse_z * coarse_x, body, 0)


def local(coarse, saved_pre, out_grad, up_weight, refine_weight):
    part_ch = saved_pre.shape[0]
    planes_z = saved_pre.shape[1]
    planes_x = saved_pre.shape[2]
    cells_y = saved_pre.shape[3]
    all_ch = part_ch * lax.axis_size("ch")
    channel_start = lax.axis_index("ch") * part_ch

    rows = out_grad.reshape(part_ch, planes_z, planes_x // 2, 2, cells_y)
    rows = jnp.transpose(rows, (1, 3, 2, 0, 4))
    count = lax.axis_size(("gz", "sec"))
    forward = [(i, (i + 1) % count) for i in range(count)]
    backward = [(target, source) for source, target in forward]
    swap = [(i, i ^ 1) for i in range(lax.axis_size("ch"))]
    low = lax.ppermute(rows[planes_z - 2 :], ("gz", "sec"), forward)
    high = lax.ppermute(rows[:2], ("gz", "sec"), backward)
    rows_other = lax.ppermute(rows, "ch", swap)
    low_other = lax.ppermute(low, "ch", swap)
    high_other = lax.ppermute(high, "ch", swap)
    halo_z = low.shape[0] + planes_z + high.shape[0]
    pre_rows = jnp.transpose(saved_pre, (1, 2, 0, 3))

    refine_cols = lax.dynamic_slice_in_dim(refine_weight, channel_start, part_ch, 2)
    refine_cols = jnp.roll(refine_cols, -channel_start, axis=1)
    refine_w = refine_cols.reshape(3, 3, 3, all_ch, part_ch)[::-1, ::-1]
    refine_w = jnp.transpose(refine_w, (2, 4, 0, 1, 3)).reshape(3 * part_ch, 9 * all_ch)

    def fine_rows(z_lo, z_hi):
        return pl.pallas_call(
            functools.partial(fine_kernel, z_lo, z_hi),
            out_shape=(
                jax.ShapeDtypeStruct((z_hi - z_lo, planes_x, part_ch, cells_y), jnp.bfloat16),
                jax.ShapeDtypeStruct((9 * all_ch, 3 * part_ch), jnp.float32),
            ),
            in_specs=[pl.BlockSpec(memory_space=pl.ANY)] * 6 + vmem_specs(2),
            out_specs=tuple(vmem_specs(2)),
            scratch_shapes=[
                pltpu.VMEM(
                    (2, halo_z // 2, 2, planes_x // 2 + 2, all_ch, cells_y), jnp.bfloat16
                ),
                pltpu.SemaphoreType.DMA((4 * halo_z,)),
            ],
        )(low, rows, high, low_other, rows_other, high_other, pre_rows, refine_w)

    grad_last, refine_last = fine_rows(planes_z - 1, planes_z)
    last_rows = grad_last.reshape(1, planes_x * part_ch, cells_y)
    below_z = passed_along(last_rows, ("gz", "sec"), 1)
    grad_main, refine_main = fine_rows(0, planes_z - 1)
    grad_rows = grad_main.reshape(planes_z - 1, planes_x * part_ch, cells_y)
    refine_acc = refine_main + refine_last
    refine_terms = refine_acc.reshape(3, 3, all_ch, 3, part_ch)[::-1, ::-1]
    refine_terms = jnp.transpose(refine_terms, (0, 1, 3, 2, 4)).reshape(27, all_ch, part_ch)
    refine_terms = jnp.roll(refine_terms, channel_start, axis=1)


    coarse_own = jnp.transpose(coarse, (1, 2, 0, 3))
    coarse_rows = jnp.concatenate([coarse_own, lax.ppermute(coarse_own, "ch", swap)], axis=2)
    coarse_in = coarse_rows.shape[2]
    coarse_start = lax.axis_index("ch") * coarse.shape[0]
    coarse_z, coarse_x, cells_yc = coarse.shape[1], coarse.shape[2], coarse.shape[3]
    up_rows = lax.dynamic_slice_in_dim(up_weight, channel_start, part_ch, 1)
    up_rows = jnp.roll(up_rows, -coarse_start, axis=2)
    up_w = jnp.transpose(up_rows.reshape(3, 9, part_ch, coarse_in), (0, 3, 1, 2))
    up_w = up_w.reshape(3, coarse_in, 9 * part_ch)

    coarse_acc, up_acc = pl.pallas_call(
        coarse_kernel,
        out_shape=(
            jax.ShapeDtypeStruct((coarse_z, coarse_x, coarse_in, cells_yc), jnp.float32),
            jax.ShapeDtypeStruct((3, 9 * part_ch, coarse_in), jnp.float32),
        ),
        in_specs=vmem_specs(5),
        out_specs=tuple(vmem_specs(2)),
        scratch_shapes=[
            pltpu.VMEM((planes_z + 1, planes_x + 1, 3, part_ch, cells_yc), jnp.bfloat16)
        ],
    )(grad_rows, last_rows, below_z, coarse_rows, up_w)
    up_terms = jnp.roll(up_acc.reshape(27, part_ch, coarse_in), coarse_start, axis=2)
    own_k = coarse.shape[0]
    received = lax.ppermute(coarse_acc[:, :, own_k:], "ch", swap)
    coarse_summed = coarse_acc[:, :, :own_k] + received
    grad_coarse = jnp.transpose(coarse_summed, (2, 0, 1, 3)).astype(jnp.bfloat16)
    flat = jnp.concatenate([up_terms.reshape(-1), refine_terms.reshape(-1)])
    flat = summed_over_slabs(flat, ("gz", "sec"))
    up_summed = flat[: up_terms.size].reshape(up_terms.shape)
    refine_summed = flat[up_terms.size :].reshape(refine_terms.shape)
    fine_total = planes_z * lax.axis_size("gz") * lax.axis_size("sec") * planes_x * cells_y
    coarse_total = fine_total // 8
    grad_up = up_summed * float(coarse_total) ** (-0.5)
    grad_refine = refine_summed * float(fine_total) ** (-0.5)
    return (grad_coarse, grad_up, grad_refine)


def solution(mesh):
    placed = (
        P("ch", ("groups", "gz", "sec"), None, None),
        P("ch", ("groups", "gz", "sec"), None, None),
        P("ch", ("groups", "gz", "sec"), None, None),
        P(),
        P(),
    )
    return jax.shard_map(
        local,
        mesh=mesh,
        in_specs=placed,
        out_specs=(
            P("ch", ("groups", "gz", "sec"), None, None),
            P("groups", "ch", None),
            P("groups", None, "ch"),
        ),
        check_vma=False,
    )
```

```python
import functools

import jax
import jax.numpy as jnp
from jax import lax
from jax.experimental import pallas as pl
from jax.experimental.pallas import tpu as pltpu
from jax.sharding import PartitionSpec as P

leak_slope = 0.2


def padded(block, sides, width):
    for axis, dim in sides:
        count = lax.axis_size(axis)
        forward = [(i, i + 1) for i in range(count - 1)]
        forward.append((count - 1, 0))
        backward = [(target, source) for source, target in forward]
        low = lax.ppermute(
            lax.slice_in_dim(block, block.shape[dim] - width, None, axis=dim), axis, forward
        )
        high = lax.ppermute(lax.slice_in_dim(block, 0, width, axis=dim), axis, backward)
        block = jnp.concatenate([low, block, high], axis=dim)
    return block


def passed_along(block, axis, distance):
    devices = range(lax.axis_size(axis))
    route = [((i - distance) % len(devices), i) for i in devices]
    return lax.ppermute(block, axis, route)


def summed_over_slabs(block, axis):
    count = lax.axis_size(axis)
    if count & (count - 1):
        return lax.psum(block, axis)
    step = 1
    while step < count:
        route = [(i, i ^ step) for i in range(count)]
        block = block + lax.ppermute(block, axis, route)
        step *= 2
    return block


def vmem_specs(count):
    return [pl.BlockSpec(memory_space=pltpu.VMEM)] * count


def fine_kernel(z_lo, z_hi, scale, *refs):
    pieces = refs[:6]
    if len(refs) == 13:
        sp_ref, w_ref, start_ref, gp_ref, r_ref, g_ref, sems = refs[6:]
    else:
        sp_ref, w_ref, gp_ref, r_ref, g_ref, sems = refs[6:]
        start_ref = None
    planes_z, planes_x, part_ch, cells_y = sp_ref.shape
    wide = g_ref.shape[4]
    low_count = pieces[0].shape[0]
    needed = sorted({z + 4 - 2 * dz for z in range(z_lo, z_hi) for dz in range(3)})
    edge = jnp.zeros(g_ref[:, :, :, 0].shape, g_ref.dtype)
    g_ref[:, :, :, 0] = edge
    g_ref[:, :, :, planes_x // 2 + 1] = edge
    copies = []
    for plane in needed:
        if plane < low_count:
            part, at = 0, plane
        elif plane < low_count + planes_z:
            part, at = 1, plane - low_count
        else:
            part, at = 2, plane - low_count - planes_z
        for half in range(2):
            for parity in range(2):
                copy = pltpu.make_async_copy(
                    pieces[3 * half + part].at[at, parity],
                    g_ref.at[
                        plane % 2,
                        plane // 2,
                        parity,
                        pl.ds(1, planes_x // 2),
                        pl.ds(half * part_ch, part_ch),
                    ],
                    sems.at[len(copies)],
                )
                copy.start()
                copies.append(copy)
    if start_ref is None:
        r_ref[...] = jnp.zeros(r_ref.shape, r_ref.dtype)
    else:
        r_ref[...] = start_ref[...]
    for copy in copies:
        copy.wait()

    def body(step, carry):
        z = z_lo + step // planes_x
        x = step % planes_x
        pre_act = sp_ref[z, x].astype(jnp.float32)
        slopes = jnp.where(pre_act > 0, 1.0, leak_slope).astype(jnp.float32)
        hidden = (pre_act * slopes).astype(jnp.bfloat16).astype(jnp.float32)
        rolled = jnp.concatenate(
            [pltpu.roll(hidden, 2, 1), hidden, pltpu.roll(hidden, cells_y - 2, 1)], axis=0
        ).astype(jnp.bfloat16)
        block = g_ref[z % 2, pl.ds(z // 2, 3), x % 2, pl.ds(x // 2, 3)]
        block = block.reshape(9 * wide, cells_y)
        total = jnp.dot(w_ref[...], block, preferred_element_type=jnp.float32)
        r_ref[...] += lax.dot_general(
            block, rolled, (((1,), (1,)), ((), ())), preferred_element_type=jnp.float32
        )
        grad_hidden = (
            pltpu.roll(total[:part_ch], cells_y - 2, 1)
            + total[part_ch : 2 * part_ch]
            + pltpu.roll(total[2 * part_ch :], 2, 1)
        )
        gp_ref[z - z_lo, x] = (grad_hidden * slopes).astype(gp_ref.dtype)
        return carry

    lax.fori_loop(0, (z_hi - z_lo) * planes_x, body, 0)
    if scale != 1.0:
        r_ref[...] = r_ref[...] * scale


def coarse_kernel(scale, gp_ref, last_ref, below_ref, c_ref, u_ref, gc_ref, gu_ref, y_ref):
    planes_z = gp_ref.shape[0] + 1
    cells_y = gp_ref.shape[2]
    rows_x = y_ref.shape[1] - 1
    part_ch = y_ref.shape[3]
    half_y = y_ref.shape[4]
    coarse_z, coarse_x = c_ref.shape[0], c_ref.shape[1]
    at_y = lax.broadcasted_iota(jnp.int32, (cells_y, 3 * half_y), 0)
    col = lax.broadcasted_iota(jnp.int32, (cells_y, 3 * half_y), 1)
    target = 2 * (col % half_y) + col // half_y - 1
    target = jnp.where(target < 0, target + cells_y, target)
    pick = (at_y == target).astype(jnp.bfloat16)
    y_ref[:, 0] = jnp.zeros(y_ref[:, 0].shape, y_ref.dtype)
    for zg in range(planes_z + 1):
        if zg == 0:
            source = below_ref[0]
        elif zg == planes_z:
            source = last_ref[0]
        else:
            source = gp_ref[zg - 1]
        picked = jnp.dot(source, pick, preferred_element_type=jnp.float32).astype(y_ref.dtype)
        for dy in range(3):
            part = picked[:, dy * half_y : (dy + 1) * half_y]
            y_ref[zg, 1:, dy] = part.reshape(rows_x, part_ch, half_y)
    gu_ref[...] = jnp.zeros(gu_ref.shape, gu_ref.dtype)

    def body(step, carry):
        iz = step // coarse_x
        ix = step % coarse_x
        crow = c_ref[iz, ix]
        total = jnp.zeros(gc_ref.shape[2:], jnp.float32)
        for dz in range(3):
            block = y_ref[2 * iz + dz, pl.ds(2 * ix, 3)]
            block = block.reshape(9 * part_ch, half_y)
            total = total + jnp.dot(u_ref[dz], block, preferred_element_type=jnp.float32)
            gu_ref[dz] += lax.dot_general(
                block, crow, (((1,), (1,)), ((), ())), preferred_element_type=jnp.float32
            )
        gc_ref[iz, ix] = total
        return carry

    lax.fori_loop(0, coarse_z * coarse_x, body, 0)
    gu_ref[...] = gu_ref[...] * scale


def local(coarse, saved_pre, out_grad, up_weight, refine_weight):
    part_ch = saved_pre.shape[0]
    planes_z = saved_pre.shape[1]
    planes_x = saved_pre.shape[2]
    cells_y = saved_pre.shape[3]
    all_ch = part_ch * lax.axis_size("ch")
    channel_start = lax.axis_index("ch") * part_ch

    rows = out_grad.reshape(part_ch, planes_z, planes_x // 2, 2, cells_y)
    rows = jnp.transpose(rows, (1, 3, 2, 0, 4))
    count = lax.axis_size(("gz", "sec"))
    forward = [(i, (i + 1) % count) for i in range(count)]
    backward = [(target, source) for source, target in forward]
    swap = [(i, i ^ 1) for i in range(lax.axis_size("ch"))]
    low = lax.ppermute(rows[planes_z - 2 :], ("gz", "sec"), forward)
    high = lax.ppermute(rows[:2], ("gz", "sec"), backward)
    rows_other = lax.ppermute(rows, "ch", swap)
    low_other = lax.ppermute(low, "ch", swap)
    high_other = lax.ppermute(high, "ch", swap)
    halo_z = low.shape[0] + planes_z + high.shape[0]
    pre_rows = jnp.transpose(saved_pre, (1, 2, 0, 3))

    refine_cols = lax.dynamic_slice_in_dim(refine_weight, channel_start, part_ch, 2)
    refine_cols = jnp.roll(refine_cols, -channel_start, axis=1)
    refine_w = refine_cols.reshape(3, 3, 3, all_ch, part_ch)[::-1, ::-1]
    refine_w = jnp.transpose(refine_w, (2, 4, 0, 1, 3)).reshape(3 * part_ch, 9 * all_ch)

    fine_total = planes_z * lax.axis_size("gz") * lax.axis_size("sec") * planes_x * cells_y
    coarse_total = fine_total // 8

    def fine_rows(z_lo, z_hi, *start):
        scale = float(fine_total) ** (-0.5) if start else 1.0
        return pl.pallas_call(
            functools.partial(fine_kernel, z_lo, z_hi, scale),
            out_shape=(
                jax.ShapeDtypeStruct((z_hi - z_lo, planes_x, part_ch, cells_y), jnp.bfloat16),
                jax.ShapeDtypeStruct((9 * all_ch, 3 * part_ch), jnp.float32),
            ),
            in_specs=[pl.BlockSpec(memory_space=pl.ANY)] * 6 + vmem_specs(2 + len(start)),
            out_specs=tuple(vmem_specs(2)),
            scratch_shapes=[
                pltpu.VMEM(
                    (2, halo_z // 2, 2, planes_x // 2 + 2, all_ch, cells_y), jnp.bfloat16
                ),
                pltpu.SemaphoreType.DMA((4 * halo_z,)),
            ],
        )(low, rows, high, low_other, rows_other, high_other, pre_rows, refine_w, *start)

    grad_last, refine_last = fine_rows(planes_z - 1, planes_z)
    last_rows = grad_last.reshape(1, planes_x * part_ch, cells_y)
    below_z = passed_along(last_rows, ("gz", "sec"), 1)
    grad_main, refine_acc = fine_rows(0, planes_z - 1, refine_last)
    grad_rows = grad_main.reshape(planes_z - 1, planes_x * part_ch, cells_y)
    refine_terms = refine_acc.reshape(3, 3, all_ch, 3, part_ch)[::-1, ::-1]
    refine_terms = jnp.transpose(refine_terms, (0, 1, 3, 2, 4)).reshape(27, all_ch, part_ch)
    refine_terms = jnp.roll(refine_terms, channel_start, axis=1)


    coarse_own = jnp.transpose(coarse, (1, 2, 0, 3))
    coarse_other = lax.ppermute(coarse_own, "ch", swap)
    own_k = coarse.shape[0]
    coarse_start = lax.axis_index("ch") * own_k
    coarse_rows = jnp.concatenate([coarse_own, coarse_other, coarse_own], axis=2)
    coarse_rows = lax.dynamic_slice_in_dim(coarse_rows, coarse_start, 2 * own_k, 2)
    coarse_in = coarse_rows.shape[2]
    coarse_z, coarse_x, cells_yc = coarse.shape[1], coarse.shape[2], coarse.shape[3]
    up_rows = lax.dynamic_slice_in_dim(up_weight, channel_start, part_ch, 1)
    up_w = jnp.transpose(up_rows.reshape(3, 9, part_ch, coarse_in), (0, 3, 1, 2))
    up_w = up_w.reshape(3, coarse_in, 9 * part_ch)

    coarse_acc, up_acc = pl.pallas_call(
        functools.partial(coarse_kernel, float(coarse_total) ** (-0.5)),
        out_shape=(
            jax.ShapeDtypeStruct((coarse_z, coarse_x, coarse_in, cells_yc), jnp.float32),
            jax.ShapeDtypeStruct((3, 9 * part_ch, coarse_in), jnp.float32),
        ),
        in_specs=vmem_specs(5),
        out_specs=tuple(vmem_specs(2)),
        scratch_shapes=[
            pltpu.VMEM((planes_z + 1, planes_x + 1, 3, part_ch, cells_yc), jnp.bfloat16)
        ],
    )(grad_rows, last_rows, below_z, coarse_rows, up_w)
    up_terms = up_acc.reshape(27, part_ch, coarse_in)
    other_start = own_k - coarse_start
    received = lax.ppermute(lax.dynamic_slice_in_dim(coarse_acc, other_start, own_k, 2), "ch", swap)
    coarse_summed = lax.dynamic_slice_in_dim(coarse_acc, coarse_start, own_k, 2) + received
    grad_coarse = jnp.transpose(coarse_summed, (2, 0, 1, 3)).astype(jnp.bfloat16)
    flat = jnp.concatenate([up_terms.reshape(-1), refine_terms.reshape(-1)])
    flat = summed_over_slabs(flat, ("gz", "sec"))
    grad_up = flat[: up_terms.size].reshape(up_terms.shape)
    grad_refine = flat[up_terms.size :].reshape(refine_terms.shape)
    return (grad_coarse, grad_up, grad_refine)


def solution(mesh):
    placed = (
        P("ch", ("groups", "gz", "sec"), None, None),
        P("ch", ("groups", "gz", "sec"), None, None),
        P("ch", ("groups", "gz", "sec"), None, None),
        P(),
        P(),
    )
    return jax.shard_map(
        local,
        mesh=mesh,
        in_specs=placed,
        out_specs=(
            P("ch", ("groups", "gz", "sec"), None, None),
            P("groups", "ch", None),
            P("groups", None, "ch"),
        ),
        check_vma=False,
    )
```

```python
import functools

import jax
import jax.numpy as jnp
from jax import lax
from jax.experimental import pallas as pl
from jax.experimental.pallas import tpu as pltpu
from jax.sharding import PartitionSpec as P

leak_slope = 0.2


def padded(block, sides, width):
    for axis, dim in sides:
        count = lax.axis_size(axis)
        forward = [(i, i + 1) for i in range(count - 1)]
        forward.append((count - 1, 0))
        backward = [(target, source) for source, target in forward]
        low = lax.ppermute(
            lax.slice_in_dim(block, block.shape[dim] - width, None, axis=dim), axis, forward
        )
        high = lax.ppermute(lax.slice_in_dim(block, 0, width, axis=dim), axis, backward)
        block = jnp.concatenate([low, block, high], axis=dim)
    return block


def passed_along(block, axis, distance):
    devices = range(lax.axis_size(axis))
    route = [((i - distance) % len(devices), i) for i in devices]
    return lax.ppermute(block, axis, route)


def summed_over_slabs(block, axis):
    count = lax.axis_size(axis)
    if count & (count - 1):
        return lax.psum(block, axis)
    step = 1
    while step < count:
        route = [(i, i ^ step) for i in range(count)]
        block = block + lax.ppermute(block, axis, route)
        step *= 2
    return block


def vmem_specs(count):
    return [pl.BlockSpec(memory_space=pltpu.VMEM)] * count


def fine_kernel(z_lo, z_hi, scale, *refs):
    pieces = refs[:6]
    if len(refs) == 13:
        sp_ref, w_ref, start_ref, gp_ref, r_ref, g_ref, sems = refs[6:]
    else:
        sp_ref, w_ref, gp_ref, r_ref, g_ref, sems = refs[6:]
        start_ref = None
    planes_z, planes_x, part_ch, cells_y = sp_ref.shape
    wide = g_ref.shape[4]
    low_count = pieces[0].shape[0]
    needed = sorted({z + 4 - 2 * dz for z in range(z_lo, z_hi) for dz in range(3)})
    edge = jnp.zeros(g_ref[:, :, :, 0].shape, g_ref.dtype)
    g_ref[:, :, :, 0] = edge
    g_ref[:, :, :, planes_x // 2 + 1] = edge
    copies = []
    for plane in needed:
        if plane < low_count:
            part, at = 0, plane
        elif plane < low_count + planes_z:
            part, at = 1, plane - low_count
        else:
            part, at = 2, plane - low_count - planes_z
        for half in range(2):
            for parity in range(2):
                copy = pltpu.make_async_copy(
                    pieces[3 * half + part].at[at, parity],
                    g_ref.at[
                        plane % 2,
                        plane // 2,
                        parity,
                        pl.ds(1, planes_x // 2),
                        pl.ds(half * part_ch, part_ch),
                    ],
                    sems.at[len(copies)],
                )
                copy.start()
                copies.append(copy)
    if start_ref is None:
        r_ref[...] = jnp.zeros(r_ref.shape, r_ref.dtype)
    else:
        r_ref[...] = start_ref[...]
    for copy in copies:
        copy.wait()

    def body(step, carry):
        z = z_lo + step // planes_x
        x = step % planes_x
        pre_act = sp_ref[z, x].astype(jnp.float32)
        slopes = jnp.where(pre_act > 0, 1.0, leak_slope).astype(jnp.float32)
        hidden = (pre_act * slopes).astype(jnp.bfloat16).astype(jnp.float32)
        rolled = jnp.concatenate(
            [pltpu.roll(hidden, 2, 1), hidden, pltpu.roll(hidden, cells_y - 2, 1)], axis=0
        ).astype(jnp.bfloat16)
        block = g_ref[z % 2, pl.ds(z // 2, 3), x % 2, pl.ds(x // 2, 3)]
        block = block.reshape(9 * wide, cells_y)
        total = jnp.dot(w_ref[...], block, preferred_element_type=jnp.float32)
        r_ref[...] += lax.dot_general(
            block, rolled, (((1,), (1,)), ((), ())), preferred_element_type=jnp.float32
        )
        grad_hidden = (
            pltpu.roll(total[:part_ch], cells_y - 2, 1)
            + total[part_ch : 2 * part_ch]
            + pltpu.roll(total[2 * part_ch :], 2, 1)
        )
        gp_ref[z - z_lo, x] = (grad_hidden * slopes).astype(gp_ref.dtype)
        return carry

    lax.fori_loop(0, (z_hi - z_lo) * planes_x, body, 0)
    if scale != 1.0:
        r_ref[...] = r_ref[...] * scale


def coarse_kernel(scale, gp_ref, last_ref, below_ref, c_ref, u_ref, gc_ref, gu_ref, y_ref):
    planes_z = gp_ref.shape[0] + 1
    cells_y = gp_ref.shape[2]
    rows_x = y_ref.shape[1] - 1
    part_ch = y_ref.shape[3]
    half_y = y_ref.shape[4]
    coarse_z, coarse_x = c_ref.shape[0], c_ref.shape[1]
    at_y = lax.broadcasted_iota(jnp.int32, (cells_y, 3 * half_y), 0)
    col = lax.broadcasted_iota(jnp.int32, (cells_y, 3 * half_y), 1)
    target = 2 * (col % half_y) + col // half_y - 1
    target = jnp.where(target < 0, target + cells_y, target)
    pick = (at_y == target).astype(jnp.bfloat16)
    y_ref[:, 0] = jnp.zeros(y_ref[:, 0].shape, y_ref.dtype)
    for zg in range(planes_z + 1):
        if zg == 0:
            source = below_ref[0]
        elif zg == planes_z:
            source = last_ref[0]
        else:
            source = gp_ref[zg - 1]
        picked = jnp.dot(source, pick, preferred_element_type=jnp.float32).astype(y_ref.dtype)
        for dy in range(3):
            part = picked[:, dy * half_y : (dy + 1) * half_y]
            y_ref[zg, 1:, dy] = part.reshape(rows_x, part_ch, half_y)
    gu_ref[...] = jnp.zeros(gu_ref.shape, gu_ref.dtype)

    def body(step, carry):
        iz = step // coarse_x
        ix = step % coarse_x
        crow = c_ref[iz, ix]
        total = jnp.zeros(gc_ref.shape[2:], jnp.float32)
        for dz in range(3):
            block = y_ref[2 * iz + dz, pl.ds(2 * ix, 3)]
            block = block.reshape(9 * part_ch, half_y)
            total = total + jnp.dot(u_ref[dz], block, preferred_element_type=jnp.float32)
            gu_ref[dz] += lax.dot_general(
                block, crow, (((1,), (1,)), ((), ())), preferred_element_type=jnp.float32
            )
        gc_ref[iz, ix] = total
        return carry

    lax.fori_loop(0, coarse_z * coarse_x, body, 0)
    gu_ref[...] = gu_ref[...] * scale


def local(coarse, saved_pre, out_grad, up_weight, refine_weight):
    part_ch = saved_pre.shape[0]
    planes_z = saved_pre.shape[1]
    planes_x = saved_pre.shape[2]
    cells_y = saved_pre.shape[3]
    all_ch = part_ch * lax.axis_size("ch")
    channel_start = lax.axis_index("ch") * part_ch

    rows = out_grad.reshape(part_ch, planes_z, planes_x // 2, 2, cells_y)
    rows = jnp.transpose(rows, (1, 3, 2, 0, 4))
    count = lax.axis_size(("gz", "sec"))
    forward = [(i, (i + 1) % count) for i in range(count)]
    backward = [(target, source) for source, target in forward]
    swap = [(i, i ^ 1) for i in range(lax.axis_size("ch"))]
    low = lax.ppermute(rows[planes_z - 2 :], ("gz", "sec"), forward)
    high = lax.ppermute(rows[:2], ("gz", "sec"), backward)
    rows_other = lax.ppermute(rows, "ch", swap)
    low_other = lax.ppermute(low, "ch", swap)
    high_other = lax.ppermute(high, "ch", swap)
    halo_z = low.shape[0] + planes_z + high.shape[0]
    pre_rows = jnp.transpose(saved_pre, (1, 2, 0, 3))

    refine_cols = lax.dynamic_slice_in_dim(refine_weight, channel_start, part_ch, 2)
    refine_cols = jnp.roll(refine_cols, -channel_start, axis=1)
    refine_w = refine_cols.reshape(3, 3, 3, all_ch, part_ch)[::-1, ::-1]
    refine_w = jnp.transpose(refine_w, (2, 4, 0, 1, 3)).reshape(3 * part_ch, 9 * all_ch)

    fine_total = planes_z * lax.axis_size("gz") * lax.axis_size("sec") * planes_x * cells_y
    coarse_total = fine_total // 8

    def fine_rows(z_lo, z_hi, *start):
        scale = float(fine_total) ** (-0.5) if start else 1.0
        return pl.pallas_call(
            functools.partial(fine_kernel, z_lo, z_hi, scale),
            out_shape=(
                jax.ShapeDtypeStruct((z_hi - z_lo, planes_x, part_ch, cells_y), jnp.bfloat16),
                jax.ShapeDtypeStruct((9 * all_ch, 3 * part_ch), jnp.float32),
            ),
            in_specs=[pl.BlockSpec(memory_space=pl.ANY)] * 6 + vmem_specs(2 + len(start)),
            out_specs=tuple(vmem_specs(2)),
            cost_estimate=pl.CostEstimate(
                flops=4 * (z_hi - z_lo) * planes_x * 27 * all_ch * part_ch * cells_y,
                bytes_accessed=2 * halo_z * planes_x * all_ch * cells_y,
                transcendentals=0,
            ),
            scratch_shapes=[
                pltpu.VMEM(
                    (2, halo_z // 2, 2, planes_x // 2 + 2, all_ch, cells_y), jnp.bfloat16
                ),
                pltpu.SemaphoreType.DMA((4 * halo_z,)),
            ],
        )(low, rows, high, low_other, rows_other, high_other, pre_rows, refine_w, *start)

    grad_last, refine_last = fine_rows(planes_z - 1, planes_z)
    last_rows = grad_last.reshape(1, planes_x * part_ch, cells_y)
    below_z = passed_along(last_rows, ("gz", "sec"), 1)
    grad_main, refine_acc = fine_rows(0, planes_z - 1, refine_last)
    grad_rows = grad_main.reshape(planes_z - 1, planes_x * part_ch, cells_y)
    refine_terms = refine_acc.reshape(3, 3, all_ch, 3, part_ch)[::-1, ::-1]
    refine_terms = jnp.transpose(refine_terms, (0, 1, 3, 2, 4)).reshape(27, all_ch, part_ch)
    refine_terms = jnp.roll(refine_terms, channel_start, axis=1)
    grad_refine = summed_over_slabs(refine_terms, ("gz", "sec"))


    coarse_own = jnp.transpose(coarse, (1, 2, 0, 3))
    coarse_other = lax.ppermute(coarse_own, "ch", swap)
    own_k = coarse.shape[0]
    coarse_start = lax.axis_index("ch") * own_k
    coarse_rows = jnp.concatenate([coarse_own, coarse_other, coarse_own], axis=2)
    coarse_rows = lax.dynamic_slice_in_dim(coarse_rows, coarse_start, 2 * own_k, 2)
    coarse_in = coarse_rows.shape[2]
    coarse_z, coarse_x, cells_yc = coarse.shape[1], coarse.shape[2], coarse.shape[3]
    up_rows = lax.dynamic_slice_in_dim(up_weight, channel_start, part_ch, 1)
    up_w = jnp.transpose(up_rows.reshape(3, 9, part_ch, coarse_in), (0, 3, 1, 2))
    up_w = up_w.reshape(3, coarse_in, 9 * part_ch)

    coarse_acc, up_acc = pl.pallas_call(
        functools.partial(coarse_kernel, float(coarse_total) ** (-0.5)),
        out_shape=(
            jax.ShapeDtypeStruct((coarse_z, coarse_x, coarse_in, cells_yc), jnp.float32),
            jax.ShapeDtypeStruct((3, 9 * part_ch, coarse_in), jnp.float32),
        ),
        in_specs=vmem_specs(5),
        out_specs=tuple(vmem_specs(2)),
        cost_estimate=pl.CostEstimate(
            flops=4 * coarse_z * coarse_x * 27 * part_ch * coarse_in * cells_yc
            + 2 * (planes_z + 1) * planes_x * part_ch * cells_y * 3 * cells_yc,
            bytes_accessed=2 * (planes_z + 1) * planes_x * part_ch * cells_y,
            transcendentals=0,
        ),
        scratch_shapes=[
            pltpu.VMEM((planes_z + 1, planes_x + 1, 3, part_ch, cells_yc), jnp.bfloat16)
        ],
    )(grad_rows, last_rows, below_z, coarse_rows, up_w)
    up_terms = up_acc.reshape(27, part_ch, coarse_in)
    other_start = own_k - coarse_start
    received = lax.ppermute(lax.dynamic_slice_in_dim(coarse_acc, other_start, own_k, 2), "ch", swap)
    coarse_summed = lax.dynamic_slice_in_dim(coarse_acc, coarse_start, own_k, 2) + received
    grad_coarse = jnp.transpose(coarse_summed, (2, 0, 1, 3)).astype(jnp.bfloat16)
    grad_up = summed_over_slabs(up_terms, ("gz", "sec"))
    return (grad_coarse, grad_up, grad_refine)


def solution(mesh):
    placed = (
        P("ch", ("groups", "gz", "sec"), None, None),
        P("ch", ("groups", "gz", "sec"), None, None),
        P("ch", ("groups", "gz", "sec"), None, None),
        P(),
        P(),
    )
    return jax.shard_map(
        local,
        mesh=mesh,
        in_specs=placed,
        out_specs=(
            P("ch", ("groups", "gz", "sec"), None, None),
            P("groups", "ch", None),
            P("groups", None, "ch"),
        ),
        check_vma=False,
    )
```

```python
import functools

import jax
import jax.numpy as jnp
from jax import lax
from jax.experimental import pallas as pl
from jax.experimental.pallas import tpu as pltpu
from jax.sharding import PartitionSpec as P

leak_slope = 0.2


def padded(block, sides, width):
    for axis, dim in sides:
        count = lax.axis_size(axis)
        forward = [(i, i + 1) for i in range(count - 1)]
        forward.append((count - 1, 0))
        backward = [(target, source) for source, target in forward]
        low = lax.ppermute(
            lax.slice_in_dim(block, block.shape[dim] - width, None, axis=dim), axis, forward
        )
        high = lax.ppermute(lax.slice_in_dim(block, 0, width, axis=dim), axis, backward)
        block = jnp.concatenate([low, block, high], axis=dim)
    return block


def passed_along(block, axis, distance):
    devices = range(lax.axis_size(axis))
    route = [((i - distance) % len(devices), i) for i in devices]
    return lax.ppermute(block, axis, route)


def summed_over_slabs(block, axis):
    count = lax.axis_size(axis)
    if count & (count - 1):
        return lax.psum(block, axis)
    step = 1
    while step < count:
        route = [(i, i ^ step) for i in range(count)]
        block = block + lax.ppermute(block, axis, route)
        step *= 2
    return block


def vmem_specs(count):
    return [pl.BlockSpec(memory_space=pltpu.VMEM)] * count


def fine_kernel(z_lo, z_hi, scale, *refs):
    pieces = refs[:6]
    if len(refs) == 13:
        sp_ref, w_ref, start_ref, gp_ref, r_ref, g_ref, sems = refs[6:]
    else:
        sp_ref, w_ref, gp_ref, r_ref, g_ref, sems = refs[6:]
        start_ref = None
    planes_z, planes_x, part_ch, cells_y = sp_ref.shape
    wide = g_ref.shape[4]
    low_count = pieces[0].shape[0]
    needed = sorted({z + 4 - 2 * dz for z in range(z_lo, z_hi) for dz in range(3)})
    edge = jnp.zeros(g_ref[:, :, :, 0].shape, g_ref.dtype)
    g_ref[:, :, :, 0] = edge
    g_ref[:, :, :, planes_x // 2 + 1] = edge
    copies = []
    for plane in needed:
        if plane < low_count:
            part, at = 0, plane
        elif plane < low_count + planes_z:
            part, at = 1, plane - low_count
        else:
            part, at = 2, plane - low_count - planes_z
        for half in range(2):
            for parity in range(2):
                copy = pltpu.make_async_copy(
                    pieces[3 * half + part].at[at, parity],
                    g_ref.at[
                        plane % 2,
                        plane // 2,
                        parity,
                        pl.ds(1, planes_x // 2),
                        pl.ds(half * part_ch, part_ch),
                    ],
                    sems.at[len(copies)],
                )
                copy.start()
                copies.append(copy)
    if start_ref is None:
        r_ref[...] = jnp.zeros(r_ref.shape, r_ref.dtype)
    else:
        r_ref[...] = start_ref[...]
    for copy in copies:
        copy.wait()

    def body(step, carry):
        z = z_lo + step // planes_x
        x = step % planes_x
        pre_act = sp_ref[z, x].astype(jnp.float32)
        slopes = jnp.where(pre_act > 0, 1.0, leak_slope).astype(jnp.float32)
        hidden = (pre_act * slopes).astype(jnp.bfloat16).astype(jnp.float32)
        rolled = jnp.concatenate(
            [pltpu.roll(hidden, 2, 1), hidden, pltpu.roll(hidden, cells_y - 2, 1)], axis=0
        ).astype(jnp.bfloat16)
        block = g_ref[z % 2, pl.ds(z // 2, 3), x % 2, pl.ds(x // 2, 3)]
        block = block.reshape(9 * wide, cells_y)
        total = jnp.dot(w_ref[...], block, preferred_element_type=jnp.float32)
        r_ref[...] += lax.dot_general(
            block, rolled, (((1,), (1,)), ((), ())), preferred_element_type=jnp.float32
        )
        grad_hidden = (
            pltpu.roll(total[:part_ch], cells_y - 2, 1)
            + total[part_ch : 2 * part_ch]
            + pltpu.roll(total[2 * part_ch :], 2, 1)
        )
        gp_ref[z - z_lo, x] = (grad_hidden * slopes).astype(gp_ref.dtype)
        return carry

    lax.fori_loop(0, (z_hi - z_lo) * planes_x, body, 0)
    if scale != 1.0:
        r_ref[...] = r_ref[...] * scale


def coarse_kernel(scale, gp_ref, last_ref, below_ref, own_ref, other_ref, u_ref, gc_ref, gu_ref, y_ref):
    planes_z = gp_ref.shape[0] + 1
    cells_y = gp_ref.shape[2]
    rows_x = y_ref.shape[1] - 1
    part_ch = y_ref.shape[3]
    half_y = y_ref.shape[4]
    coarse_z, coarse_x = own_ref.shape[0], own_ref.shape[1]
    first = lax.axis_index("ch") == 0
    at_y = lax.broadcasted_iota(jnp.int32, (cells_y, 3 * half_y), 0)
    col = lax.broadcasted_iota(jnp.int32, (cells_y, 3 * half_y), 1)
    target = 2 * (col % half_y) + col // half_y - 1
    target = jnp.where(target < 0, target + cells_y, target)
    pick = (at_y == target).astype(jnp.bfloat16)
    y_ref[:, 0] = jnp.zeros(y_ref[:, 0].shape, y_ref.dtype)
    for zg in range(planes_z + 1):
        if zg == 0:
            source = below_ref[0]
        elif zg == planes_z:
            source = last_ref[0]
        else:
            source = gp_ref[zg - 1]
        picked = jnp.dot(source, pick, preferred_element_type=jnp.float32).astype(y_ref.dtype)
        for dy in range(3):
            part = picked[:, dy * half_y : (dy + 1) * half_y]
            y_ref[zg, 1:, dy] = part.reshape(rows_x, part_ch, half_y)
    gu_ref[...] = jnp.zeros(gu_ref.shape, gu_ref.dtype)

    def body(step, carry):
        iz = step // coarse_x
        ix = step % coarse_x
        own = own_ref[iz, ix]
        other = other_ref[iz, ix]
        crow = jnp.concatenate(
            [jnp.where(first, own, other), jnp.where(first, other, own)], axis=0
        )
        total = jnp.zeros(gc_ref.shape[2:], jnp.float32)
        for dz in range(3):
            block = y_ref[2 * iz + dz, pl.ds(2 * ix, 3)]
            block = block.reshape(9 * part_ch, half_y)
            total = total + jnp.dot(u_ref[dz], block, preferred_element_type=jnp.float32)
            gu_ref[dz] += lax.dot_general(
                block, crow, (((1,), (1,)), ((), ())), preferred_element_type=jnp.float32
            )
        gc_ref[iz, ix] = total
        return carry

    lax.fori_loop(0, coarse_z * coarse_x, body, 0)
    gu_ref[...] = gu_ref[...] * scale


def local(coarse, saved_pre, out_grad, up_weight, refine_weight):
    part_ch = saved_pre.shape[0]
    planes_z = saved_pre.shape[1]
    planes_x = saved_pre.shape[2]
    cells_y = saved_pre.shape[3]
    all_ch = part_ch * lax.axis_size("ch")
    channel_start = lax.axis_index("ch") * part_ch

    rows = out_grad.reshape(part_ch, planes_z, planes_x // 2, 2, cells_y)
    rows = jnp.transpose(rows, (1, 3, 2, 0, 4))
    count = lax.axis_size(("gz", "sec"))
    forward = [(i, (i + 1) % count) for i in range(count)]
    backward = [(target, source) for source, target in forward]
    swap = [(i, i ^ 1) for i in range(lax.axis_size("ch"))]
    low = lax.ppermute(rows[planes_z - 2 :], ("gz", "sec"), forward)
    high = lax.ppermute(rows[:2], ("gz", "sec"), backward)
    rows_other = lax.ppermute(rows, "ch", swap)
    low_other = lax.ppermute(low, "ch", swap)
    high_other = lax.ppermute(high, "ch", swap)
    halo_z = low.shape[0] + planes_z + high.shape[0]
    pre_rows = jnp.transpose(saved_pre, (1, 2, 0, 3))

    refine_cols = lax.dynamic_slice_in_dim(refine_weight, channel_start, part_ch, 2)
    refine_cols = jnp.roll(refine_cols, -channel_start, axis=1)
    refine_w = refine_cols.reshape(3, 3, 3, all_ch, part_ch)[::-1, ::-1]
    refine_w = jnp.transpose(refine_w, (2, 4, 0, 1, 3)).reshape(3 * part_ch, 9 * all_ch)

    fine_total = planes_z * lax.axis_size("gz") * lax.axis_size("sec") * planes_x * cells_y
    coarse_total = fine_total // 8

    def fine_rows(z_lo, z_hi, *start):
        scale = float(fine_total) ** (-0.5) if start else 1.0
        return pl.pallas_call(
            functools.partial(fine_kernel, z_lo, z_hi, scale),
            out_shape=(
                jax.ShapeDtypeStruct((z_hi - z_lo, planes_x, part_ch, cells_y), jnp.bfloat16),
                jax.ShapeDtypeStruct((9 * all_ch, 3 * part_ch), jnp.float32),
            ),
            in_specs=[pl.BlockSpec(memory_space=pl.ANY)] * 6 + vmem_specs(2 + len(start)),
            out_specs=tuple(vmem_specs(2)),
            scratch_shapes=[
                pltpu.VMEM(
                    (2, halo_z // 2, 2, planes_x // 2 + 2, all_ch, cells_y), jnp.bfloat16
                ),
                pltpu.SemaphoreType.DMA((4 * halo_z,)),
            ],
        )(low, rows, high, low_other, rows_other, high_other, pre_rows, refine_w, *start)

    grad_last, refine_last = fine_rows(planes_z - 1, planes_z)
    last_rows = grad_last.reshape(1, planes_x * part_ch, cells_y)
    below_z = passed_along(last_rows, ("gz", "sec"), 1)
    grad_main, refine_acc = fine_rows(0, planes_z - 1, refine_last)
    grad_rows = grad_main.reshape(planes_z - 1, planes_x * part_ch, cells_y)
    refine_terms = refine_acc.reshape(3, 3, all_ch, 3, part_ch)[::-1, ::-1]
    refine_terms = jnp.transpose(refine_terms, (0, 1, 3, 2, 4)).reshape(27, all_ch, part_ch)
    refine_terms = jnp.roll(refine_terms, channel_start, axis=1)


    coarse_own = jnp.transpose(coarse, (1, 2, 0, 3))
    coarse_other = lax.ppermute(coarse_own, "ch", swap)
    own_k = coarse.shape[0]
    coarse_start = lax.axis_index("ch") * own_k
    coarse_in = 2 * own_k
    coarse_z, coarse_x, cells_yc = coarse.shape[1], coarse.shape[2], coarse.shape[3]
    up_rows = lax.dynamic_slice_in_dim(up_weight, channel_start, part_ch, 1)
    up_w = jnp.transpose(up_rows.reshape(3, 9, part_ch, coarse_in), (0, 3, 1, 2))
    up_w = up_w.reshape(3, coarse_in, 9 * part_ch)

    coarse_acc, up_acc = pl.pallas_call(
        functools.partial(coarse_kernel, float(coarse_total) ** (-0.5)),
        out_shape=(
            jax.ShapeDtypeStruct((coarse_z, coarse_x, coarse_in, cells_yc), jnp.float32),
            jax.ShapeDtypeStruct((3, 9 * part_ch, coarse_in), jnp.float32),
        ),
        in_specs=vmem_specs(6),
        out_specs=tuple(vmem_specs(2)),
        scratch_shapes=[
            pltpu.VMEM((planes_z + 1, planes_x + 1, 3, part_ch, cells_yc), jnp.bfloat16)
        ],
    )(grad_rows, last_rows, below_z, coarse_own, coarse_other, up_w)
    up_terms = up_acc.reshape(27, part_ch, coarse_in)
    other_start = own_k - coarse_start
    received = lax.ppermute(lax.dynamic_slice_in_dim(coarse_acc, other_start, own_k, 2), "ch", swap)
    coarse_summed = lax.dynamic_slice_in_dim(coarse_acc, coarse_start, own_k, 2) + received
    grad_coarse = jnp.transpose(coarse_summed, (2, 0, 1, 3)).astype(jnp.bfloat16)
    flat = jnp.concatenate([up_terms.reshape(-1), refine_terms.reshape(-1)])
    flat = summed_over_slabs(flat, ("gz", "sec"))
    grad_up = flat[: up_terms.size].reshape(up_terms.shape)
    grad_refine = flat[up_terms.size :].reshape(refine_terms.shape)
    return (grad_coarse, grad_up, grad_refine)


def solution(mesh):
    placed = (
        P("ch", ("groups", "gz", "sec"), None, None),
        P("ch", ("groups", "gz", "sec"), None, None),
        P("ch", ("groups", "gz", "sec"), None, None),
        P(),
        P(),
    )
    return jax.shard_map(
        local,
        mesh=mesh,
        in_specs=placed,
        out_specs=(
            P("ch", ("groups", "gz", "sec"), None, None),
            P("groups", "ch", None),
            P("groups", None, "ch"),
        ),
        check_vma=False,
    )
```

```python
import functools

import jax
import jax.numpy as jnp
from jax import lax
from jax.experimental import pallas as pl
from jax.experimental.pallas import tpu as pltpu
from jax.sharding import PartitionSpec as P

leak_slope = 0.2


def padded(block, sides, width):
    for axis, dim in sides:
        count = lax.axis_size(axis)
        forward = [(i, i + 1) for i in range(count - 1)]
        forward.append((count - 1, 0))
        backward = [(target, source) for source, target in forward]
        low = lax.ppermute(
            lax.slice_in_dim(block, block.shape[dim] - width, None, axis=dim), axis, forward
        )
        high = lax.ppermute(lax.slice_in_dim(block, 0, width, axis=dim), axis, backward)
        block = jnp.concatenate([low, block, high], axis=dim)
    return block


def passed_along(block, axis, distance):
    devices = range(lax.axis_size(axis))
    route = [((i - distance) % len(devices), i) for i in devices]
    return lax.ppermute(block, axis, route)


def summed_over_slabs(block, axis):
    count = lax.axis_size(axis)
    if count & (count - 1):
        return lax.psum(block, axis)
    step = 1
    while step < count:
        route = [(i, i ^ step) for i in range(count)]
        block = block + lax.ppermute(block, axis, route)
        step *= 2
    return block


def vmem_specs(count):
    return [pl.BlockSpec(memory_space=pltpu.VMEM)] * count


def fine_kernel(z_lo, z_hi, scale, *refs):
    pieces = refs[:6]
    if len(refs) == 13:
        sp_ref, w_ref, start_ref, gp_ref, r_ref, g_ref, sems = refs[6:]
    else:
        sp_ref, w_ref, gp_ref, r_ref, g_ref, sems = refs[6:]
        start_ref = None
    planes_z, planes_x, part_ch, cells_y = sp_ref.shape
    wide = g_ref.shape[4]
    low_count = pieces[0].shape[0]
    needed = sorted({z + 4 - 2 * dz for z in range(z_lo, z_hi) for dz in range(3)})
    edge = jnp.zeros(g_ref[:, :, :, 0].shape, g_ref.dtype)
    g_ref[:, :, :, 0] = edge
    g_ref[:, :, :, planes_x // 2 + 1] = edge
    copies = []
    for plane in needed:
        if plane < low_count:
            part, at = 0, plane
        elif plane < low_count + planes_z:
            part, at = 1, plane - low_count
        else:
            part, at = 2, plane - low_count - planes_z
        for half in range(2):
            for parity in range(2):
                copy = pltpu.make_async_copy(
                    pieces[3 * half + part].at[at, parity],
                    g_ref.at[
                        plane % 2,
                        plane // 2,
                        parity,
                        pl.ds(1, planes_x // 2),
                        pl.ds(half * part_ch, part_ch),
                    ],
                    sems.at[len(copies)],
                )
                copy.start()
                copies.append(copy)
    if start_ref is None:
        r_ref[...] = jnp.zeros(r_ref.shape, r_ref.dtype)
    else:
        r_ref[...] = start_ref[...]
    for copy in copies:
        copy.wait()

    def body(step, carry):
        z = z_lo + step // planes_x
        x = step % planes_x
        pre_act = sp_ref[z, x].astype(jnp.float32)
        slopes = jnp.where(pre_act > 0, 1.0, leak_slope).astype(jnp.float32)
        hidden = (pre_act * slopes).astype(jnp.bfloat16).astype(jnp.float32)
        rolled = jnp.concatenate(
            [pltpu.roll(hidden, 2, 1), hidden, pltpu.roll(hidden, cells_y - 2, 1)], axis=0
        ).astype(jnp.bfloat16)
        block = g_ref[z % 2, pl.ds(z // 2, 3), x % 2, pl.ds(x // 2, 3)]
        block = block.reshape(9 * wide, cells_y)
        total = jnp.dot(w_ref[...], block, preferred_element_type=jnp.float32)
        r_ref[...] += lax.dot_general(
            block, rolled, (((1,), (1,)), ((), ())), preferred_element_type=jnp.float32
        )
        grad_hidden = (
            pltpu.roll(total[:part_ch], cells_y - 2, 1)
            + total[part_ch : 2 * part_ch]
            + pltpu.roll(total[2 * part_ch :], 2, 1)
        )
        gp_ref[z - z_lo, x] = (grad_hidden * slopes).astype(gp_ref.dtype)
        return carry

    lax.fori_loop(0, (z_hi - z_lo) * planes_x, body, 0)
    if scale != 1.0:
        r_ref[...] = r_ref[...] * scale


def coarse_kernel(scale, gp_ref, last_ref, below_ref, own_ref, other_ref, u_ref, gc_ref, gu_ref, y_ref):
    planes_z = gp_ref.shape[0] + 1
    cells_y = gp_ref.shape[2]
    rows_x = y_ref.shape[1] - 1
    part_ch = y_ref.shape[3]
    half_y = y_ref.shape[4]
    coarse_z, coarse_x = own_ref.shape[0], own_ref.shape[1]
    first = lax.axis_index("ch") == 0
    at_y = lax.broadcasted_iota(jnp.int32, (cells_y, 3 * half_y), 0)
    col = lax.broadcasted_iota(jnp.int32, (cells_y, 3 * half_y), 1)
    target = 2 * (col % half_y) + col // half_y - 1
    target = jnp.where(target < 0, target + cells_y, target)
    pick = (at_y == target).astype(jnp.bfloat16)
    y_ref[:, 0] = jnp.zeros(y_ref[:, 0].shape, y_ref.dtype)
    for zg in range(planes_z + 1):
        if zg == 0:
            source = below_ref[0]
        elif zg == planes_z:
            source = last_ref[0]
        else:
            source = gp_ref[zg - 1]
        picked = jnp.dot(source, pick, preferred_element_type=jnp.float32).astype(y_ref.dtype)
        for dy in range(3):
            part = picked[:, dy * half_y : (dy + 1) * half_y]
            y_ref[zg, 1:, dy] = part.reshape(rows_x, part_ch, half_y)
    gu_ref[...] = jnp.zeros(gu_ref.shape, gu_ref.dtype)

    def body(step, carry):
        iz = step // coarse_x
        ix = step % coarse_x
        own = own_ref[iz, ix]
        other = other_ref[iz, ix]
        crow = jnp.concatenate(
            [jnp.where(first, own, other), jnp.where(first, other, own)], axis=0
        )
        total = jnp.zeros(gc_ref.shape[2:], jnp.float32)
        for dz in range(3):
            block = y_ref[2 * iz + dz, pl.ds(2 * ix, 3)]
            block = block.reshape(9 * part_ch, half_y)
            total = total + jnp.dot(u_ref[dz], block, preferred_element_type=jnp.float32)
            gu_ref[dz] += lax.dot_general(
                block, crow, (((1,), (1,)), ((), ())), preferred_element_type=jnp.float32
            )
        gc_ref[iz, ix] = total
        return carry

    lax.fori_loop(0, coarse_z * coarse_x, body, 0)
    gu_ref[...] = gu_ref[...] * scale


def local(coarse, saved_pre, out_grad, up_weight, refine_weight):
    part_ch = saved_pre.shape[0]
    planes_z = saved_pre.shape[1]
    planes_x = saved_pre.shape[2]
    cells_y = saved_pre.shape[3]
    all_ch = part_ch * lax.axis_size("ch")
    channel_start = lax.axis_index("ch") * part_ch

    rows = out_grad.reshape(part_ch, planes_z, planes_x // 2, 2, cells_y)
    rows = jnp.transpose(rows, (1, 3, 2, 0, 4))
    count = lax.axis_size(("gz", "sec"))
    forward = [(i, (i + 1) % count) for i in range(count)]
    backward = [(target, source) for source, target in forward]
    swap = [(i, i ^ 1) for i in range(lax.axis_size("ch"))]
    low = lax.ppermute(rows[planes_z - 2 :], ("gz", "sec"), forward)
    high = lax.ppermute(rows[:2], ("gz", "sec"), backward)
    rows_other = lax.ppermute(rows, "ch", swap)
    cores = lax.axis_size("ch")
    cross_forward = [
        (s * cores + c, t * cores + (c ^ 1)) for s, t in forward for c in range(cores)
    ]
    cross_backward = [
        (s * cores + c, t * cores + (c ^ 1)) for s, t in backward for c in range(cores)
    ]
    low_other = lax.ppermute(rows[planes_z - 2 :], ("gz", "sec", "ch"), cross_forward)
    high_other = lax.ppermute(rows[:2], ("gz", "sec", "ch"), cross_backward)
    halo_z = low.shape[0] + planes_z + high.shape[0]
    pre_rows = jnp.transpose(saved_pre, (1, 2, 0, 3))

    refine_cols = lax.dynamic_slice_in_dim(refine_weight, channel_start, part_ch, 2)
    refine_cols = jnp.roll(refine_cols, -channel_start, axis=1)
    refine_w = refine_cols.reshape(3, 3, 3, all_ch, part_ch)[::-1, ::-1]
    refine_w = jnp.transpose(refine_w, (2, 4, 0, 1, 3)).reshape(3 * part_ch, 9 * all_ch)

    fine_total = planes_z * lax.axis_size("gz") * lax.axis_size("sec") * planes_x * cells_y
    coarse_total = fine_total // 8

    def fine_rows(z_lo, z_hi, *start):
        scale = float(fine_total) ** (-0.5) if start else 1.0
        return pl.pallas_call(
            functools.partial(fine_kernel, z_lo, z_hi, scale),
            out_shape=(
                jax.ShapeDtypeStruct((z_hi - z_lo, planes_x, part_ch, cells_y), jnp.bfloat16),
                jax.ShapeDtypeStruct((9 * all_ch, 3 * part_ch), jnp.float32),
            ),
            in_specs=[pl.BlockSpec(memory_space=pl.ANY)] * 6 + vmem_specs(2 + len(start)),
            out_specs=tuple(vmem_specs(2)),
            scratch_shapes=[
                pltpu.VMEM(
                    (2, halo_z // 2, 2, planes_x // 2 + 2, all_ch, cells_y), jnp.bfloat16
                ),
                pltpu.SemaphoreType.DMA((4 * halo_z,)),
            ],
        )(low, rows, high, low_other, rows_other, high_other, pre_rows, refine_w, *start)

    grad_last, refine_last = fine_rows(planes_z - 1, planes_z)
    last_rows = grad_last.reshape(1, planes_x * part_ch, cells_y)
    below_z = passed_along(last_rows, ("gz", "sec"), 1)
    grad_main, refine_acc = fine_rows(0, planes_z - 1, refine_last)
    grad_rows = grad_main.reshape(planes_z - 1, planes_x * part_ch, cells_y)
    refine_terms = refine_acc.reshape(3, 3, all_ch, 3, part_ch)[::-1, ::-1]
    refine_terms = jnp.transpose(refine_terms, (0, 1, 3, 2, 4)).reshape(27, all_ch, part_ch)
    refine_terms = jnp.roll(refine_terms, channel_start, axis=1)


    coarse_own = jnp.transpose(coarse, (1, 2, 0, 3))
    coarse_other = lax.ppermute(coarse_own, "ch", swap)
    own_k = coarse.shape[0]
    coarse_start = lax.axis_index("ch") * own_k
    coarse_in = 2 * own_k
    coarse_z, coarse_x, cells_yc = coarse.shape[1], coarse.shape[2], coarse.shape[3]
    up_rows = lax.dynamic_slice_in_dim(up_weight, channel_start, part_ch, 1)
    up_w = jnp.transpose(up_rows.reshape(3, 9, part_ch, coarse_in), (0, 3, 1, 2))
    up_w = up_w.reshape(3, coarse_in, 9 * part_ch)

    coarse_acc, up_acc = pl.pallas_call(
        functools.partial(coarse_kernel, float(coarse_total) ** (-0.5)),
        out_shape=(
            jax.ShapeDtypeStruct((coarse_z, coarse_x, coarse_in, cells_yc), jnp.float32),
            jax.ShapeDtypeStruct((3, 9 * part_ch, coarse_in), jnp.float32),
        ),
        in_specs=vmem_specs(6),
        out_specs=tuple(vmem_specs(2)),
        scratch_shapes=[
            pltpu.VMEM((planes_z + 1, planes_x + 1, 3, part_ch, cells_yc), jnp.bfloat16)
        ],
    )(grad_rows, last_rows, below_z, coarse_own, coarse_other, up_w)
    up_terms = up_acc.reshape(27, part_ch, coarse_in)
    other_start = own_k - coarse_start
    received = lax.ppermute(lax.dynamic_slice_in_dim(coarse_acc, other_start, own_k, 2), "ch", swap)
    coarse_summed = lax.dynamic_slice_in_dim(coarse_acc, coarse_start, own_k, 2) + received
    grad_coarse = jnp.transpose(coarse_summed, (2, 0, 1, 3)).astype(jnp.bfloat16)
    flat = jnp.concatenate([up_terms.reshape(-1), refine_terms.reshape(-1)])
    flat = summed_over_slabs(flat, ("gz", "sec"))
    grad_up = flat[: up_terms.size].reshape(up_terms.shape)
    grad_refine = flat[up_terms.size :].reshape(refine_terms.shape)
    return (grad_coarse, grad_up, grad_refine)


def solution(mesh):
    placed = (
        P("ch", ("groups", "gz", "sec"), None, None),
        P("ch", ("groups", "gz", "sec"), None, None),
        P("ch", ("groups", "gz", "sec"), None, None),
        P(),
        P(),
    )
    return jax.shard_map(
        local,
        mesh=mesh,
        in_specs=placed,
        out_specs=(
            P("ch", ("groups", "gz", "sec"), None, None),
            P("groups", "ch", None),
            P("groups", None, "ch"),
        ),
        check_vma=False,
    )
```

```python
import functools

import jax
import jax.numpy as jnp
from jax import lax
from jax.experimental import pallas as pl
from jax.experimental.pallas import tpu as pltpu
from jax.sharding import PartitionSpec as P

leak_slope = 0.2


def padded(block, sides, width):
    for axis, dim in sides:
        count = lax.axis_size(axis)
        forward = [(i, i + 1) for i in range(count - 1)]
        forward.append((count - 1, 0))
        backward = [(target, source) for source, target in forward]
        low = lax.ppermute(
            lax.slice_in_dim(block, block.shape[dim] - width, None, axis=dim), axis, forward
        )
        high = lax.ppermute(lax.slice_in_dim(block, 0, width, axis=dim), axis, backward)
        block = jnp.concatenate([low, block, high], axis=dim)
    return block


def passed_along(block, axis, distance):
    devices = range(lax.axis_size(axis))
    route = [((i - distance) % len(devices), i) for i in devices]
    return lax.ppermute(block, axis, route)


def summed_over_slabs(block, axis):
    count = lax.axis_size(axis)
    if count & (count - 1):
        return lax.psum(block, axis)
    step = 1
    while step < count:
        route = [(i, i ^ step) for i in range(count)]
        block = block + lax.ppermute(block, axis, route)
        step *= 2
    return block


def vmem_specs(count):
    return [pl.BlockSpec(memory_space=pltpu.VMEM)] * count


def fine_kernel(z_lo, z_hi, scale, *refs):
    pieces = refs[:6]
    if len(refs) == 14:
        sp_ref, w_ref, start_ref, gp_ref, r_ref, final_ref, g_ref, sems = refs[6:]
    else:
        sp_ref, w_ref, gp_ref, r_ref, g_ref, sems = refs[6:]
        start_ref = final_ref = None
    planes_z, planes_x, part_ch, cells_y = sp_ref.shape
    wide = g_ref.shape[4]
    low_count = pieces[0].shape[0]
    core = lax.axis_index("ch")
    needed = sorted({z + 4 - 2 * dz for z in range(z_lo, z_hi) for dz in range(3)})
    edge = jnp.zeros(g_ref[:, :, :, 0].shape, g_ref.dtype)
    g_ref[:, :, :, 0] = edge
    g_ref[:, :, :, planes_x // 2 + 1] = edge
    copies = []
    for plane in needed:
        if plane < low_count:
            part, at = 0, plane
        elif plane < low_count + planes_z:
            part, at = 1, plane - low_count
        else:
            part, at = 2, plane - low_count - planes_z
        for half in range(2):
            for parity in range(2):
                copy = pltpu.make_async_copy(
                    pieces[3 * half + part].at[at, parity],
                    g_ref.at[
                        plane % 2,
                        plane // 2,
                        parity,
                        pl.ds(1, planes_x // 2),
                        pl.ds(pl.multiple_of(((half + core) % 2) * part_ch, part_ch), part_ch),
                    ],
                    sems.at[len(copies)],
                )
                copy.start()
                copies.append(copy)
    if start_ref is None:
        r_ref[...] = jnp.zeros(r_ref.shape, r_ref.dtype)
    else:
        r_ref[...] = start_ref[...]
    for copy in copies:
        copy.wait()

    def body(step, carry):
        z = z_lo + step // planes_x
        x = step % planes_x
        pre_act = sp_ref[z, x].astype(jnp.float32)
        slopes = jnp.where(pre_act > 0, 1.0, leak_slope).astype(jnp.float32)
        hidden = (pre_act * slopes).astype(jnp.bfloat16).astype(jnp.float32)
        rolled = jnp.concatenate(
            [pltpu.roll(hidden, 2, 1), hidden, pltpu.roll(hidden, cells_y - 2, 1)], axis=0
        ).astype(jnp.bfloat16)
        block = g_ref[z % 2, pl.ds(z // 2, 3), x % 2, pl.ds(x // 2, 3)]
        block = block.reshape(9 * wide, cells_y)
        total = jnp.dot(w_ref[...], block, preferred_element_type=jnp.float32)
        r_ref[...] += lax.dot_general(
            block, rolled, (((1,), (1,)), ((), ())), preferred_element_type=jnp.float32
        )
        grad_hidden = (
            pltpu.roll(total[:part_ch], cells_y - 2, 1)
            + total[part_ch : 2 * part_ch]
            + pltpu.roll(total[2 * part_ch :], 2, 1)
        )
        gp_ref[z - z_lo, x] = (grad_hidden * slopes).astype(gp_ref.dtype)
        return carry

    lax.fori_loop(0, (z_hi - z_lo) * planes_x, body, 0)
    if final_ref is not None:
        acc = r_ref[...] * scale
        for dz in range(3):
            for dx in range(3):
                rows_at = (3 * (2 - dz) + (2 - dx)) * wide
                for dy in range(3):
                    final_ref[9 * dz + 3 * dx + dy] = acc[
                        rows_at : rows_at + wide, dy * part_ch : (dy + 1) * part_ch
                    ]


def coarse_kernel(scale, gp_ref, last_ref, below_ref, own_ref, other_ref, u_ref, gc_ref, gu_ref, y_ref):
    planes_z = gp_ref.shape[0] + 1
    cells_y = gp_ref.shape[2]
    rows_x = y_ref.shape[1] - 1
    part_ch = y_ref.shape[3]
    half_y = y_ref.shape[4]
    coarse_z, coarse_x = own_ref.shape[0], own_ref.shape[1]
    first = lax.axis_index("ch") == 0
    at_y = lax.broadcasted_iota(jnp.int32, (cells_y, 3 * half_y), 0)
    col = lax.broadcasted_iota(jnp.int32, (cells_y, 3 * half_y), 1)
    target = 2 * (col % half_y) + col // half_y - 1
    target = jnp.where(target < 0, target + cells_y, target)
    pick = (at_y == target).astype(jnp.bfloat16)
    y_ref[:, 0] = jnp.zeros(y_ref[:, 0].shape, y_ref.dtype)
    for zg in range(planes_z + 1):
        if zg == 0:
            source = below_ref[0]
        elif zg == planes_z:
            source = last_ref[0]
        else:
            source = gp_ref[zg - 1]
        picked = jnp.dot(source, pick, preferred_element_type=jnp.float32).astype(y_ref.dtype)
        for dy in range(3):
            part = picked[:, dy * half_y : (dy + 1) * half_y]
            y_ref[zg, 1:, dy] = part.reshape(rows_x, part_ch, half_y)
    gu_ref[...] = jnp.zeros(gu_ref.shape, gu_ref.dtype)

    def body(step, carry):
        iz = step // coarse_x
        ix = step % coarse_x
        own = own_ref[iz, ix]
        other = other_ref[iz, ix]
        crow = jnp.concatenate(
            [jnp.where(first, own, other), jnp.where(first, other, own)], axis=0
        )
        total = jnp.zeros(gc_ref.shape[2:], jnp.float32)
        for dz in range(3):
            block = y_ref[2 * iz + dz, pl.ds(2 * ix, 3)]
            block = block.reshape(9 * part_ch, half_y)
            total = total + jnp.dot(u_ref[dz], block, preferred_element_type=jnp.float32)
            gu_ref[dz] += lax.dot_general(
                block, crow, (((1,), (1,)), ((), ())), preferred_element_type=jnp.float32
            )
        gc_ref[iz, ix] = total
        return carry

    lax.fori_loop(0, coarse_z * coarse_x, body, 0)
    gu_ref[...] = gu_ref[...] * scale


def local(coarse, saved_pre, out_grad, up_weight, refine_weight):
    part_ch = saved_pre.shape[0]
    planes_z = saved_pre.shape[1]
    planes_x = saved_pre.shape[2]
    cells_y = saved_pre.shape[3]
    all_ch = part_ch * lax.axis_size("ch")
    channel_start = lax.axis_index("ch") * part_ch

    rows = out_grad.reshape(part_ch, planes_z, planes_x // 2, 2, cells_y)
    rows = jnp.transpose(rows, (1, 3, 2, 0, 4))
    count = lax.axis_size(("gz", "sec"))
    forward = [(i, (i + 1) % count) for i in range(count)]
    backward = [(target, source) for source, target in forward]
    swap = [(i, i ^ 1) for i in range(lax.axis_size("ch"))]
    low = lax.ppermute(rows[planes_z - 2 :], ("gz", "sec"), forward)
    high = lax.ppermute(rows[:2], ("gz", "sec"), backward)
    rows_other = lax.ppermute(rows, "ch", swap)
    low_other = lax.ppermute(low, "ch", swap)
    high_other = lax.ppermute(high, "ch", swap)
    halo_z = low.shape[0] + planes_z + high.shape[0]
    pre_rows = jnp.transpose(saved_pre, (1, 2, 0, 3))

    refine_cols = lax.dynamic_slice_in_dim(refine_weight, channel_start, part_ch, 2)
    refine_w = refine_cols.reshape(3, 3, 3, all_ch, part_ch)[::-1, ::-1]
    refine_w = jnp.transpose(refine_w, (2, 4, 0, 1, 3)).reshape(3 * part_ch, 9 * all_ch)

    fine_total = planes_z * lax.axis_size("gz") * lax.axis_size("sec") * planes_x * cells_y
    coarse_total = fine_total // 8

    def fine_rows(z_lo, z_hi, *start):
        scale = float(fine_total) ** (-0.5) if start else 1.0
        return pl.pallas_call(
            functools.partial(fine_kernel, z_lo, z_hi, scale),
            out_shape=(
                jax.ShapeDtypeStruct((z_hi - z_lo, planes_x, part_ch, cells_y), jnp.bfloat16),
                jax.ShapeDtypeStruct((9 * all_ch, 3 * part_ch), jnp.float32),
            )
            + ((jax.ShapeDtypeStruct((27, all_ch, part_ch), jnp.float32),) if start else ()),
            in_specs=[pl.BlockSpec(memory_space=pl.ANY)] * 6 + vmem_specs(2 + len(start)),
            out_specs=tuple(vmem_specs(2 + len(start))),
            scratch_shapes=[
                pltpu.VMEM(
                    (2, halo_z // 2, 2, planes_x // 2 + 2, all_ch, cells_y), jnp.bfloat16
                ),
                pltpu.SemaphoreType.DMA((4 * halo_z,)),
            ],
        )(low, rows, high, low_other, rows_other, high_other, pre_rows, refine_w, *start)

    grad_last, refine_last = fine_rows(planes_z - 1, planes_z)
    last_rows = grad_last.reshape(1, planes_x * part_ch, cells_y)
    below_z = passed_along(last_rows, ("gz", "sec"), 1)
    grad_main, _, refine_terms = fine_rows(0, planes_z - 1, refine_last)
    grad_rows = grad_main.reshape(planes_z - 1, planes_x * part_ch, cells_y)

    coarse_own = jnp.transpose(coarse, (1, 2, 0, 3))
    coarse_other = lax.ppermute(coarse_own, "ch", swap)
    own_k = coarse.shape[0]
    coarse_start = lax.axis_index("ch") * own_k
    coarse_in = 2 * own_k
    coarse_z, coarse_x, cells_yc = coarse.shape[1], coarse.shape[2], coarse.shape[3]
    up_rows = lax.dynamic_slice_in_dim(up_weight, channel_start, part_ch, 1)
    up_w = jnp.transpose(up_rows.reshape(3, 9, part_ch, coarse_in), (0, 3, 1, 2))
    up_w = up_w.reshape(3, coarse_in, 9 * part_ch)

    coarse_acc, up_acc = pl.pallas_call(
        functools.partial(coarse_kernel, float(coarse_total) ** (-0.5)),
        out_shape=(
            jax.ShapeDtypeStruct((coarse_z, coarse_x, coarse_in, cells_yc), jnp.float32),
            jax.ShapeDtypeStruct((3, 9 * part_ch, coarse_in), jnp.float32),
        ),
        in_specs=vmem_specs(6),
        out_specs=tuple(vmem_specs(2)),
        scratch_shapes=[
            pltpu.VMEM((planes_z + 1, planes_x + 1, 3, part_ch, cells_yc), jnp.bfloat16)
        ],
    )(grad_rows, last_rows, below_z, coarse_own, coarse_other, up_w)
    up_terms = up_acc.reshape(27, part_ch, coarse_in)
    other_start = own_k - coarse_start
    received = lax.ppermute(lax.dynamic_slice_in_dim(coarse_acc, other_start, own_k, 2), "ch", swap)
    coarse_summed = lax.dynamic_slice_in_dim(coarse_acc, coarse_start, own_k, 2) + received
    grad_coarse = jnp.transpose(coarse_summed, (2, 0, 1, 3)).astype(jnp.bfloat16)
    flat = jnp.concatenate([up_terms.reshape(-1), refine_terms.reshape(-1)])
    flat = summed_over_slabs(flat, ("gz", "sec"))
    grad_up = flat[: up_terms.size].reshape(up_terms.shape)
    grad_refine = flat[up_terms.size :].reshape(refine_terms.shape)
    return (grad_coarse, grad_up, grad_refine)


def solution(mesh):
    placed = (
        P("ch", ("groups", "gz", "sec"), None, None),
        P("ch", ("groups", "gz", "sec"), None, None),
        P("ch", ("groups", "gz", "sec"), None, None),
        P(),
        P(),
    )
    return jax.shard_map(
        local,
        mesh=mesh,
        in_specs=placed,
        out_specs=(
            P("ch", ("groups", "gz", "sec"), None, None),
            P("groups", "ch", None),
            P("groups", None, "ch"),
        ),
        check_vma=False,
    )
```

```python
import functools

import jax
import jax.numpy as jnp
from jax import lax
from jax.experimental import pallas as pl
from jax.experimental.pallas import tpu as pltpu
from jax.sharding import PartitionSpec as P

leak_slope = 0.2


def padded(block, sides, width):
    for axis, dim in sides:
        count = lax.axis_size(axis)
        forward = [(i, i + 1) for i in range(count - 1)]
        forward.append((count - 1, 0))
        backward = [(target, source) for source, target in forward]
        low = lax.ppermute(
            lax.slice_in_dim(block, block.shape[dim] - width, None, axis=dim), axis, forward
        )
        high = lax.ppermute(lax.slice_in_dim(block, 0, width, axis=dim), axis, backward)
        block = jnp.concatenate([low, block, high], axis=dim)
    return block


def passed_along(block, axis, distance):
    devices = range(lax.axis_size(axis))
    route = [((i - distance) % len(devices), i) for i in devices]
    return lax.ppermute(block, axis, route)


def summed_over_slabs(block, axis):
    count = lax.axis_size(axis)
    if count & (count - 1):
        return lax.psum(block, axis)
    step = 1
    while step < count:
        route = [(i, i ^ step) for i in range(count)]
        block = block + lax.ppermute(block, axis, route)
        step *= 2
    return block


def vmem_specs(count):
    return [pl.BlockSpec(memory_space=pltpu.VMEM)] * count


def fine_kernel(z_lo, z_hi, scale, *refs):
    pieces = refs[:6]
    if len(refs) == 14:
        sp_ref, w_ref, start_ref, gp_ref, r_ref, final_ref, g_ref, sems = refs[6:]
    else:
        sp_ref, w_ref, gp_ref, r_ref, g_ref, sems = refs[6:]
        start_ref = final_ref = None
    planes_z, planes_x, part_ch, cells_y = sp_ref.shape
    wide = g_ref.shape[4]
    low_count = pieces[0].shape[0]
    core = lax.axis_index("ch")
    needed = sorted({z + 4 - 2 * dz for z in range(z_lo, z_hi) for dz in range(3)})
    edge = jnp.zeros(g_ref[:, :, :, 0].shape, g_ref.dtype)
    g_ref[:, :, :, 0] = edge
    g_ref[:, :, :, planes_x // 2 + 1] = edge
    copies = []
    for plane in needed:
        if plane < low_count:
            part, at = 0, plane
        elif plane < low_count + planes_z:
            part, at = 1, plane - low_count
        else:
            part, at = 2, plane - low_count - planes_z
        for half in range(2):
            for parity in range(2):
                copy = pltpu.make_async_copy(
                    pieces[3 * half + part].at[at, parity],
                    g_ref.at[
                        plane % 2,
                        plane // 2,
                        parity,
                        pl.ds(1, planes_x // 2),
                        pl.ds(pl.multiple_of(((half + core) % 2) * part_ch, part_ch), part_ch),
                    ],
                    sems.at[len(copies)],
                )
                copy.start()
                copies.append(copy)
    if start_ref is None:
        r_ref[...] = jnp.zeros(r_ref.shape, r_ref.dtype)
    else:
        r_ref[...] = start_ref[...]
    for copy in copies:
        copy.wait()

    def body(step, carry):
        z = z_lo + step // planes_x
        x = step % planes_x
        pre_act = sp_ref[z, x].astype(jnp.float32)
        slopes = jnp.where(pre_act > 0, 1.0, leak_slope).astype(jnp.float32)
        hidden = (pre_act * slopes).astype(jnp.bfloat16).astype(jnp.float32)
        rolled = jnp.concatenate(
            [pltpu.roll(hidden, 2, 1), hidden, pltpu.roll(hidden, cells_y - 2, 1)], axis=0
        ).astype(jnp.bfloat16)
        block = g_ref[z % 2, pl.ds(z // 2, 3), x % 2, pl.ds(x // 2, 3)]
        block = block.reshape(9 * wide, cells_y)
        total = jnp.dot(w_ref[...], block, preferred_element_type=jnp.float32)
        r_ref[...] += lax.dot_general(
            block, rolled, (((1,), (1,)), ((), ())), preferred_element_type=jnp.float32
        )
        grad_hidden = (
            pltpu.roll(total[:part_ch], cells_y - 2, 1)
            + total[part_ch : 2 * part_ch]
            + pltpu.roll(total[2 * part_ch :], 2, 1)
        )
        gp_ref[z - z_lo, x] = (grad_hidden * slopes).astype(gp_ref.dtype)
        return carry

    lax.fori_loop(0, (z_hi - z_lo) * planes_x, body, 0)
    if final_ref is not None:
        acc = r_ref[...] * scale
        for dz in range(3):
            for dx in range(3):
                rows_at = (3 * (2 - dz) + (2 - dx)) * wide
                for dy in range(3):
                    final_ref[9 * dz + 3 * dx + dy] = acc[
                        rows_at : rows_at + wide, dy * part_ch : (dy + 1) * part_ch
                    ]


def coarse_kernel(scale, gp_ref, last_ref, below_ref, own_ref, other_ref, u_ref, gc_ref, gu_ref, y_ref):
    planes_z = gp_ref.shape[0] + 1
    cells_y = gp_ref.shape[2]
    rows_x = y_ref.shape[1] - 1
    part_ch = y_ref.shape[3]
    half_y = y_ref.shape[4]
    coarse_z, coarse_x = own_ref.shape[0], own_ref.shape[1]
    first = lax.axis_index("ch") == 0
    at_y = lax.broadcasted_iota(jnp.int32, (cells_y, 3 * half_y), 0)
    col = lax.broadcasted_iota(jnp.int32, (cells_y, 3 * half_y), 1)
    target = 2 * (col % half_y) + col // half_y - 1
    target = jnp.where(target < 0, target + cells_y, target)
    pick = (at_y == target).astype(jnp.bfloat16)
    y_ref[:, 0] = jnp.zeros(y_ref[:, 0].shape, y_ref.dtype)
    for zg in range(planes_z + 1):
        if zg == 0:
            source = below_ref[0]
        elif zg == planes_z:
            source = last_ref[0]
        else:
            source = gp_ref[zg - 1]
        picked = jnp.dot(source, pick, preferred_element_type=jnp.float32).astype(y_ref.dtype)
        for dy in range(3):
            part = picked[:, dy * half_y : (dy + 1) * half_y]
            y_ref[zg, 1:, dy] = part.reshape(rows_x, part_ch, half_y)
    gu_ref[...] = jnp.zeros(gu_ref.shape, gu_ref.dtype)

    def body(step, carry):
        iz = step // coarse_x
        ix = step % coarse_x
        own = own_ref[iz, ix]
        other = other_ref[iz, ix]
        crow = jnp.concatenate(
            [jnp.where(first, own, other), jnp.where(first, other, own)], axis=0
        )
        total = jnp.zeros(gc_ref.shape[2:], jnp.float32)
        for dz in range(3):
            block = y_ref[2 * iz + dz, pl.ds(2 * ix, 3)]
            block = block.reshape(9 * part_ch, half_y)
            total = total + jnp.dot(u_ref[dz], block, preferred_element_type=jnp.float32)
            gu_ref[dz] += lax.dot_general(
                block, crow, (((1,), (1,)), ((), ())), preferred_element_type=jnp.float32
            )
        gc_ref[iz, ix] = total
        return carry

    lax.fori_loop(0, coarse_z * coarse_x, body, 0)
    gu_ref[...] = gu_ref[...] * scale


def local(coarse, saved_pre, out_grad, up_weight, refine_weight):
    part_ch = saved_pre.shape[0]
    planes_z = saved_pre.shape[1]
    planes_x = saved_pre.shape[2]
    cells_y = saved_pre.shape[3]
    all_ch = part_ch * lax.axis_size("ch")
    channel_start = lax.axis_index("ch") * part_ch

    rows = out_grad.reshape(part_ch, planes_z, planes_x // 2, 2, cells_y)
    rows = jnp.transpose(rows, (1, 3, 2, 0, 4))
    count = lax.axis_size(("gz", "sec"))
    forward = [(i, (i + 1) % count) for i in range(count)]
    backward = [(target, source) for source, target in forward]
    swap = [(i, i ^ 1) for i in range(lax.axis_size("ch"))]
    def laid_out(block):
        block = block.reshape(part_ch, block.shape[1], planes_x // 2, 2, cells_y)
        return jnp.transpose(block, (1, 3, 2, 0, 4))

    low = laid_out(lax.ppermute(out_grad[:, planes_z - 2 :], ("gz", "sec"), forward))
    high = laid_out(lax.ppermute(out_grad[:, :2], ("gz", "sec"), backward))
    rows_other = lax.ppermute(rows, "ch", swap)
    low_other = lax.ppermute(low, "ch", swap)
    high_other = lax.ppermute(high, "ch", swap)
    halo_z = low.shape[0] + planes_z + high.shape[0]
    pre_rows = jnp.transpose(saved_pre, (1, 2, 0, 3))

    refine_cols = lax.dynamic_slice_in_dim(refine_weight, channel_start, part_ch, 2)
    refine_w = refine_cols.reshape(3, 3, 3, all_ch, part_ch)[::-1, ::-1]
    refine_w = jnp.transpose(refine_w, (2, 4, 0, 1, 3)).reshape(3 * part_ch, 9 * all_ch)

    fine_total = planes_z * lax.axis_size("gz") * lax.axis_size("sec") * planes_x * cells_y
    coarse_total = fine_total // 8

    def fine_rows(z_lo, z_hi, *start):
        scale = float(fine_total) ** (-0.5) if start else 1.0
        return pl.pallas_call(
            functools.partial(fine_kernel, z_lo, z_hi, scale),
            out_shape=(
                jax.ShapeDtypeStruct((z_hi - z_lo, planes_x, part_ch, cells_y), jnp.bfloat16),
                jax.ShapeDtypeStruct((9 * all_ch, 3 * part_ch), jnp.float32),
            )
            + ((jax.ShapeDtypeStruct((27, all_ch, part_ch), jnp.float32),) if start else ()),
            in_specs=[pl.BlockSpec(memory_space=pl.ANY)] * 6 + vmem_specs(2 + len(start)),
            out_specs=tuple(vmem_specs(2 + len(start))),
            scratch_shapes=[
                pltpu.VMEM(
                    (2, halo_z // 2, 2, planes_x // 2 + 2, all_ch, cells_y), jnp.bfloat16
                ),
                pltpu.SemaphoreType.DMA((4 * halo_z,)),
            ],
        )(low, rows, high, low_other, rows_other, high_other, pre_rows, refine_w, *start)

    grad_last, refine_last = fine_rows(planes_z - 1, planes_z)
    last_rows = grad_last.reshape(1, planes_x * part_ch, cells_y)
    below_z = passed_along(last_rows, ("gz", "sec"), 1)
    grad_main, _, refine_terms = fine_rows(0, planes_z - 1, refine_last)
    grad_rows = grad_main.reshape(planes_z - 1, planes_x * part_ch, cells_y)

    coarse_own = jnp.transpose(coarse, (1, 2, 0, 3))
    coarse_other = lax.ppermute(coarse_own, "ch", swap)
    own_k = coarse.shape[0]
    coarse_start = lax.axis_index("ch") * own_k
    coarse_in = 2 * own_k
    coarse_z, coarse_x, cells_yc = coarse.shape[1], coarse.shape[2], coarse.shape[3]
    up_rows = lax.dynamic_slice_in_dim(up_weight, channel_start, part_ch, 1)
    up_w = jnp.transpose(up_rows.reshape(3, 9, part_ch, coarse_in), (0, 3, 1, 2))
    up_w = up_w.reshape(3, coarse_in, 9 * part_ch)

    coarse_acc, up_acc = pl.pallas_call(
        functools.partial(coarse_kernel, float(coarse_total) ** (-0.5)),
        out_shape=(
            jax.ShapeDtypeStruct((coarse_z, coarse_x, coarse_in, cells_yc), jnp.float32),
            jax.ShapeDtypeStruct((3, 9 * part_ch, coarse_in), jnp.float32),
        ),
        in_specs=vmem_specs(6),
        out_specs=tuple(vmem_specs(2)),
        scratch_shapes=[
            pltpu.VMEM((planes_z + 1, planes_x + 1, 3, part_ch, cells_yc), jnp.bfloat16)
        ],
    )(grad_rows, last_rows, below_z, coarse_own, coarse_other, up_w)
    up_terms = up_acc.reshape(27, part_ch, coarse_in)
    other_start = own_k - coarse_start
    received = lax.ppermute(lax.dynamic_slice_in_dim(coarse_acc, other_start, own_k, 2), "ch", swap)
    coarse_summed = lax.dynamic_slice_in_dim(coarse_acc, coarse_start, own_k, 2) + received
    grad_coarse = jnp.transpose(coarse_summed, (2, 0, 1, 3)).astype(jnp.bfloat16)
    flat = jnp.concatenate([up_terms.reshape(-1), refine_terms.reshape(-1)])
    flat = summed_over_slabs(flat, ("gz", "sec"))
    grad_up = flat[: up_terms.size].reshape(up_terms.shape)
    grad_refine = flat[up_terms.size :].reshape(refine_terms.shape)
    return (grad_coarse, grad_up, grad_refine)


def solution(mesh):
    placed = (
        P("ch", ("groups", "gz", "sec"), None, None),
        P("ch", ("groups", "gz", "sec"), None, None),
        P("ch", ("groups", "gz", "sec"), None, None),
        P(),
        P(),
    )
    return jax.shard_map(
        local,
        mesh=mesh,
        in_specs=placed,
        out_specs=(
            P("ch", ("groups", "gz", "sec"), None, None),
            P("groups", "ch", None),
            P("groups", None, "ch"),
        ),
        check_vma=False,
    )
```

```python
import functools

import jax
import jax.numpy as jnp
from jax import lax
from jax.experimental import pallas as pl
from jax.experimental.pallas import tpu as pltpu
from jax.sharding import PartitionSpec as P

leak_slope = 0.2


def padded(block, sides, width):
    for axis, dim in sides:
        count = lax.axis_size(axis)
        forward = [(i, i + 1) for i in range(count - 1)]
        forward.append((count - 1, 0))
        backward = [(target, source) for source, target in forward]
        low = lax.ppermute(
            lax.slice_in_dim(block, block.shape[dim] - width, None, axis=dim), axis, forward
        )
        high = lax.ppermute(lax.slice_in_dim(block, 0, width, axis=dim), axis, backward)
        block = jnp.concatenate([low, block, high], axis=dim)
    return block


def passed_along(block, axis, distance):
    devices = range(lax.axis_size(axis))
    route = [((i - distance) % len(devices), i) for i in devices]
    return lax.ppermute(block, axis, route)


def summed_over_slabs(block, axis):
    count = lax.axis_size(axis)
    if count & (count - 1):
        return lax.psum(block, axis)
    step = 1
    while step < count:
        route = [(i, i ^ step) for i in range(count)]
        block = block + lax.ppermute(block, axis, route)
        step *= 2
    return block


def vmem_specs(count):
    return [pl.BlockSpec(memory_space=pltpu.VMEM)] * count


def fine_kernel(z_lo, z_hi, scale, *refs):
    pieces = refs[:4]
    if len(refs) == 12:
        sp_ref, w_ref, start_ref, gp_ref, r_ref, final_ref, g_ref, sems = refs[4:]
    else:
        sp_ref, w_ref, gp_ref, r_ref, g_ref, sems = refs[4:]
        start_ref = final_ref = None
    planes_z, planes_x, part_ch, cells_y = sp_ref.shape
    wide = g_ref.shape[4]
    low_count = pieces[0].shape[0] // 2
    core = lax.axis_index("ch")
    needed = sorted({z + 4 - 2 * dz for z in range(z_lo, z_hi) for dz in range(3)})
    edge = jnp.zeros(g_ref[:, :, :, 0].shape, g_ref.dtype)
    g_ref[:, :, :, 0] = edge
    g_ref[:, :, :, planes_x // 2 + 1] = edge
    copies = []
    for plane in needed:
        if plane < low_count:
            part, at = 0, plane
        elif plane < low_count + planes_z:
            part, at = 1, plane - low_count
        else:
            part, at = 0, plane - planes_z
        for half in range(2):
            for parity in range(2):
                copy = pltpu.make_async_copy(
                    pieces[2 * half + part].at[at, parity],
                    g_ref.at[
                        plane % 2,
                        plane // 2,
                        parity,
                        pl.ds(1, planes_x // 2),
                        pl.ds(pl.multiple_of(((half + core) % 2) * part_ch, part_ch), part_ch),
                    ],
                    sems.at[len(copies)],
                )
                copy.start()
                copies.append(copy)
    if start_ref is None:
        r_ref[...] = jnp.zeros(r_ref.shape, r_ref.dtype)
    else:
        r_ref[...] = start_ref[...]
    for copy in copies:
        copy.wait()

    def body(step, carry):
        z = z_lo + step // planes_x
        x = step % planes_x
        pre_act = sp_ref[z, x].astype(jnp.float32)
        slopes = jnp.where(pre_act > 0, 1.0, leak_slope).astype(jnp.float32)
        hidden = (pre_act * slopes).astype(jnp.bfloat16).astype(jnp.float32)
        rolled = jnp.concatenate(
            [pltpu.roll(hidden, 2, 1), hidden, pltpu.roll(hidden, cells_y - 2, 1)], axis=0
        ).astype(jnp.bfloat16)
        block = g_ref[z % 2, pl.ds(z // 2, 3), x % 2, pl.ds(x // 2, 3)]
        block = block.reshape(9 * wide, cells_y)
        total = jnp.dot(w_ref[...], block, preferred_element_type=jnp.float32)
        r_ref[...] += lax.dot_general(
            block, rolled, (((1,), (1,)), ((), ())), preferred_element_type=jnp.float32
        )
        grad_hidden = (
            pltpu.roll(total[:part_ch], cells_y - 2, 1)
            + total[part_ch : 2 * part_ch]
            + pltpu.roll(total[2 * part_ch :], 2, 1)
        )
        gp_ref[z - z_lo, x] = (grad_hidden * slopes).astype(gp_ref.dtype)
        return carry

    lax.fori_loop(0, (z_hi - z_lo) * planes_x, body, 0)
    if final_ref is not None:
        acc = r_ref[...] * scale
        for dz in range(3):
            for dx in range(3):
                rows_at = (3 * (2 - dz) + (2 - dx)) * wide
                for dy in range(3):
                    final_ref[9 * dz + 3 * dx + dy] = acc[
                        rows_at : rows_at + wide, dy * part_ch : (dy + 1) * part_ch
                    ]


def coarse_kernel(scale, gp_ref, last_ref, below_ref, own_ref, other_ref, u_ref, gc_ref, gu_ref, y_ref):
    planes_z = gp_ref.shape[0] + 1
    cells_y = gp_ref.shape[2]
    rows_x = y_ref.shape[1] - 1
    part_ch = y_ref.shape[3]
    half_y = y_ref.shape[4]
    coarse_z, coarse_x = own_ref.shape[0], own_ref.shape[1]
    first = lax.axis_index("ch") == 0
    at_y = lax.broadcasted_iota(jnp.int32, (cells_y, 3 * half_y), 0)
    col = lax.broadcasted_iota(jnp.int32, (cells_y, 3 * half_y), 1)
    target = 2 * (col % half_y) + col // half_y - 1
    target = jnp.where(target < 0, target + cells_y, target)
    pick = (at_y == target).astype(jnp.bfloat16)
    y_ref[:, 0] = jnp.zeros(y_ref[:, 0].shape, y_ref.dtype)
    for zg in range(planes_z + 1):
        if zg == 0:
            source = below_ref[0]
        elif zg == planes_z:
            source = last_ref[0]
        else:
            source = gp_ref[zg - 1]
        picked = jnp.dot(source, pick, preferred_element_type=jnp.float32).astype(y_ref.dtype)
        for dy in range(3):
            part = picked[:, dy * half_y : (dy + 1) * half_y]
            y_ref[zg, 1:, dy] = part.reshape(rows_x, part_ch, half_y)
    gu_ref[...] = jnp.zeros(gu_ref.shape, gu_ref.dtype)

    def body(step, carry):
        iz = step // coarse_x
        ix = step % coarse_x
        own = own_ref[iz, ix]
        other = other_ref[iz, ix]
        crow = jnp.concatenate(
            [jnp.where(first, own, other), jnp.where(first, other, own)], axis=0
        )
        total = jnp.zeros(gc_ref.shape[2:], jnp.float32)
        for dz in range(3):
            block = y_ref[2 * iz + dz, pl.ds(2 * ix, 3)]
            block = block.reshape(9 * part_ch, half_y)
            total = total + jnp.dot(u_ref[dz], block, preferred_element_type=jnp.float32)
            gu_ref[dz] += lax.dot_general(
                block, crow, (((1,), (1,)), ((), ())), preferred_element_type=jnp.float32
            )
        gc_ref[iz, ix] = total
        return carry

    lax.fori_loop(0, coarse_z * coarse_x, body, 0)
    gu_ref[...] = gu_ref[...] * scale


def local(coarse, saved_pre, out_grad, up_weight, refine_weight):
    part_ch = saved_pre.shape[0]
    planes_z = saved_pre.shape[1]
    planes_x = saved_pre.shape[2]
    cells_y = saved_pre.shape[3]
    all_ch = part_ch * lax.axis_size("ch")
    channel_start = lax.axis_index("ch") * part_ch

    rows = out_grad.reshape(part_ch, planes_z, planes_x // 2, 2, cells_y)
    rows = jnp.transpose(rows, (1, 3, 2, 0, 4))
    count = lax.axis_size(("gz", "sec"))
    forward = [(i, (i + 1) % count) for i in range(count)]
    backward = [(target, source) for source, target in forward]
    swap = [(i, i ^ 1) for i in range(lax.axis_size("ch"))]
    def laid_out(block):
        block = block.reshape(part_ch, block.shape[1], planes_x // 2, 2, cells_y)
        return jnp.transpose(block, (1, 3, 2, 0, 4))

    low_raw = lax.ppermute(out_grad[:, planes_z - 2 :], ("gz", "sec"), forward)
    high_raw = lax.ppermute(out_grad[:, :2], ("gz", "sec"), backward)
    halos = laid_out(jnp.concatenate([low_raw, high_raw], axis=1))
    rows_other = lax.ppermute(rows, "ch", swap)
    halos_other = lax.ppermute(halos, "ch", swap)
    halo_z = halos.shape[0] + planes_z
    pre_rows = jnp.transpose(saved_pre, (1, 2, 0, 3))

    refine_cols = lax.dynamic_slice_in_dim(refine_weight, channel_start, part_ch, 2)
    refine_w = refine_cols.reshape(3, 3, 3, all_ch, part_ch)[::-1, ::-1]
    refine_w = jnp.transpose(refine_w, (2, 4, 0, 1, 3)).reshape(3 * part_ch, 9 * all_ch)

    fine_total = planes_z * lax.axis_size("gz") * lax.axis_size("sec") * planes_x * cells_y
    coarse_total = fine_total // 8

    def fine_rows(z_lo, z_hi, *start):
        scale = float(fine_total) ** (-0.5) if start else 1.0
        return pl.pallas_call(
            functools.partial(fine_kernel, z_lo, z_hi, scale),
            out_shape=(
                jax.ShapeDtypeStruct((z_hi - z_lo, planes_x, part_ch, cells_y), jnp.bfloat16),
                jax.ShapeDtypeStruct((9 * all_ch, 3 * part_ch), jnp.float32),
            )
            + ((jax.ShapeDtypeStruct((27, all_ch, part_ch), jnp.float32),) if start else ()),
            in_specs=[pl.BlockSpec(memory_space=pl.ANY)] * 4 + vmem_specs(2 + len(start)),
            out_specs=tuple(vmem_specs(2 + len(start))),
            scratch_shapes=[
                pltpu.VMEM(
                    (2, halo_z // 2, 2, planes_x // 2 + 2, all_ch, cells_y), jnp.bfloat16
                ),
                pltpu.SemaphoreType.DMA((4 * halo_z,)),
            ],
        )(halos, rows, halos_other, rows_other, pre_rows, refine_w, *start)

    grad_last, refine_last = fine_rows(planes_z - 1, planes_z)
    last_rows = grad_last.reshape(1, planes_x * part_ch, cells_y)
    below_z = passed_along(last_rows, ("gz", "sec"), 1)
    grad_main, _, refine_terms = fine_rows(0, planes_z - 1, refine_last)
    grad_rows = grad_main.reshape(planes_z - 1, planes_x * part_ch, cells_y)

    coarse_own = jnp.transpose(coarse, (1, 2, 0, 3))
    coarse_other = lax.ppermute(coarse_own, "ch", swap)
    own_k = coarse.shape[0]
    coarse_start = lax.axis_index("ch") * own_k
    coarse_in = 2 * own_k
    coarse_z, coarse_x, cells_yc = coarse.shape[1], coarse.shape[2], coarse.shape[3]
    up_rows = lax.dynamic_slice_in_dim(up_weight, channel_start, part_ch, 1)
    up_w = jnp.transpose(up_rows.reshape(3, 9, part_ch, coarse_in), (0, 3, 1, 2))
    up_w = up_w.reshape(3, coarse_in, 9 * part_ch)

    coarse_acc, up_acc = pl.pallas_call(
        functools.partial(coarse_kernel, float(coarse_total) ** (-0.5)),
        out_shape=(
            jax.ShapeDtypeStruct((coarse_z, coarse_x, coarse_in, cells_yc), jnp.float32),
            jax.ShapeDtypeStruct((3, 9 * part_ch, coarse_in), jnp.float32),
        ),
        in_specs=vmem_specs(6),
        out_specs=tuple(vmem_specs(2)),
        scratch_shapes=[
            pltpu.VMEM((planes_z + 1, planes_x + 1, 3, part_ch, cells_yc), jnp.bfloat16)
        ],
    )(grad_rows, last_rows, below_z, coarse_own, coarse_other, up_w)
    up_terms = up_acc.reshape(27, part_ch, coarse_in)
    other_start = own_k - coarse_start
    received = lax.ppermute(lax.dynamic_slice_in_dim(coarse_acc, other_start, own_k, 2), "ch", swap)
    coarse_summed = lax.dynamic_slice_in_dim(coarse_acc, coarse_start, own_k, 2) + received
    grad_coarse = jnp.transpose(coarse_summed, (2, 0, 1, 3)).astype(jnp.bfloat16)
    flat = jnp.concatenate([up_terms.reshape(-1), refine_terms.reshape(-1)])
    flat = summed_over_slabs(flat, ("gz", "sec"))
    grad_up = flat[: up_terms.size].reshape(up_terms.shape)
    grad_refine = flat[up_terms.size :].reshape(refine_terms.shape)
    return (grad_coarse, grad_up, grad_refine)


def solution(mesh):
    placed = (
        P("ch", ("groups", "gz", "sec"), None, None),
        P("ch", ("groups", "gz", "sec"), None, None),
        P("ch", ("groups", "gz", "sec"), None, None),
        P(),
        P(),
    )
    return jax.shard_map(
        local,
        mesh=mesh,
        in_specs=placed,
        out_specs=(
            P("ch", ("groups", "gz", "sec"), None, None),
            P("groups", "ch", None),
            P("groups", None, "ch"),
        ),
        check_vma=False,
    )
```

```python
import functools

import jax
import jax.numpy as jnp
from jax import lax
from jax.experimental import pallas as pl
from jax.experimental.pallas import tpu as pltpu
from jax.sharding import PartitionSpec as P

leak_slope = 0.2


def padded(block, sides, width):
    for axis, dim in sides:
        count = lax.axis_size(axis)
        forward = [(i, i + 1) for i in range(count - 1)]
        forward.append((count - 1, 0))
        backward = [(target, source) for source, target in forward]
        low = lax.ppermute(
            lax.slice_in_dim(block, block.shape[dim] - width, None, axis=dim), axis, forward
        )
        high = lax.ppermute(lax.slice_in_dim(block, 0, width, axis=dim), axis, backward)
        block = jnp.concatenate([low, block, high], axis=dim)
    return block


def passed_along(block, axis, distance):
    devices = range(lax.axis_size(axis))
    route = [((i - distance) % len(devices), i) for i in devices]
    return lax.ppermute(block, axis, route)


def summed_over_slabs(block, axis):
    count = lax.axis_size(axis)
    if count & (count - 1):
        return lax.psum(block, axis)
    step = 1
    while step < count:
        route = [(i, i ^ step) for i in range(count)]
        block = block + lax.ppermute(block, axis, route)
        step *= 2
    return block


def summed_into(block, axis, shapes):
    count = lax.axis_size(axis)
    if count & (count - 1) or count < 2:
        block = summed_over_slabs(block, axis)
        other = jnp.zeros_like(block)
    else:
        step = 1
        while step < count // 2:
            route = [(i, i ^ step) for i in range(count)]
            block = block + lax.ppermute(block, axis, route)
            step *= 2
        other = lax.ppermute(block, axis, [(i, i ^ step) for i in range(count)])
    parts, at = [], 0
    for shape in shapes:
        size = 1
        for extent in shape:
            size *= extent
        parts.append(block[at : at + size].reshape(shape) + other[at : at + size].reshape(shape))
        at += size
    return parts


def vmem_specs(count):
    return [pl.BlockSpec(memory_space=pltpu.VMEM)] * count


def fine_kernel(z_lo, z_hi, scale, *refs):
    pieces = refs[:4]
    if len(refs) == 12:
        sp_ref, w_ref, start_ref, gp_ref, r_ref, final_ref, g_ref, sems = refs[4:]
    else:
        sp_ref, w_ref, gp_ref, r_ref, g_ref, sems = refs[4:]
        start_ref = final_ref = None
    planes_z, planes_x, part_ch, cells_y = sp_ref.shape
    wide = g_ref.shape[4]
    low_count = pieces[0].shape[0] // 2
    core = lax.axis_index("ch")
    needed = sorted({z + 4 - 2 * dz for z in range(z_lo, z_hi) for dz in range(3)})
    edge = jnp.zeros(g_ref[:, :, :, 0].shape, g_ref.dtype)
    g_ref[:, :, :, 0] = edge
    g_ref[:, :, :, planes_x // 2 + 1] = edge
    copies = []
    for plane in needed:
        if plane < low_count:
            part, at = 0, plane
        elif plane < low_count + planes_z:
            part, at = 1, plane - low_count
        else:
            part, at = 0, plane - planes_z
        for half in range(2):
            for parity in range(2):
                copy = pltpu.make_async_copy(
                    pieces[2 * half + part].at[at, parity],
                    g_ref.at[
                        plane % 2,
                        plane // 2,
                        parity,
                        pl.ds(1, planes_x // 2),
                        pl.ds(pl.multiple_of(((half + core) % 2) * part_ch, part_ch), part_ch),
                    ],
                    sems.at[len(copies)],
                )
                copy.start()
                copies.append(copy)
    if start_ref is None:
        r_ref[...] = jnp.zeros(r_ref.shape, r_ref.dtype)
    else:
        r_ref[...] = start_ref[...]
    for copy in copies:
        copy.wait()

    def body(step, carry):
        z = z_lo + step // planes_x
        x = step % planes_x
        pre_act = sp_ref[z, x].astype(jnp.float32)
        slopes = jnp.where(pre_act > 0, 1.0, leak_slope).astype(jnp.float32)
        hidden = (pre_act * slopes).astype(jnp.bfloat16).astype(jnp.float32)
        rolled = jnp.concatenate(
            [pltpu.roll(hidden, 2, 1), hidden, pltpu.roll(hidden, cells_y - 2, 1)], axis=0
        ).astype(jnp.bfloat16)
        block = g_ref[z % 2, pl.ds(z // 2, 3), x % 2, pl.ds(x // 2, 3)]
        block = block.reshape(9 * wide, cells_y)
        total = jnp.dot(w_ref[...], block, preferred_element_type=jnp.float32)
        r_ref[...] += lax.dot_general(
            block, rolled, (((1,), (1,)), ((), ())), preferred_element_type=jnp.float32
        )
        grad_hidden = (
            pltpu.roll(total[:part_ch], cells_y - 2, 1)
            + total[part_ch : 2 * part_ch]
            + pltpu.roll(total[2 * part_ch :], 2, 1)
        )
        gp_ref[z - z_lo, x] = (grad_hidden * slopes).astype(gp_ref.dtype)
        return carry

    lax.fori_loop(0, (z_hi - z_lo) * planes_x, body, 0)
    if final_ref is not None:
        acc = r_ref[...] * scale
        for dz in range(3):
            for dx in range(3):
                rows_at = (3 * (2 - dz) + (2 - dx)) * wide
                for dy in range(3):
                    final_ref[9 * dz + 3 * dx + dy] = acc[
                        rows_at : rows_at + wide, dy * part_ch : (dy + 1) * part_ch
                    ]


def coarse_kernel(scale, gp_ref, last_ref, below_ref, own_ref, other_ref, u_ref, gc_ref, gu_ref, y_ref):
    planes_z = gp_ref.shape[0] + 1
    cells_y = gp_ref.shape[2]
    rows_x = y_ref.shape[1] - 1
    part_ch = y_ref.shape[3]
    half_y = y_ref.shape[4]
    coarse_z, coarse_x = own_ref.shape[0], own_ref.shape[1]
    first = lax.axis_index("ch") == 0
    at_y = lax.broadcasted_iota(jnp.int32, (cells_y, 3 * half_y), 0)
    col = lax.broadcasted_iota(jnp.int32, (cells_y, 3 * half_y), 1)
    target = 2 * (col % half_y) + col // half_y - 1
    target = jnp.where(target < 0, target + cells_y, target)
    pick = (at_y == target).astype(jnp.bfloat16)
    y_ref[:, 0] = jnp.zeros(y_ref[:, 0].shape, y_ref.dtype)
    for zg in range(planes_z + 1):
        if zg == 0:
            source = below_ref[0]
        elif zg == planes_z:
            source = last_ref[0]
        else:
            source = gp_ref[zg - 1]
        picked = jnp.dot(source, pick, preferred_element_type=jnp.float32).astype(y_ref.dtype)
        for dy in range(3):
            part = picked[:, dy * half_y : (dy + 1) * half_y]
            y_ref[zg, 1:, dy] = part.reshape(rows_x, part_ch, half_y)
    gu_ref[...] = jnp.zeros(gu_ref.shape, gu_ref.dtype)

    def body(step, carry):
        iz = step // coarse_x
        ix = step % coarse_x
        own = own_ref[iz, ix]
        other = other_ref[iz, ix]
        crow = jnp.concatenate(
            [jnp.where(first, own, other), jnp.where(first, other, own)], axis=0
        )
        total = jnp.zeros(gc_ref.shape[2:], jnp.float32)
        for dz in range(3):
            block = y_ref[2 * iz + dz, pl.ds(2 * ix, 3)]
            block = block.reshape(9 * part_ch, half_y)
            total = total + jnp.dot(u_ref[dz], block, preferred_element_type=jnp.float32)
            gu_ref[dz] += lax.dot_general(
                block, crow, (((1,), (1,)), ((), ())), preferred_element_type=jnp.float32
            )
        gc_ref[iz, ix] = total
        return carry

    lax.fori_loop(0, coarse_z * coarse_x, body, 0)
    gu_ref[...] = gu_ref[...] * scale


def local(coarse, saved_pre, out_grad, up_weight, refine_weight):
    part_ch = saved_pre.shape[0]
    planes_z = saved_pre.shape[1]
    planes_x = saved_pre.shape[2]
    cells_y = saved_pre.shape[3]
    all_ch = part_ch * lax.axis_size("ch")
    channel_start = lax.axis_index("ch") * part_ch

    rows = out_grad.reshape(part_ch, planes_z, planes_x // 2, 2, cells_y)
    rows = jnp.transpose(rows, (1, 3, 2, 0, 4))
    count = lax.axis_size(("gz", "sec"))
    forward = [(i, (i + 1) % count) for i in range(count)]
    backward = [(target, source) for source, target in forward]
    swap = [(i, i ^ 1) for i in range(lax.axis_size("ch"))]
    def laid_out(block):
        block = block.reshape(part_ch, block.shape[1], planes_x // 2, 2, cells_y)
        return jnp.transpose(block, (1, 3, 2, 0, 4))

    low_raw = lax.ppermute(out_grad[:, planes_z - 2 :], ("gz", "sec"), forward)
    high_raw = lax.ppermute(out_grad[:, :2], ("gz", "sec"), backward)
    halos = laid_out(jnp.concatenate([low_raw, high_raw], axis=1))
    rows_other = lax.ppermute(rows, "ch", swap)
    halos_other = lax.ppermute(halos, "ch", swap)
    halo_z = halos.shape[0] + planes_z
    pre_rows = jnp.transpose(saved_pre, (1, 2, 0, 3))

    refine_cols = lax.dynamic_slice_in_dim(refine_weight, channel_start, part_ch, 2)
    refine_w = refine_cols.reshape(3, 3, 3, all_ch, part_ch)[::-1, ::-1]
    refine_w = jnp.transpose(refine_w, (2, 4, 0, 1, 3)).reshape(3 * part_ch, 9 * all_ch)

    fine_total = planes_z * lax.axis_size("gz") * lax.axis_size("sec") * planes_x * cells_y
    coarse_total = fine_total // 8

    def fine_rows(z_lo, z_hi, *start):
        scale = float(fine_total) ** (-0.5) if start else 1.0
        return pl.pallas_call(
            functools.partial(fine_kernel, z_lo, z_hi, scale),
            out_shape=(
                jax.ShapeDtypeStruct((z_hi - z_lo, planes_x, part_ch, cells_y), jnp.bfloat16),
                jax.ShapeDtypeStruct((9 * all_ch, 3 * part_ch), jnp.float32),
            )
            + ((jax.ShapeDtypeStruct((27, all_ch, part_ch), jnp.float32),) if start else ()),
            in_specs=[pl.BlockSpec(memory_space=pl.ANY)] * 4 + vmem_specs(2 + len(start)),
            out_specs=tuple(vmem_specs(2 + len(start))),
            scratch_shapes=[
                pltpu.VMEM(
                    (2, halo_z // 2, 2, planes_x // 2 + 2, all_ch, cells_y), jnp.bfloat16
                ),
                pltpu.SemaphoreType.DMA((4 * halo_z,)),
            ],
        )(halos, rows, halos_other, rows_other, pre_rows, refine_w, *start)

    grad_last, refine_last = fine_rows(planes_z - 1, planes_z)
    last_rows = grad_last.reshape(1, planes_x * part_ch, cells_y)
    below_z = passed_along(last_rows, ("gz", "sec"), 1)
    grad_main, _, refine_terms = fine_rows(0, planes_z - 1, refine_last)
    grad_rows = grad_main.reshape(planes_z - 1, planes_x * part_ch, cells_y)

    coarse_own = jnp.transpose(coarse, (1, 2, 0, 3))
    coarse_other = lax.ppermute(coarse_own, "ch", swap)
    own_k = coarse.shape[0]
    coarse_start = lax.axis_index("ch") * own_k
    coarse_in = 2 * own_k
    coarse_z, coarse_x, cells_yc = coarse.shape[1], coarse.shape[2], coarse.shape[3]
    up_rows = lax.dynamic_slice_in_dim(up_weight, channel_start, part_ch, 1)
    up_w = jnp.transpose(up_rows.reshape(3, 9, part_ch, coarse_in), (0, 3, 1, 2))
    up_w = up_w.reshape(3, coarse_in, 9 * part_ch)

    coarse_acc, up_acc = pl.pallas_call(
        functools.partial(coarse_kernel, float(coarse_total) ** (-0.5)),
        out_shape=(
            jax.ShapeDtypeStruct((coarse_z, coarse_x, coarse_in, cells_yc), jnp.float32),
            jax.ShapeDtypeStruct((3, 9 * part_ch, coarse_in), jnp.float32),
        ),
        in_specs=vmem_specs(6),
        out_specs=tuple(vmem_specs(2)),
        scratch_shapes=[
            pltpu.VMEM((planes_z + 1, planes_x + 1, 3, part_ch, cells_yc), jnp.bfloat16)
        ],
    )(grad_rows, last_rows, below_z, coarse_own, coarse_other, up_w)
    up_terms = up_acc.reshape(27, part_ch, coarse_in)
    other_start = own_k - coarse_start
    received = lax.ppermute(lax.dynamic_slice_in_dim(coarse_acc, other_start, own_k, 2), "ch", swap)
    coarse_summed = lax.dynamic_slice_in_dim(coarse_acc, coarse_start, own_k, 2) + received
    grad_coarse = jnp.transpose(coarse_summed, (2, 0, 1, 3)).astype(jnp.bfloat16)
    flat = jnp.concatenate([up_terms.reshape(-1), refine_terms.reshape(-1)])
    grad_up, grad_refine = summed_into(flat, ("gz", "sec"), (up_terms.shape, refine_terms.shape))
    return (grad_coarse, grad_up, grad_refine)


def solution(mesh):
    placed = (
        P("ch", ("groups", "gz", "sec"), None, None),
        P("ch", ("groups", "gz", "sec"), None, None),
        P("ch", ("groups", "gz", "sec"), None, None),
        P(),
        P(),
    )
    return jax.shard_map(
        local,
        mesh=mesh,
        in_specs=placed,
        out_specs=(
            P("ch", ("groups", "gz", "sec"), None, None),
            P("groups", "ch", None),
            P("groups", None, "ch"),
        ),
        check_vma=False,
    )
```

```python
import functools

import jax
import jax.numpy as jnp
from jax import lax
from jax.experimental import pallas as pl
from jax.experimental.pallas import tpu as pltpu
from jax.sharding import PartitionSpec as P

leak_slope = 0.2


def padded(block, sides, width):
    for axis, dim in sides:
        count = lax.axis_size(axis)
        forward = [(i, i + 1) for i in range(count - 1)]
        forward.append((count - 1, 0))
        backward = [(target, source) for source, target in forward]
        low = lax.ppermute(
            lax.slice_in_dim(block, block.shape[dim] - width, None, axis=dim), axis, forward
        )
        high = lax.ppermute(lax.slice_in_dim(block, 0, width, axis=dim), axis, backward)
        block = jnp.concatenate([low, block, high], axis=dim)
    return block


def passed_along(block, axis, distance):
    devices = range(lax.axis_size(axis))
    route = [((i - distance) % len(devices), i) for i in devices]
    return lax.ppermute(block, axis, route)


def summed_over_slabs(block, axis):
    count = lax.axis_size(axis)
    if count & (count - 1):
        return lax.psum(block, axis)
    step = 1
    while step < count:
        route = [(i, i ^ step) for i in range(count)]
        block = block + lax.ppermute(block, axis, route)
        step *= 2
    return block


def summed_into(block, axis, shapes):
    count = lax.axis_size(axis)
    if count & (count - 1) or count < 2:
        block = summed_over_slabs(block, axis)
        other = jnp.zeros_like(block)
    else:
        step = count // 2
        while step > 1:
            route = [(i, i ^ step) for i in range(count)]
            block = block + lax.ppermute(block, axis, route)
            step //= 2
        other = lax.ppermute(block, axis, [(i, i ^ step) for i in range(count)])
    parts, at = [], 0
    for shape in shapes:
        size = 1
        for extent in shape:
            size *= extent
        parts.append(block[at : at + size].reshape(shape) + other[at : at + size].reshape(shape))
        at += size
    return parts


def vmem_specs(count):
    return [pl.BlockSpec(memory_space=pltpu.VMEM)] * count


def fine_kernel(z_lo, z_hi, scale, *refs):
    pieces = refs[:4]
    if len(refs) == 12:
        sp_ref, w_ref, start_ref, gp_ref, r_ref, final_ref, g_ref, sems = refs[4:]
    else:
        sp_ref, w_ref, gp_ref, r_ref, g_ref, sems = refs[4:]
        start_ref = final_ref = None
    planes_z, planes_x, part_ch, cells_y = sp_ref.shape
    wide = g_ref.shape[4]
    low_count = pieces[0].shape[0] // 2
    core = lax.axis_index("ch")
    needed = sorted({z + 4 - 2 * dz for z in range(z_lo, z_hi) for dz in range(3)})
    edge = jnp.zeros(g_ref[:, :, :, 0].shape, g_ref.dtype)
    g_ref[:, :, :, 0] = edge
    g_ref[:, :, :, planes_x // 2 + 1] = edge
    copies = []
    for plane in needed:
        if plane < low_count:
            part, at = 0, plane
        elif plane < low_count + planes_z:
            part, at = 1, plane - low_count
        else:
            part, at = 0, plane - planes_z
        for half in range(2):
            for parity in range(2):
                copy = pltpu.make_async_copy(
                    pieces[2 * half + part].at[at, parity],
                    g_ref.at[
                        plane % 2,
                        plane // 2,
                        parity,
                        pl.ds(1, planes_x // 2),
                        pl.ds(pl.multiple_of(((half + core) % 2) * part_ch, part_ch), part_ch),
                    ],
                    sems.at[len(copies)],
                )
                copy.start()
                copies.append(copy)
    if start_ref is None:
        r_ref[...] = jnp.zeros(r_ref.shape, r_ref.dtype)
    else:
        r_ref[...] = start_ref[...]
    for copy in copies:
        copy.wait()

    def body(step, carry):
        z = z_lo + step // planes_x
        x = step % planes_x
        pre_act = sp_ref[z, x].astype(jnp.float32)
        slopes = jnp.where(pre_act > 0, 1.0, leak_slope).astype(jnp.float32)
        hidden = (pre_act * slopes).astype(jnp.bfloat16).astype(jnp.float32)
        rolled = jnp.concatenate(
            [pltpu.roll(hidden, 2, 1), hidden, pltpu.roll(hidden, cells_y - 2, 1)], axis=0
        ).astype(jnp.bfloat16)
        block = g_ref[z % 2, pl.ds(z // 2, 3), x % 2, pl.ds(x // 2, 3)]
        block = block.reshape(9 * wide, cells_y)
        total = jnp.dot(w_ref[...], block, preferred_element_type=jnp.float32)
        r_ref[...] += lax.dot_general(
            block, rolled, (((1,), (1,)), ((), ())), preferred_element_type=jnp.float32
        )
        grad_hidden = (
            pltpu.roll(total[:part_ch], cells_y - 2, 1)
            + total[part_ch : 2 * part_ch]
            + pltpu.roll(total[2 * part_ch :], 2, 1)
        )
        gp_ref[z - z_lo, x] = (grad_hidden * slopes).astype(gp_ref.dtype)
        return carry

    lax.fori_loop(0, (z_hi - z_lo) * planes_x, body, 0)
    if final_ref is not None:
        acc = r_ref[...] * scale
        for dz in range(3):
            for dx in range(3):
                rows_at = (3 * (2 - dz) + (2 - dx)) * wide
                for dy in range(3):
                    final_ref[9 * dz + 3 * dx + dy] = acc[
                        rows_at : rows_at + wide, dy * part_ch : (dy + 1) * part_ch
                    ]


def coarse_kernel(scale, gp_ref, last_ref, below_ref, own_ref, other_ref, u_ref, gc_ref, gu_ref, y_ref):
    planes_z = gp_ref.shape[0] + 1
    cells_y = gp_ref.shape[2]
    rows_x = y_ref.shape[1] - 1
    part_ch = y_ref.shape[3]
    half_y = y_ref.shape[4]
    coarse_z, coarse_x = own_ref.shape[0], own_ref.shape[1]
    first = lax.axis_index("ch") == 0
    at_y = lax.broadcasted_iota(jnp.int32, (cells_y, 3 * half_y), 0)
    col = lax.broadcasted_iota(jnp.int32, (cells_y, 3 * half_y), 1)
    target = 2 * (col % half_y) + col // half_y - 1
    target = jnp.where(target < 0, target + cells_y, target)
    pick = (at_y == target).astype(jnp.bfloat16)
    y_ref[:, 0] = jnp.zeros(y_ref[:, 0].shape, y_ref.dtype)
    for zg in range(planes_z + 1):
        if zg == 0:
            source = below_ref[0]
        elif zg == planes_z:
            source = last_ref[0]
        else:
            source = gp_ref[zg - 1]
        picked = jnp.dot(source, pick, preferred_element_type=jnp.float32).astype(y_ref.dtype)
        for dy in range(3):
            part = picked[:, dy * half_y : (dy + 1) * half_y]
            y_ref[zg, 1:, dy] = part.reshape(rows_x, part_ch, half_y)
    gu_ref[...] = jnp.zeros(gu_ref.shape, gu_ref.dtype)

    def body(step, carry):
        iz = step // coarse_x
        ix = step % coarse_x
        own = own_ref[iz, ix]
        other = other_ref[iz, ix]
        crow = jnp.concatenate(
            [jnp.where(first, own, other), jnp.where(first, other, own)], axis=0
        )
        total = jnp.zeros(gc_ref.shape[2:], jnp.float32)
        for dz in range(3):
            block = y_ref[2 * iz + dz, pl.ds(2 * ix, 3)]
            block = block.reshape(9 * part_ch, half_y)
            total = total + jnp.dot(u_ref[dz], block, preferred_element_type=jnp.float32)
            gu_ref[dz] += lax.dot_general(
                block, crow, (((1,), (1,)), ((), ())), preferred_element_type=jnp.float32
            )
        gc_ref[iz, ix] = total
        return carry

    lax.fori_loop(0, coarse_z * coarse_x, body, 0)
    gu_ref[...] = gu_ref[...] * scale


def local(coarse, saved_pre, out_grad, up_weight, refine_weight):
    part_ch = saved_pre.shape[0]
    planes_z = saved_pre.shape[1]
    planes_x = saved_pre.shape[2]
    cells_y = saved_pre.shape[3]
    all_ch = part_ch * lax.axis_size("ch")
    channel_start = lax.axis_index("ch") * part_ch

    rows = out_grad.reshape(part_ch, planes_z, planes_x // 2, 2, cells_y)
    rows = jnp.transpose(rows, (1, 3, 2, 0, 4))
    count = lax.axis_size(("gz", "sec"))
    forward = [(i, (i + 1) % count) for i in range(count)]
    backward = [(target, source) for source, target in forward]
    swap = [(i, i ^ 1) for i in range(lax.axis_size("ch"))]
    def laid_out(block):
        block = block.reshape(part_ch, block.shape[1], planes_x // 2, 2, cells_y)
        return jnp.transpose(block, (1, 3, 2, 0, 4))

    low_raw = lax.ppermute(out_grad[:, planes_z - 2 :], ("gz", "sec"), forward)
    high_raw = lax.ppermute(out_grad[:, :2], ("gz", "sec"), backward)
    halos = laid_out(jnp.concatenate([low_raw, high_raw], axis=1))
    rows_other = lax.ppermute(rows, "ch", swap)
    halos_other = lax.ppermute(halos, "ch", swap)
    halo_z = halos.shape[0] + planes_z
    pre_rows = jnp.transpose(saved_pre, (1, 2, 0, 3))

    refine_cols = lax.dynamic_slice_in_dim(refine_weight, channel_start, part_ch, 2)
    refine_w = refine_cols.reshape(3, 3, 3, all_ch, part_ch)[::-1, ::-1]
    refine_w = jnp.transpose(refine_w, (2, 4, 0, 1, 3)).reshape(3 * part_ch, 9 * all_ch)

    fine_total = planes_z * lax.axis_size("gz") * lax.axis_size("sec") * planes_x * cells_y
    coarse_total = fine_total // 8

    def fine_rows(z_lo, z_hi, *start):
        scale = float(fine_total) ** (-0.5) if start else 1.0
        return pl.pallas_call(
            functools.partial(fine_kernel, z_lo, z_hi, scale),
            out_shape=(
                jax.ShapeDtypeStruct((z_hi - z_lo, planes_x, part_ch, cells_y), jnp.bfloat16),
                jax.ShapeDtypeStruct((9 * all_ch, 3 * part_ch), jnp.float32),
            )
            + ((jax.ShapeDtypeStruct((27, all_ch, part_ch), jnp.float32),) if start else ()),
            in_specs=[pl.BlockSpec(memory_space=pl.ANY)] * 4 + vmem_specs(2 + len(start)),
            out_specs=tuple(vmem_specs(2 + len(start))),
            scratch_shapes=[
                pltpu.VMEM(
                    (2, halo_z // 2, 2, planes_x // 2 + 2, all_ch, cells_y), jnp.bfloat16
                ),
                pltpu.SemaphoreType.DMA((4 * halo_z,)),
            ],
        )(halos, rows, halos_other, rows_other, pre_rows, refine_w, *start)

    grad_last, refine_last = fine_rows(planes_z - 1, planes_z)
    last_rows = grad_last.reshape(1, planes_x * part_ch, cells_y)
    below_z = passed_along(last_rows, ("gz", "sec"), 1)
    grad_main, _, refine_terms = fine_rows(0, planes_z - 1, refine_last)
    grad_rows = grad_main.reshape(planes_z - 1, planes_x * part_ch, cells_y)

    coarse_own = jnp.transpose(coarse, (1, 2, 0, 3))
    coarse_other = lax.ppermute(coarse_own, "ch", swap)
    own_k = coarse.shape[0]
    coarse_start = lax.axis_index("ch") * own_k
    coarse_in = 2 * own_k
    coarse_z, coarse_x, cells_yc = coarse.shape[1], coarse.shape[2], coarse.shape[3]
    up_rows = lax.dynamic_slice_in_dim(up_weight, channel_start, part_ch, 1)
    up_w = jnp.transpose(up_rows.reshape(3, 9, part_ch, coarse_in), (0, 3, 1, 2))
    up_w = up_w.reshape(3, coarse_in, 9 * part_ch)

    coarse_acc, up_acc = pl.pallas_call(
        functools.partial(coarse_kernel, float(coarse_total) ** (-0.5)),
        out_shape=(
            jax.ShapeDtypeStruct((coarse_z, coarse_x, coarse_in, cells_yc), jnp.float32),
            jax.ShapeDtypeStruct((3, 9 * part_ch, coarse_in), jnp.float32),
        ),
        in_specs=vmem_specs(6),
        out_specs=tuple(vmem_specs(2)),
        scratch_shapes=[
            pltpu.VMEM((planes_z + 1, planes_x + 1, 3, part_ch, cells_yc), jnp.bfloat16)
        ],
    )(grad_rows, last_rows, below_z, coarse_own, coarse_other, up_w)
    up_terms = up_acc.reshape(27, part_ch, coarse_in)
    other_start = own_k - coarse_start
    received = lax.ppermute(lax.dynamic_slice_in_dim(coarse_acc, other_start, own_k, 2), "ch", swap)
    coarse_summed = lax.dynamic_slice_in_dim(coarse_acc, coarse_start, own_k, 2) + received
    grad_coarse = jnp.transpose(coarse_summed, (2, 0, 1, 3)).astype(jnp.bfloat16)
    flat = jnp.concatenate([up_terms.reshape(-1), refine_terms.reshape(-1)])
    grad_up, grad_refine = summed_into(flat, ("gz", "sec"), (up_terms.shape, refine_terms.shape))
    return (grad_coarse, grad_up, grad_refine)


def solution(mesh):
    placed = (
        P("ch", ("groups", "gz", "sec"), None, None),
        P("ch", ("groups", "gz", "sec"), None, None),
        P("ch", ("groups", "gz", "sec"), None, None),
        P(),
        P(),
    )
    return jax.shard_map(
        local,
        mesh=mesh,
        in_specs=placed,
        out_specs=(
            P("ch", ("groups", "gz", "sec"), None, None),
            P("groups", "ch", None),
            P("groups", None, "ch"),
        ),
        check_vma=False,
    )
```

```python
import functools

import jax
import jax.numpy as jnp
from jax import lax
from jax.experimental import pallas as pl
from jax.experimental.pallas import tpu as pltpu
from jax.sharding import PartitionSpec as P

leak_slope = 0.2


def padded(block, sides, width):
    for axis, dim in sides:
        count = lax.axis_size(axis)
        forward = [(i, i + 1) for i in range(count - 1)]
        forward.append((count - 1, 0))
        backward = [(target, source) for source, target in forward]
        low = lax.ppermute(
            lax.slice_in_dim(block, block.shape[dim] - width, None, axis=dim), axis, forward
        )
        high = lax.ppermute(lax.slice_in_dim(block, 0, width, axis=dim), axis, backward)
        block = jnp.concatenate([low, block, high], axis=dim)
    return block


def passed_along(block, axis, distance):
    devices = range(lax.axis_size(axis))
    route = [((i - distance) % len(devices), i) for i in devices]
    return lax.ppermute(block, axis, route)


def summed_over_slabs(block, axis):
    count = lax.axis_size(axis)
    if count & (count - 1):
        return lax.psum(block, axis)
    step = 1
    while step < count:
        route = [(i, i ^ step) for i in range(count)]
        block = block + lax.ppermute(block, axis, route)
        step *= 2
    return block


def summed_into(block, axis, shapes):
    count = lax.axis_size(axis)
    if count & (count - 1) or count < 2:
        block = summed_over_slabs(block, axis)
        other = jnp.zeros_like(block)
    else:
        step = 1
        while step < count // 2:
            route = [(i, i ^ step) for i in range(count)]
            block = block + lax.ppermute(block, axis, route)
            step *= 2
        other = lax.ppermute(block, axis, [(i, i ^ step) for i in range(count)])
    parts, at = [], 0
    for shape in shapes:
        size = 1
        for extent in shape:
            size *= extent
        parts.append(block[at : at + size].reshape(shape) + other[at : at + size].reshape(shape))
        at += size
    return parts


def vmem_specs(count):
    return [pl.BlockSpec(memory_space=pltpu.VMEM)] * count


def fine_kernel(z_lo, z_hi, scale, *refs):
    pieces = refs[:4]
    if len(refs) == 12:
        sp_ref, w_ref, start_ref, gp_ref, r_ref, final_ref, g_ref, sems = refs[4:]
    else:
        sp_ref, w_ref, gp_ref, r_ref, g_ref, sems = refs[4:]
        start_ref = final_ref = None
    planes_z, planes_x, part_ch, cells_y = sp_ref.shape
    wide = g_ref.shape[4]
    low_count = pieces[0].shape[0] // 2
    core = lax.axis_index("ch")
    needed = sorted({z + 4 - 2 * dz for z in range(z_lo, z_hi) for dz in range(3)})
    edge = jnp.zeros(g_ref[:, :, :, 0].shape, g_ref.dtype)
    g_ref[:, :, :, 0] = edge
    g_ref[:, :, :, planes_x // 2 + 1] = edge
    copies = []
    for plane in needed:
        if plane < low_count:
            part, at = 0, plane
        elif plane < low_count + planes_z:
            part, at = 1, plane - low_count
        else:
            part, at = 0, plane - planes_z
        for half in range(2):
            for parity in range(2):
                copy = pltpu.make_async_copy(
                    pieces[2 * half + part].at[at, parity],
                    g_ref.at[
                        plane % 2,
                        plane // 2,
                        parity,
                        pl.ds(1, planes_x // 2),
                        pl.ds(pl.multiple_of(((half + core) % 2) * part_ch, part_ch), part_ch),
                    ],
                    sems.at[len(copies)],
                )
                copy.start()
                copies.append(copy)
    if start_ref is None:
        r_ref[...] = jnp.zeros(r_ref.shape, r_ref.dtype)
    else:
        r_ref[...] = start_ref[...]
    for copy in copies:
        copy.wait()

    def body(step, carry):
        z = z_lo + step // planes_x
        x = step % planes_x
        pre_act = sp_ref[z, x].astype(jnp.float32)
        slopes = jnp.where(pre_act > 0, 1.0, leak_slope).astype(jnp.float32)
        hidden = (pre_act * slopes).astype(jnp.bfloat16)
        rolled = jnp.concatenate(
            [pltpu.roll(hidden, 2, 1), hidden, pltpu.roll(hidden, cells_y - 2, 1)], axis=0
        )
        block = g_ref[z % 2, pl.ds(z // 2, 3), x % 2, pl.ds(x // 2, 3)]
        block = block.reshape(9 * wide, cells_y)
        total = jnp.dot(w_ref[...], block, preferred_element_type=jnp.float32)
        r_ref[...] += lax.dot_general(
            block, rolled, (((1,), (1,)), ((), ())), preferred_element_type=jnp.float32
        )
        grad_hidden = (
            pltpu.roll(total[:part_ch], cells_y - 2, 1)
            + total[part_ch : 2 * part_ch]
            + pltpu.roll(total[2 * part_ch :], 2, 1)
        )
        gp_ref[z - z_lo, x] = (grad_hidden * slopes).astype(gp_ref.dtype)
        return carry

    lax.fori_loop(0, (z_hi - z_lo) * planes_x, body, 0)
    if final_ref is not None:
        acc = r_ref[...] * scale
        for dz in range(3):
            for dx in range(3):
                rows_at = (3 * (2 - dz) + (2 - dx)) * wide
                for dy in range(3):
                    final_ref[9 * dz + 3 * dx + dy] = acc[
                        rows_at : rows_at + wide, dy * part_ch : (dy + 1) * part_ch
                    ]


def coarse_kernel(scale, gp_ref, last_ref, below_ref, own_ref, other_ref, u_ref, gc_ref, gu_ref, y_ref):
    planes_z = gp_ref.shape[0] + 1
    cells_y = gp_ref.shape[2]
    rows_x = y_ref.shape[1] - 1
    part_ch = y_ref.shape[3]
    half_y = y_ref.shape[4]
    coarse_z, coarse_x = own_ref.shape[0], own_ref.shape[1]
    first = lax.axis_index("ch") == 0
    at_y = lax.broadcasted_iota(jnp.int32, (cells_y, 3 * half_y), 0)
    col = lax.broadcasted_iota(jnp.int32, (cells_y, 3 * half_y), 1)
    target = 2 * (col % half_y) + col // half_y - 1
    target = jnp.where(target < 0, target + cells_y, target)
    pick = (at_y == target).astype(jnp.bfloat16)
    y_ref[:, 0] = jnp.zeros(y_ref[:, 0].shape, y_ref.dtype)
    for zg in range(planes_z + 1):
        if zg == 0:
            source = below_ref[0]
        elif zg == planes_z:
            source = last_ref[0]
        else:
            source = gp_ref[zg - 1]
        picked = jnp.dot(source, pick, preferred_element_type=jnp.float32).astype(y_ref.dtype)
        for dy in range(3):
            part = picked[:, dy * half_y : (dy + 1) * half_y]
            y_ref[zg, 1:, dy] = part.reshape(rows_x, part_ch, half_y)
    gu_ref[...] = jnp.zeros(gu_ref.shape, gu_ref.dtype)

    def body(step, carry):
        iz = step // coarse_x
        ix = step % coarse_x
        own = own_ref[iz, ix]
        other = other_ref[iz, ix]
        crow = jnp.concatenate(
            [jnp.where(first, own, other), jnp.where(first, other, own)], axis=0
        )
        total = jnp.zeros(gc_ref.shape[2:], jnp.float32)
        for dz in range(3):
            block = y_ref[2 * iz + dz, pl.ds(2 * ix, 3)]
            block = block.reshape(9 * part_ch, half_y)
            total = total + jnp.dot(u_ref[dz], block, preferred_element_type=jnp.float32)
            gu_ref[dz] += lax.dot_general(
                block, crow, (((1,), (1,)), ((), ())), preferred_element_type=jnp.float32
            )
        gc_ref[iz, ix] = total
        return carry

    lax.fori_loop(0, coarse_z * coarse_x, body, 0)
    gu_ref[...] = gu_ref[...] * scale


def local(coarse, saved_pre, out_grad, up_weight, refine_weight):
    part_ch = saved_pre.shape[0]
    planes_z = saved_pre.shape[1]
    planes_x = saved_pre.shape[2]
    cells_y = saved_pre.shape[3]
    all_ch = part_ch * lax.axis_size("ch")
    channel_start = lax.axis_index("ch") * part_ch

    rows = out_grad.reshape(part_ch, planes_z, planes_x // 2, 2, cells_y)
    rows = jnp.transpose(rows, (1, 3, 2, 0, 4))
    count = lax.axis_size(("gz", "sec"))
    forward = [(i, (i + 1) % count) for i in range(count)]
    backward = [(target, source) for source, target in forward]
    swap = [(i, i ^ 1) for i in range(lax.axis_size("ch"))]
    def laid_out(block):
        block = block.reshape(part_ch, block.shape[1], planes_x // 2, 2, cells_y)
        return jnp.transpose(block, (1, 3, 2, 0, 4))

    low_raw = lax.ppermute(out_grad[:, planes_z - 2 :], ("gz", "sec"), forward)
    high_raw = lax.ppermute(out_grad[:, :2], ("gz", "sec"), backward)
    halos = laid_out(jnp.concatenate([low_raw, high_raw], axis=1))
    rows_other = lax.ppermute(rows, "ch", swap)
    halos_other = lax.ppermute(halos, "ch", swap)
    halo_z = halos.shape[0] + planes_z
    pre_rows = jnp.transpose(saved_pre, (1, 2, 0, 3))

    refine_cols = lax.dynamic_slice_in_dim(refine_weight, channel_start, part_ch, 2)
    refine_w = refine_cols.reshape(3, 3, 3, all_ch, part_ch)[::-1, ::-1]
    refine_w = jnp.transpose(refine_w, (2, 4, 0, 1, 3)).reshape(3 * part_ch, 9 * all_ch)

    fine_total = planes_z * lax.axis_size("gz") * lax.axis_size("sec") * planes_x * cells_y
    coarse_total = fine_total // 8

    def fine_rows(z_lo, z_hi, *start):
        scale = float(fine_total) ** (-0.5) if start else 1.0
        return pl.pallas_call(
            functools.partial(fine_kernel, z_lo, z_hi, scale),
            out_shape=(
                jax.ShapeDtypeStruct((z_hi - z_lo, planes_x, part_ch, cells_y), jnp.bfloat16),
                jax.ShapeDtypeStruct((9 * all_ch, 3 * part_ch), jnp.float32),
            )
            + ((jax.ShapeDtypeStruct((27, all_ch, part_ch), jnp.float32),) if start else ()),
            in_specs=[pl.BlockSpec(memory_space=pl.ANY)] * 4 + vmem_specs(2 + len(start)),
            out_specs=tuple(vmem_specs(2 + len(start))),
            scratch_shapes=[
                pltpu.VMEM(
                    (2, halo_z // 2, 2, planes_x // 2 + 2, all_ch, cells_y), jnp.bfloat16
                ),
                pltpu.SemaphoreType.DMA((4 * halo_z,)),
            ],
        )(halos, rows, halos_other, rows_other, pre_rows, refine_w, *start)

    grad_last, refine_last = fine_rows(planes_z - 1, planes_z)
    last_rows = grad_last.reshape(1, planes_x * part_ch, cells_y)
    below_z = passed_along(last_rows, ("gz", "sec"), 1)
    grad_main, _, refine_terms = fine_rows(0, planes_z - 1, refine_last)
    grad_rows = grad_main.reshape(planes_z - 1, planes_x * part_ch, cells_y)

    coarse_own = jnp.transpose(coarse, (1, 2, 0, 3))
    coarse_other = lax.ppermute(coarse_own, "ch", swap)
    own_k = coarse.shape[0]
    coarse_start = lax.axis_index("ch") * own_k
    coarse_in = 2 * own_k
    coarse_z, coarse_x, cells_yc = coarse.shape[1], coarse.shape[2], coarse.shape[3]
    up_rows = lax.dynamic_slice_in_dim(up_weight, channel_start, part_ch, 1)
    up_w = jnp.transpose(up_rows.reshape(3, 9, part_ch, coarse_in), (0, 3, 1, 2))
    up_w = up_w.reshape(3, coarse_in, 9 * part_ch)

    coarse_acc, up_acc = pl.pallas_call(
        functools.partial(coarse_kernel, float(coarse_total) ** (-0.5)),
        out_shape=(
            jax.ShapeDtypeStruct((coarse_z, coarse_x, coarse_in, cells_yc), jnp.float32),
            jax.ShapeDtypeStruct((3, 9 * part_ch, coarse_in), jnp.float32),
        ),
        in_specs=vmem_specs(6),
        out_specs=tuple(vmem_specs(2)),
        scratch_shapes=[
            pltpu.VMEM((planes_z + 1, planes_x + 1, 3, part_ch, cells_yc), jnp.bfloat16)
        ],
    )(grad_rows, last_rows, below_z, coarse_own, coarse_other, up_w)
    up_terms = up_acc.reshape(27, part_ch, coarse_in)
    other_start = own_k - coarse_start
    received = lax.ppermute(lax.dynamic_slice_in_dim(coarse_acc, other_start, own_k, 2), "ch", swap)
    coarse_summed = lax.dynamic_slice_in_dim(coarse_acc, coarse_start, own_k, 2) + received
    grad_coarse = jnp.transpose(coarse_summed, (2, 0, 1, 3)).astype(jnp.bfloat16)
    flat = jnp.concatenate([up_terms.reshape(-1), refine_terms.reshape(-1)])
    grad_up, grad_refine = summed_into(flat, ("gz", "sec"), (up_terms.shape, refine_terms.shape))
    return (grad_coarse, grad_up, grad_refine)


def solution(mesh):
    placed = (
        P("ch", ("groups", "gz", "sec"), None, None),
        P("ch", ("groups", "gz", "sec"), None, None),
        P("ch", ("groups", "gz", "sec"), None, None),
        P(),
        P(),
    )
    return jax.shard_map(
        local,
        mesh=mesh,
        in_specs=placed,
        out_specs=(
            P("ch", ("groups", "gz", "sec"), None, None),
            P("groups", "ch", None),
            P("groups", None, "ch"),
        ),
        check_vma=False,
    )
```

```python
import functools

import jax
import jax.numpy as jnp
from jax import lax
from jax.experimental import pallas as pl
from jax.experimental.pallas import tpu as pltpu
from jax.sharding import PartitionSpec as P

leak_slope = 0.2


def padded(block, sides, width):
    for axis, dim in sides:
        count = lax.axis_size(axis)
        forward = [(i, i + 1) for i in range(count - 1)]
        forward.append((count - 1, 0))
        backward = [(target, source) for source, target in forward]
        low = lax.ppermute(
            lax.slice_in_dim(block, block.shape[dim] - width, None, axis=dim), axis, forward
        )
        high = lax.ppermute(lax.slice_in_dim(block, 0, width, axis=dim), axis, backward)
        block = jnp.concatenate([low, block, high], axis=dim)
    return block


def passed_along(block, axis, distance):
    devices = range(lax.axis_size(axis))
    route = [((i - distance) % len(devices), i) for i in devices]
    return lax.ppermute(block, axis, route)


def summed_over_slabs(block, axis):
    count = lax.axis_size(axis)
    if count & (count - 1):
        return lax.psum(block, axis)
    step = 1
    while step < count:
        route = [(i, i ^ step) for i in range(count)]
        block = block + lax.ppermute(block, axis, route)
        step *= 2
    return block


def summed_into(block, axis, shapes):
    count = lax.axis_size(axis)
    if count & (count - 1) or count < 2:
        block = summed_over_slabs(block, axis)
        other = jnp.zeros_like(block)
    else:
        step = 1
        while step < count // 2:
            route = [(i, i ^ step) for i in range(count)]
            block = block + lax.ppermute(block, axis, route)
            step *= 2
        other = lax.ppermute(block, axis, [(i, i ^ step) for i in range(count)])
    parts, at = [], 0
    for shape in shapes:
        size = 1
        for extent in shape:
            size *= extent
        parts.append(block[at : at + size].reshape(shape) + other[at : at + size].reshape(shape))
        at += size
    return parts


def vmem_specs(count):
    return [pl.BlockSpec(memory_space=pltpu.VMEM)] * count


def fine_kernel(z_lo, z_hi, scale, *refs):
    pieces = refs[:4]
    if len(refs) == 12:
        sp_ref, w_ref, start_ref, gp_ref, r_ref, final_ref, g_ref, sems = refs[4:]
    else:
        sp_ref, w_ref, gp_ref, r_ref, g_ref, sems = refs[4:]
        start_ref = final_ref = None
    planes_z, planes_x, part_ch, cells_y = sp_ref.shape
    wide = g_ref.shape[4]
    low_count = pieces[0].shape[0] // 2
    core = lax.axis_index("ch")
    needed = sorted({z + 4 - 2 * dz for z in range(z_lo, z_hi) for dz in range(3)})
    edge = jnp.zeros(g_ref[:, :, :, 0].shape, g_ref.dtype)
    g_ref[:, :, :, 0] = edge
    g_ref[:, :, :, planes_x // 2 + 1] = edge
    copies = []
    by_plane = {}
    for plane in needed:
        if plane < low_count:
            part, at = 0, plane
        elif plane < low_count + planes_z:
            part, at = 1, plane - low_count
        else:
            part, at = 0, plane - planes_z
        for half in range(2):
            for parity in range(2):
                copy = pltpu.make_async_copy(
                    pieces[2 * half + part].at[at, parity],
                    g_ref.at[
                        plane % 2,
                        plane // 2,
                        parity,
                        pl.ds(1, planes_x // 2),
                        pl.ds(pl.multiple_of(((half + core) % 2) * part_ch, part_ch), part_ch),
                    ],
                    sems.at[len(copies)],
                )
                copy.start()
                copies.append(copy)
                by_plane.setdefault(plane, []).append(copy)
    if start_ref is None:
        r_ref[...] = jnp.zeros(r_ref.shape, r_ref.dtype)
    else:
        r_ref[...] = start_ref[...]

    def body(step, carry):
        z = z_lo + step // planes_x
        x = step % planes_x
        pre_act = sp_ref[z, x].astype(jnp.float32)
        slopes = jnp.where(pre_act > 0, 1.0, leak_slope).astype(jnp.float32)
        hidden = (pre_act * slopes).astype(jnp.bfloat16).astype(jnp.float32)
        rolled = jnp.concatenate(
            [pltpu.roll(hidden, 2, 1), hidden, pltpu.roll(hidden, cells_y - 2, 1)], axis=0
        ).astype(jnp.bfloat16)
        block = g_ref[z % 2, pl.ds(z // 2, 3), x % 2, pl.ds(x // 2, 3)]
        block = block.reshape(9 * wide, cells_y)
        total = jnp.dot(w_ref[...], block, preferred_element_type=jnp.float32)
        r_ref[...] += lax.dot_general(
            block, rolled, (((1,), (1,)), ((), ())), preferred_element_type=jnp.float32
        )
        grad_hidden = (
            pltpu.roll(total[:part_ch], cells_y - 2, 1)
            + total[part_ch : 2 * part_ch]
            + pltpu.roll(total[2 * part_ch :], 2, 1)
        )
        gp_ref[z - z_lo, x] = (grad_hidden * slopes).astype(gp_ref.dtype)
        return carry

    for z in range(z_lo, z_hi):
        for plane in sorted({z + 4 - 2 * dz for dz in range(3)}):
            for copy in by_plane.pop(plane, []):
                copy.wait()
        lax.fori_loop((z - z_lo) * planes_x, (z - z_lo + 1) * planes_x, body, 0)
    if final_ref is not None:
        acc = r_ref[...] * scale
        for dz in range(3):
            for dx in range(3):
                rows_at = (3 * (2 - dz) + (2 - dx)) * wide
                for dy in range(3):
                    final_ref[9 * dz + 3 * dx + dy] = acc[
                        rows_at : rows_at + wide, dy * part_ch : (dy + 1) * part_ch
                    ]


def coarse_kernel(scale, gp_ref, last_ref, below_ref, own_ref, other_ref, u_ref, gc_ref, gu_ref, y_ref):
    planes_z = gp_ref.shape[0] + 1
    cells_y = gp_ref.shape[2]
    rows_x = y_ref.shape[1] - 1
    part_ch = y_ref.shape[3]
    half_y = y_ref.shape[4]
    coarse_z, coarse_x = own_ref.shape[0], own_ref.shape[1]
    first = lax.axis_index("ch") == 0
    at_y = lax.broadcasted_iota(jnp.int32, (cells_y, 3 * half_y), 0)
    col = lax.broadcasted_iota(jnp.int32, (cells_y, 3 * half_y), 1)
    target = 2 * (col % half_y) + col // half_y - 1
    target = jnp.where(target < 0, target + cells_y, target)
    pick = (at_y == target).astype(jnp.bfloat16)
    y_ref[:, 0] = jnp.zeros(y_ref[:, 0].shape, y_ref.dtype)
    for zg in range(planes_z + 1):
        if zg == 0:
            source = below_ref[0]
        elif zg == planes_z:
            source = last_ref[0]
        else:
            source = gp_ref[zg - 1]
        picked = jnp.dot(source, pick, preferred_element_type=jnp.float32).astype(y_ref.dtype)
        for dy in range(3):
            part = picked[:, dy * half_y : (dy + 1) * half_y]
            y_ref[zg, 1:, dy] = part.reshape(rows_x, part_ch, half_y)
    gu_ref[...] = jnp.zeros(gu_ref.shape, gu_ref.dtype)

    def body(step, carry):
        iz = step // coarse_x
        ix = step % coarse_x
        own = own_ref[iz, ix]
        other = other_ref[iz, ix]
        crow = jnp.concatenate(
            [jnp.where(first, own, other), jnp.where(first, other, own)], axis=0
        )
        total = jnp.zeros(gc_ref.shape[2:], jnp.float32)
        for dz in range(3):
            block = y_ref[2 * iz + dz, pl.ds(2 * ix, 3)]
            block = block.reshape(9 * part_ch, half_y)
            total = total + jnp.dot(u_ref[dz], block, preferred_element_type=jnp.float32)
            gu_ref[dz] += lax.dot_general(
                block, crow, (((1,), (1,)), ((), ())), preferred_element_type=jnp.float32
            )
        gc_ref[iz, ix] = total
        return carry

    lax.fori_loop(0, coarse_z * coarse_x, body, 0)
    gu_ref[...] = gu_ref[...] * scale


def local(coarse, saved_pre, out_grad, up_weight, refine_weight):
    part_ch = saved_pre.shape[0]
    planes_z = saved_pre.shape[1]
    planes_x = saved_pre.shape[2]
    cells_y = saved_pre.shape[3]
    all_ch = part_ch * lax.axis_size("ch")
    channel_start = lax.axis_index("ch") * part_ch

    rows = out_grad.reshape(part_ch, planes_z, planes_x // 2, 2, cells_y)
    rows = jnp.transpose(rows, (1, 3, 2, 0, 4))
    count = lax.axis_size(("gz", "sec"))
    forward = [(i, (i + 1) % count) for i in range(count)]
    backward = [(target, source) for source, target in forward]
    swap = [(i, i ^ 1) for i in range(lax.axis_size("ch"))]
    def laid_out(block):
        block = block.reshape(part_ch, block.shape[1], planes_x // 2, 2, cells_y)
        return jnp.transpose(block, (1, 3, 2, 0, 4))

    low_raw = lax.ppermute(out_grad[:, planes_z - 2 :], ("gz", "sec"), forward)
    high_raw = lax.ppermute(out_grad[:, :2], ("gz", "sec"), backward)
    halos = laid_out(jnp.concatenate([low_raw, high_raw], axis=1))
    rows_other = lax.ppermute(rows, "ch", swap)
    halos_other = lax.ppermute(halos, "ch", swap)
    halo_z = halos.shape[0] + planes_z
    pre_rows = jnp.transpose(saved_pre, (1, 2, 0, 3))

    refine_cols = lax.dynamic_slice_in_dim(refine_weight, channel_start, part_ch, 2)
    refine_w = refine_cols.reshape(3, 3, 3, all_ch, part_ch)[::-1, ::-1]
    refine_w = jnp.transpose(refine_w, (2, 4, 0, 1, 3)).reshape(3 * part_ch, 9 * all_ch)

    fine_total = planes_z * lax.axis_size("gz") * lax.axis_size("sec") * planes_x * cells_y
    coarse_total = fine_total // 8

    def fine_rows(z_lo, z_hi, *start):
        scale = float(fine_total) ** (-0.5) if start else 1.0
        return pl.pallas_call(
            functools.partial(fine_kernel, z_lo, z_hi, scale),
            out_shape=(
                jax.ShapeDtypeStruct((z_hi - z_lo, planes_x, part_ch, cells_y), jnp.bfloat16),
                jax.ShapeDtypeStruct((9 * all_ch, 3 * part_ch), jnp.float32),
            )
            + ((jax.ShapeDtypeStruct((27, all_ch, part_ch), jnp.float32),) if start else ()),
            in_specs=[pl.BlockSpec(memory_space=pl.ANY)] * 4 + vmem_specs(2 + len(start)),
            out_specs=tuple(vmem_specs(2 + len(start))),
            scratch_shapes=[
                pltpu.VMEM(
                    (2, halo_z // 2, 2, planes_x // 2 + 2, all_ch, cells_y), jnp.bfloat16
                ),
                pltpu.SemaphoreType.DMA((4 * halo_z,)),
            ],
        )(halos, rows, halos_other, rows_other, pre_rows, refine_w, *start)

    grad_last, refine_last = fine_rows(planes_z - 1, planes_z)
    last_rows = grad_last.reshape(1, planes_x * part_ch, cells_y)
    below_z = passed_along(last_rows, ("gz", "sec"), 1)
    grad_main, _, refine_terms = fine_rows(0, planes_z - 1, refine_last)
    grad_rows = grad_main.reshape(planes_z - 1, planes_x * part_ch, cells_y)

    coarse_own = jnp.transpose(coarse, (1, 2, 0, 3))
    coarse_other = lax.ppermute(coarse_own, "ch", swap)
    own_k = coarse.shape[0]
    coarse_start = lax.axis_index("ch") * own_k
    coarse_in = 2 * own_k
    coarse_z, coarse_x, cells_yc = coarse.shape[1], coarse.shape[2], coarse.shape[3]
    up_rows = lax.dynamic_slice_in_dim(up_weight, channel_start, part_ch, 1)
    up_w = jnp.transpose(up_rows.reshape(3, 9, part_ch, coarse_in), (0, 3, 1, 2))
    up_w = up_w.reshape(3, coarse_in, 9 * part_ch)

    coarse_acc, up_acc = pl.pallas_call(
        functools.partial(coarse_kernel, float(coarse_total) ** (-0.5)),
        out_shape=(
            jax.ShapeDtypeStruct((coarse_z, coarse_x, coarse_in, cells_yc), jnp.float32),
            jax.ShapeDtypeStruct((3, 9 * part_ch, coarse_in), jnp.float32),
        ),
        in_specs=vmem_specs(6),
        out_specs=tuple(vmem_specs(2)),
        scratch_shapes=[
            pltpu.VMEM((planes_z + 1, planes_x + 1, 3, part_ch, cells_yc), jnp.bfloat16)
        ],
    )(grad_rows, last_rows, below_z, coarse_own, coarse_other, up_w)
    up_terms = up_acc.reshape(27, part_ch, coarse_in)
    other_start = own_k - coarse_start
    received = lax.ppermute(lax.dynamic_slice_in_dim(coarse_acc, other_start, own_k, 2), "ch", swap)
    coarse_summed = lax.dynamic_slice_in_dim(coarse_acc, coarse_start, own_k, 2) + received
    grad_coarse = jnp.transpose(coarse_summed, (2, 0, 1, 3)).astype(jnp.bfloat16)
    flat = jnp.concatenate([up_terms.reshape(-1), refine_terms.reshape(-1)])
    grad_up, grad_refine = summed_into(flat, ("gz", "sec"), (up_terms.shape, refine_terms.shape))
    return (grad_coarse, grad_up, grad_refine)


def solution(mesh):
    placed = (
        P("ch", ("groups", "gz", "sec"), None, None),
        P("ch", ("groups", "gz", "sec"), None, None),
        P("ch", ("groups", "gz", "sec"), None, None),
        P(),
        P(),
    )
    return jax.shard_map(
        local,
        mesh=mesh,
        in_specs=placed,
        out_specs=(
            P("ch", ("groups", "gz", "sec"), None, None),
            P("groups", "ch", None),
            P("groups", None, "ch"),
        ),
        check_vma=False,
    )
```
